32 devices in a mesh: groups: 2 (over y), ha: 4 (over z), wa: 2 (over x), ta: 2 (over core).
Axes of the slice: x: 2, y: 2, z: 4, core: 2. Of those that a mesh axis runs over, the one named last changes fastest.
Arguments:
- clip: bfloat16 [16, 64, 64, 128], P(('groups', 'ta'), 'ha', 'wa'), parts along dimension 0
- gain_attn: float32 [128], replicated, may hold values from 0.25 to 1.75
- w_query: bfloat16 [128, 128], replicated
- w_key: bfloat16 [128, 128], replicated
- w_value: bfloat16 [128, 128], replicated, may hold values from -0.5 to 0.5
- w_out: bfloat16 [128, 128], replicated
- gain_one: float32 [128], replicated, may hold values from 0.25 to 1.75
- w_one: bfloat16 [3, 3, 3, 128, 128], replicated, may hold values from -0.109375 to 0.109375
- bias_one: float32 [128], replicated, may hold values from -3 to 3
- gain_two: float32 [128], replicated, may hold values from 0.25 to 1.75
- w_two: bfloat16 [3, 3, 3, 128, 128], replicated, may hold values from -0.109375 to 0.109375
- bias_two: float32 [128], replicated, may hold values from -3 to 3
- cotangent: bfloat16 [16, 64, 64, 128], P(('groups', 'ta'), 'ha', 'wa'), parts along dimension 0, may hold values from -6 to 6
- crop_boxes: int32 [8, 2, 4], P(('groups', 'ha'), 'wa'), parts along dimension 0, may hold values from 0 to 32, as said below
Outputs:
- block_out: bfloat16 [16, 64, 64, 128], P(('groups', 'ta'), 'ha', 'wa'), parts along dimension 0
- grad_one: float32 [6, 3, 3, 128, 128], P('groups'), parts along dimension 0
- grad_two: float32 [6, 3, 3, 128, 128], P('groups'), parts along dimension 0
The draws below stay inside these ranges and needn't reach their ends.
There are 2 independent parts, one for each index of `groups`. The reference program is written for one: setup_inputs(seed, part) draws one part's arguments, and reference() takes and returns one part's arrays. A program takes and returns all parts, laid end to end along the dimension named above; an argument that names none is the same for every part. Nothing has to cross between parts.
Inputs may be any that keep to these rules, and one draw needn't show every extreme that they name: `crop_boxes`: each tile has row start < row end <= 16 and column start < column end <= 32, all multiples of 8.
All inputs are finite; a program needn't handle non-finite values.
Results may differ from the reference program's by a relative error of at most 0.006.
The reference program's roundings to bfloat16 on the way (of `pooled`, `probs`, `mixed`, `attended`, `act_one`, `act_two`, `masked` and `back_one`) count: a program that leaves them out, or rounds other values in their place, can miss the bound.
Values may be sent and summed in bfloat16 or wider, within the bound.
No kernel may reach another device: no remote copies, remote signals or barrier semaphores. Data moves between devices by JAX's collectives and lax.ppermute only.
A program may use at most 64 MiB of HBM per device.

```python
import math
import jax
import jax.numpy as jnp
from jax import lax

C = 128
POOL = 4
TH = 16
TW = 32
FRAMES = 8
HEIGHT = 64
WIDTH = 64
N_HA = 4
N_WA = 2


def draw_clip(key, part):
    keys = jax.random.split(key, 1)
    noise = jax.random.normal(keys[0], (FRAMES, HEIGHT, WIDTH, C), jnp.float32)
    return jnp.clip(noise, -6.0, 6.0).astype(jnp.bfloat16)


def projection_matrix(key, salt):
    own = jax.random.normal(jax.random.fold_in(key, salt), (C, C), jnp.float32)
    return (own * (7.0 / math.sqrt(C))).astype(jnp.bfloat16)


def draw_w_query(key, part):
    return projection_matrix(key, 21)


def draw_w_key(key, part):
    return projection_matrix(key, 22)


def draw_w_out(key, part):
    base = jax.random.normal(jax.random.fold_in(key, 41), (C, C), jnp.float32)
    return (base * (2.5 / math.sqrt(C))).astype(jnp.bfloat16)


def draw_crop_boxes(key, part):
    keys = jax.random.split(jax.random.fold_in(key, 31), 5)
    tiles = (N_HA, N_WA)
    row_start = 8 * jax.random.randint(keys[0], tiles, 0, TH // 16 + 1)
    row_end = 8 * jax.random.randint(keys[1], tiles, TH // 16 + 1, TH // 8 + 1)
    col_start = 8 * jax.random.randint(keys[2], tiles, 0, TW // 16 + 1)
    col_end = 8 * jax.random.randint(keys[3], tiles, TW // 16 + 1, TW // 8 + 1)
    chosen = jax.random.randint(keys[4], (), 0, N_HA * N_WA)
    whole = jnp.arange(N_HA * N_WA).reshape(N_HA, N_WA) == chosen
    row_start = jnp.where(whole, 0, row_start)
    row_end = jnp.where(whole, TH, row_end)
    col_start = jnp.where(whole, 0, col_start)
    col_end = jnp.where(whole, TW, col_end)
    return jnp.stack([row_start, row_end, col_start, col_end], axis=-1).astype(jnp.int32)


def block_levels(rng, extent, cuts, low, largest):
    def one(dim, parts):
        steps = jax.random.uniform(jax.random.fold_in(jax.random.fold_in(rng, 6), dim), (parts,), jnp.float32, low / len(cuts), largest / len(cuts))
        return jnp.repeat(jnp.exp(steps), extent[dim] // parts).reshape((-1,) + (1,) * (len(extent) - dim - 1))

    level = one(*cuts[0])
    for cut in cuts[1:]:
        level = level * one(*cut)
    return level


def centred(rng, shape, deviation, limit, pieces=(), dtype=jnp.bfloat16):
    result = deviation * jax.random.normal(rng, shape, jnp.float32)
    if pieces:
        result = result * block_levels(rng, shape, pieces, -0.22, 0.18)
    return jnp.clip(result, -limit, limit).astype(dtype)


def setup_inputs(seed: int = 0, part: int = 0) -> dict:
    streams_of = jax.random.split(jax.random.key(seed), 15)
    part_keys = jax.random.split(jax.random.fold_in(streams_of[14], part), 15)
    clip = draw_clip(jax.random.fold_in(jax.random.fold_in(streams_of[14], part), 71), part)
    gain_attn = jnp.clip(1.0 + 0.15 * jax.random.normal(streams_of[1], (C,), jnp.float32), 0.25, 1.75)
    w_query = draw_w_query(jax.random.fold_in(streams_of[14], 71), part)
    w_key = draw_w_key(jax.random.fold_in(streams_of[14], 71), part)
    w_value = centred(streams_of[4], (C, C), C ** -0.5, 0.5)
    w_out = draw_w_out(jax.random.fold_in(streams_of[14], 71), part)
    gain_one = jnp.clip(1.0 + 0.15 * jax.random.normal(streams_of[6], (C,), jnp.float32), 0.25, 1.75)
    w_one = centred(streams_of[7], (3, 3, 3, C, C), (27 * C) ** -0.5, 0.109375)
    bias_one = centred(streams_of[8], (C,), 0.5, 3.0, (), jnp.float32)
    gain_two = jnp.clip(1.0 + 0.15 * jax.random.normal(streams_of[9], (C,), jnp.float32), 0.25, 1.75)
    w_two = centred(streams_of[10], (3, 3, 3, C, C), (27 * C) ** -0.5, 0.109375)
    bias_two = centred(streams_of[11], (C,), 0.5, 3.0, (), jnp.float32)
    cotangent = centred(part_keys[12], (FRAMES, HEIGHT, WIDTH, C), 1.0, 6.0, ((0, 2), (1, 4), (2, 2)))
    crop_boxes = draw_crop_boxes(jax.random.fold_in(jax.random.fold_in(streams_of[14], part), 71), part)
    return dict(clip=clip, gain_attn=gain_attn, w_query=w_query, w_key=w_key, w_value=w_value, w_out=w_out, gain_one=gain_one, w_one=w_one, bias_one=bias_one, gain_two=gain_two, w_two=w_two, bias_two=bias_two, cotangent=cotangent, crop_boxes=crop_boxes)


eps_norm = 1e-06

def rms_norm(values, gain):
    scale = lax.rsqrt(lax.optimization_barrier(jnp.mean(values * values, axis=-1, keepdims=True)) + eps_norm)
    return values * scale * gain.astype(jnp.float32)

def conv_valid(padded, kernel):
    return lax.conv_general_dilated(padded[None], kernel, (1, 1, 1), 'VALID', dimension_numbers=('NDHWC', 'DHWIO', 'NDHWC'), preferred_element_type=jnp.float32)[0]

def kernel_grad(padded, upstream):
    frames, rows, cols, chans = upstream.shape
    taps = []
    for tap_t in range(3):
        for tap_h in range(3):
            for tap_w in range(3):
                window = padded[tap_t:tap_t + frames, tap_h:tap_h + rows, tap_w:tap_w + cols]
                taps.append(lax.dot_general(window, upstream, (((0, 1, 2), (0, 1, 2)), ((), ())), preferred_element_type=jnp.float32))
    return jnp.stack(taps).reshape(3, 3, 3, chans, chans)

def norm_back(pre, gain, upstream):
    scale = lax.rsqrt(lax.optimization_barrier(jnp.mean(pre * pre, axis=-1, keepdims=True)) + eps_norm)
    normed = pre * scale
    gated = normed * gain
    sigma = jax.nn.sigmoid(gated)
    dgated = upstream * sigma * (1.0 + gated * (1.0 - sigma))
    dnormed = dgated * gain
    return scale * (dnormed - normed * lax.optimization_barrier(jnp.mean(dnormed * normed, axis=-1, keepdims=True)))

def attend(query, keys_all, values_all):
    width = query.shape[-1]
    scores = jnp.einsum('fqc,fkc->fqk', query.astype(jnp.float32), keys_all.astype(jnp.float32)) / math.sqrt(width)
    top = lax.optimization_barrier(jnp.max(scores, axis=-1, keepdims=True))
    weights = jnp.exp(scores - top)
    probs = (weights / lax.optimization_barrier(jnp.sum(weights, axis=-1, keepdims=True))).astype(jnp.bfloat16)
    return jnp.einsum('fqk,fkc->fqc', probs.astype(jnp.float32), values_all.astype(jnp.float32)).astype(jnp.bfloat16)

def reference(clip, gain_attn, w_query, w_key, w_value, w_out, gain_one, w_one, bias_one, gain_two, w_two, bias_two, cotangent, crop_boxes):
    frames, height, width, chans = clip.shape
    clip_f = clip.astype(jnp.float32)
    pooled = rms_norm(clip_f, gain_attn).reshape(frames, height // POOL, POOL, width // POOL, POOL, chans).mean(axis=(2, 4)).astype(jnp.bfloat16)
    tokens = pooled.reshape(frames, -1, chans)
    query = jnp.dot(tokens, w_query, preferred_element_type=jnp.float32).astype(jnp.bfloat16)
    keys_all = jnp.dot(tokens, w_key, preferred_element_type=jnp.float32).astype(jnp.bfloat16)
    values_all = jnp.dot(tokens, w_value, preferred_element_type=jnp.float32).astype(jnp.bfloat16)
    mixed = attend(query, keys_all, values_all)
    projected = jnp.dot(mixed, w_out, preferred_element_type=jnp.float32).reshape(frames, height // POOL, width // POOL, chans)
    upsampled = jnp.repeat(jnp.repeat(projected, POOL, axis=1), POOL, axis=2)
    attended = (clip_f + upsampled).astype(jnp.bfloat16)
    causal = ((2, 0), (1, 1), (1, 1), (0, 0))
    act_one = jax.nn.silu(rms_norm(attended.astype(jnp.float32), gain_one)).astype(jnp.bfloat16)
    padded_one = jnp.pad(act_one, causal)
    pre_two = conv_valid(padded_one, w_one) + bias_one
    act_two = jax.nn.silu(rms_norm(pre_two, gain_two)).astype(jnp.bfloat16)
    padded_two = jnp.pad(act_two, causal)
    block_out = (attended.astype(jnp.float32) + conv_valid(padded_two, w_two) + bias_two).astype(jnp.bfloat16)
    row_ids = jnp.arange(height)
    col_ids = jnp.arange(width)
    boxes = crop_boxes[(row_ids // TH)[:, None], (col_ids // TW)[None, :]]
    local_row = (row_ids % TH)[:, None]
    local_col = (col_ids % TW)[None, :]
    inside = (local_row >= boxes[..., 0]) & (local_row < boxes[..., 1]) & (local_col >= boxes[..., 2]) & (local_col < boxes[..., 3])
    masked = cotangent * inside.astype(jnp.bfloat16)[None, :, :, None]
    norm_scale = 1.0 / math.sqrt(frames * height * width)
    grad_two = kernel_grad(padded_two, masked) * norm_scale
    flipped = jnp.transpose(w_two[::-1, ::-1, ::-1], (0, 1, 2, 4, 3))
    back_two = conv_valid(jnp.pad(masked, ((0, 2), (1, 1), (1, 1), (0, 0))), flipped)
    back_one = norm_back(pre_two, gain_two, back_two).astype(jnp.bfloat16)
    grad_one = kernel_grad(padded_one, back_one) * norm_scale
    return (block_out, grad_one, grad_two)
```

```python
import math

import jax
import jax.numpy as jnp
from jax import lax
from jax.sharding import PartitionSpec as P

POOL = 4


eps_norm = 1e-06


def shifted(x, axis, by):
    size = lax.axis_size(axis)
    pairs = [(i, i + by) for i in range(size) if 0 <= i + by < size]
    return lax.ppermute(x, axis, pairs)


def padded_2(block, sides, width):
    for axis, dim in sides:
        count = lax.axis_size(axis)
        forward = [(i, i + 1) for i in range(count - 1)]
        backward = [(target, source) for source, target in forward]
        low = lax.ppermute(
            lax.slice_in_dim(block, block.shape[dim] - width, None, axis=dim), axis, forward
        )
        high = lax.ppermute(lax.slice_in_dim(block, 0, width, axis=dim), axis, backward)
        block = jnp.concatenate([low, block, high], axis=dim)
    return block


def halving_stages(axes):
    out = []
    for axis in axes:
        count = lax.axis_size(axis)
        distance = 1
        while distance < count:
            out.append((axis, distance, count))
            distance *= 2
    return out


def reduce_scatter_rows(x, stages):
    for axis, distance, count in stages:
        bit = (lax.axis_index(axis) // distance) % 2
        half = x.shape[0] // 2
        keep = lax.dynamic_slice_in_dim(x, bit * half, half)
        send = lax.dynamic_slice_in_dim(x, (1 - bit) * half, half)
        pairs = [(j, j ^ distance) for j in range(count)]
        x = keep + lax.ppermute(send, axis, pairs)
    return x


def all_gather_rows(x, stages):
    for axis, distance, count in reversed(stages):
        bit = (lax.axis_index(axis) // distance) % 2
        pairs = [(j, j ^ distance) for j in range(count)]
        got = lax.ppermute(x, axis, pairs)
        low = jnp.where(bit == 0, x, got)
        high = jnp.where(bit == 0, got, x)
        x = jnp.concatenate([low, high], axis=0)
    return x


def summed_over(value, axes, chunks=2):
    sizes = [lax.axis_size(axis) for axis in axes]
    if any(size & (size - 1) for size in sizes):
        return lax.psum(value, axes)
    stages = halving_stages(axes)
    rows = value.reshape(-1, value.shape[-1])
    while chunks > 1 and rows.shape[0] % (chunks << len(stages)):
        chunks //= 2
    if rows.shape[0] % (chunks << len(stages)):
        return lax.psum(value, axes)
    pieces = jnp.split(rows, chunks, axis=0)
    joined = [all_gather_rows(reduce_scatter_rows(piece, stages), stages) for piece in pieces]
    return jnp.concatenate(joined, axis=0).reshape(value.shape)


def gathered_tokens(tokens, axes):
    count = lax.axis_size(axes)
    if count > 8:
        return lax.all_gather(tokens, axes, axis=1, tiled=True)
    parts = [tokens]
    for by in range(1, count):
        pairs = [(i, (i + by) % count) for i in range(count)]
        parts.append(lax.ppermute(tokens, axes, pairs))
    return jnp.concatenate(parts, axis=1)


def rms_norm(values, gain):
    scale = lax.rsqrt(jnp.mean(values * values, axis=-1, keepdims=True) + eps_norm)
    return values * scale * gain


def conv_valid(padded, kernel):
    return lax.conv_general_dilated(
        padded[None],
        kernel,
        (1, 1, 1),
        "VALID",
        dimension_numbers=("NDHWC", "DHWIO", "NDHWC"),
        preferred_element_type=jnp.float32,
    )[0]


def kernel_grad(padded, upstream):
    frames, rows, cols, chans = upstream.shape
    taps = []
    for tap_t in range(3):
        for tap_h in range(3):
            for tap_w in range(3):
                window = padded[tap_t : tap_t + frames, tap_h : tap_h + rows, tap_w : tap_w + cols]
                taps.append(
                    lax.dot_general(
                        window,
                        upstream,
                        (((0, 1, 2), (0, 1, 2)), ((), ())),
                        preferred_element_type=jnp.float32,
                    )
                )
    return jnp.stack(taps).reshape(3, 3, 3, chans, chans)


def norm_back(pre, gain, upstream):
    scale = lax.rsqrt(jnp.mean(pre * pre, axis=-1, keepdims=True) + eps_norm)
    normed = pre * scale
    gated = normed * gain
    sigma = jax.nn.sigmoid(gated)
    dgated = upstream * sigma * (1.0 + gated * (1.0 - sigma))
    dnormed = dgated * gain
    return scale * (dnormed - normed * jnp.mean(dnormed * normed, axis=-1, keepdims=True))


def attend(query, keys_all, values_all):
    width = query.shape[-1]
    scores = jnp.einsum(
        "fqc,fkc->fqk", query, keys_all, preferred_element_type=jnp.float32
    ) / math.sqrt(width)
    top = jnp.max(scores, axis=-1, keepdims=True)
    weights = jnp.exp(scores - top)
    probs = (weights / jnp.sum(weights, axis=-1, keepdims=True)).astype(jnp.bfloat16)
    return jnp.einsum("fqk,fkc->fqc", probs, values_all, preferred_element_type=jnp.float32).astype(
        jnp.bfloat16
    )


def causal_padded(block):
    earlier = shifted(block[-2:], "ta", 1)
    extended = jnp.concatenate([earlier, block], axis=0)
    return padded_2(extended, (("ha", 1), ("wa", 2)), 1)


def future_padded(block):
    later = shifted(block[:2], "ta", -1)
    extended = jnp.concatenate([block, later], axis=0)
    return padded_2(extended, (("ha", 1), ("wa", 2)), 1)


def local(
    clip,
    gain_attn,
    w_query,
    w_key,
    w_value,
    w_out,
    gain_one,
    w_one,
    bias_one,
    gain_two,
    w_two,
    bias_two,
    cotangent,
    crop_boxes,
):
    frames, rows, cols, chans = clip.shape
    clip_f = clip.astype(jnp.float32)
    pooled = (
        rms_norm(clip_f, gain_attn)
        .reshape(frames, rows // POOL, POOL, cols // POOL, POOL, chans)
        .mean(axis=(2, 4))
        .astype(jnp.bfloat16)
    )
    tokens = pooled.reshape(frames, -1, chans)
    query = jnp.dot(tokens, w_query, preferred_element_type=jnp.float32).astype(jnp.bfloat16)
    tokens_all = gathered_tokens(tokens, ("ha", "wa"))
    keys_all = jnp.dot(tokens_all, w_key, preferred_element_type=jnp.float32).astype(jnp.bfloat16)
    values_all = jnp.dot(tokens_all, w_value, preferred_element_type=jnp.float32).astype(
        jnp.bfloat16
    )
    mixed = attend(query, keys_all, values_all)
    projected = jnp.dot(mixed, w_out, preferred_element_type=jnp.float32).reshape(
        frames, rows // POOL, cols // POOL, chans
    )
    upsampled = jnp.repeat(jnp.repeat(projected, POOL, axis=1), POOL, axis=2)
    attended = (clip_f + upsampled).astype(jnp.bfloat16)
    act_one = jax.nn.silu(rms_norm(attended.astype(jnp.float32), gain_one)).astype(jnp.bfloat16)
    padded_one = causal_padded(act_one)
    pre_two = conv_valid(padded_one, w_one) + bias_one
    act_two = jax.nn.silu(rms_norm(pre_two, gain_two)).astype(jnp.bfloat16)
    padded_two = causal_padded(act_two)
    block_out = (attended.astype(jnp.float32) + conv_valid(padded_two, w_two) + bias_two).astype(
        jnp.bfloat16
    )
    bounds = crop_boxes[0, 0]
    local_row = jnp.arange(rows)[:, None]
    local_col = jnp.arange(cols)[None, :]
    inside = (
        (local_row >= bounds[0])
        & (local_row < bounds[1])
        & (local_col >= bounds[2])
        & (local_col < bounds[3])
    )
    masked = cotangent * inside.astype(jnp.bfloat16)[None, :, :, None]
    total_pixels = (
        frames * lax.axis_size("ta") * rows * lax.axis_size("ha") * cols * lax.axis_size("wa")
    )
    norm_scale = 1.0 / math.sqrt(total_pixels)
    local_two = kernel_grad(padded_two, masked)
    flipped = jnp.transpose(w_two[::-1, ::-1, ::-1], (0, 1, 2, 4, 3))
    back_two = conv_valid(future_padded(masked), flipped)
    back_one = norm_back(pre_two, gain_two, back_two).astype(jnp.bfloat16)
    local_one = kernel_grad(padded_one, back_one)
    summed_two = summed_over(local_two, ("ta", "wa", "ha"))
    summed_one = summed_over(local_one, ("ta", "wa", "ha"))
    return (block_out, summed_one * norm_scale, summed_two * norm_scale)


def solution(mesh):
    in_specs = (
        P(("groups", "ta"), "ha", "wa", None),
        P(),
        P(),
        P(),
        P(),
        P(),
        P(),
        P(),
        P(),
        P(),
        P(),
        P(),
        P(("groups", "ta"), "ha", "wa", None),
        P(("groups", "ha"), "wa", None),
    )
    out_specs = (
        P(("groups", "ta"), "ha", "wa", None),
        P("groups", None, None, None, None),
        P("groups", None, None, None, None),
    )
    return jax.shard_map(local, mesh=mesh, in_specs=in_specs, out_specs=out_specs, check_vma=False)
```

```python
import math

import jax
import jax.numpy as jnp
from jax import lax
from jax.sharding import PartitionSpec as P

POOL = 4


eps_norm = 1e-06


def shifted(x, axis, by):
    size = lax.axis_size(axis)
    pairs = [(i, i + by) for i in range(size) if 0 <= i + by < size]
    return lax.ppermute(x, axis, pairs)


def padded_2(block, sides, width):
    for axis, dim in sides:
        count = lax.axis_size(axis)
        forward = [(i, i + 1) for i in range(count - 1)]
        backward = [(target, source) for source, target in forward]
        low = lax.ppermute(
            lax.slice_in_dim(block, block.shape[dim] - width, None, axis=dim), axis, forward
        )
        high = lax.ppermute(lax.slice_in_dim(block, 0, width, axis=dim), axis, backward)
        block = jnp.concatenate([low, block, high], axis=dim)
    return block


def halving_stages(axes):
    out = []
    for axis in axes:
        count = lax.axis_size(axis)
        distance = 1
        while distance < count:
            out.append((axis, distance, count))
            distance *= 2
    return out


def reduce_scatter_rows(x, stages):
    for axis, distance, count in stages:
        bit = (lax.axis_index(axis) // distance) % 2
        half = x.shape[0] // 2
        keep = lax.dynamic_slice_in_dim(x, bit * half, half)
        send = lax.dynamic_slice_in_dim(x, (1 - bit) * half, half)
        pairs = [(j, j ^ distance) for j in range(count)]
        x = keep + lax.ppermute(send, axis, pairs)
    return x


def all_gather_rows(x, stages):
    for axis, distance, count in reversed(stages):
        bit = (lax.axis_index(axis) // distance) % 2
        pairs = [(j, j ^ distance) for j in range(count)]
        got = lax.ppermute(x, axis, pairs)
        low = jnp.where(bit == 0, x, got)
        high = jnp.where(bit == 0, got, x)
        x = jnp.concatenate([low, high], axis=0)
    return x


def summed_over(value, axes, chunks=2):
    sizes = [lax.axis_size(axis) for axis in axes]
    if any(size & (size - 1) for size in sizes):
        return lax.psum(value, axes)
    stages = halving_stages(axes)
    rows = value.reshape(-1, value.shape[-1])
    while chunks > 1 and rows.shape[0] % (chunks << len(stages)):
        chunks //= 2
    if rows.shape[0] % (chunks << len(stages)):
        return lax.psum(value, axes)
    pieces = jnp.split(rows, chunks, axis=0)
    joined = [all_gather_rows(reduce_scatter_rows(piece, stages), stages) for piece in pieces]
    return jnp.concatenate(joined, axis=0).reshape(value.shape)


def gathered_tokens(tokens, axes):
    count = lax.axis_size(axes)
    if count > 8:
        return lax.all_gather(tokens, axes, axis=1, tiled=True)
    parts = [tokens]
    for by in range(1, count):
        pairs = [(i, (i + by) % count) for i in range(count)]
        parts.append(lax.ppermute(tokens, axes, pairs))
    return jnp.concatenate(parts, axis=1)


def rms_norm(values, gain):
    scale = lax.rsqrt(jnp.mean(values * values, axis=-1, keepdims=True) + eps_norm)
    return values * scale * gain


def conv_valid(padded, kernel):
    return lax.conv_general_dilated(
        padded[None],
        kernel,
        (1, 1, 1),
        "VALID",
        dimension_numbers=("NDHWC", "DHWIO", "NDHWC"),
        preferred_element_type=jnp.float32,
    )[0]


def kernel_grad(padded, upstream):
    chans_in, chans_out = padded.shape[-1], upstream.shape[-1]
    taps = lax.conv_general_dilated(
        padded[None],
        upstream[None],
        (1, 1, 1),
        "VALID",
        dimension_numbers=("CDHWN", "IDHWO", "NDHWC"),
        preferred_element_type=jnp.float32,
    )
    return jnp.transpose(taps, (1, 2, 3, 0, 4)).reshape(3, 3, 3, chans_in, chans_out)


def norm_back(pre, gain, upstream):
    scale = lax.rsqrt(jnp.mean(pre * pre, axis=-1, keepdims=True) + eps_norm)
    normed = pre * scale
    gated = normed * gain
    sigma = jax.nn.sigmoid(gated)
    dgated = upstream * sigma * (1.0 + gated * (1.0 - sigma))
    dnormed = dgated * gain
    return scale * (dnormed - normed * jnp.mean(dnormed * normed, axis=-1, keepdims=True))


def attend(query, keys_all, values_all):
    width = query.shape[-1]
    scores = jnp.einsum(
        "fqc,fkc->fqk", query, keys_all, preferred_element_type=jnp.float32
    ) / math.sqrt(width)
    top = jnp.max(scores, axis=-1, keepdims=True)
    weights = jnp.exp(scores - top)
    probs = (weights / jnp.sum(weights, axis=-1, keepdims=True)).astype(jnp.bfloat16)
    return jnp.einsum("fqk,fkc->fqc", probs, values_all, preferred_element_type=jnp.float32).astype(
        jnp.bfloat16
    )


def causal_padded(block):
    earlier = shifted(block[-2:], "ta", 1)
    extended = jnp.concatenate([earlier, block], axis=0)
    return padded_2(extended, (("ha", 1), ("wa", 2)), 1)


def future_padded(block):
    later = shifted(block[:2], "ta", -1)
    extended = jnp.concatenate([block, later], axis=0)
    return padded_2(extended, (("ha", 1), ("wa", 2)), 1)


def local(
    clip,
    gain_attn,
    w_query,
    w_key,
    w_value,
    w_out,
    gain_one,
    w_one,
    bias_one,
    gain_two,
    w_two,
    bias_two,
    cotangent,
    crop_boxes,
):
    frames, rows, cols, chans = clip.shape
    clip_f = clip.astype(jnp.float32)
    pooled = (
        rms_norm(clip_f, gain_attn)
        .reshape(frames, rows // POOL, POOL, cols // POOL, POOL, chans)
        .mean(axis=(2, 4))
        .astype(jnp.bfloat16)
    )
    tokens = pooled.reshape(frames, -1, chans)
    query = jnp.dot(tokens, w_query, preferred_element_type=jnp.float32).astype(jnp.bfloat16)
    tokens_all = gathered_tokens(tokens, ("ha", "wa"))
    keys_all = jnp.dot(tokens_all, w_key, preferred_element_type=jnp.float32).astype(jnp.bfloat16)
    values_all = jnp.dot(tokens_all, w_value, preferred_element_type=jnp.float32).astype(
        jnp.bfloat16
    )
    mixed = attend(query, keys_all, values_all)
    projected = jnp.dot(mixed, w_out, preferred_element_type=jnp.float32).reshape(
        frames, rows // POOL, cols // POOL, chans
    )
    upsampled = jnp.repeat(jnp.repeat(projected, POOL, axis=1), POOL, axis=2)
    attended = (clip_f + upsampled).astype(jnp.bfloat16)
    act_one = jax.nn.silu(rms_norm(attended.astype(jnp.float32), gain_one)).astype(jnp.bfloat16)
    padded_one = causal_padded(act_one)
    pre_two = conv_valid(padded_one, w_one) + bias_one
    act_two = jax.nn.silu(rms_norm(pre_two, gain_two)).astype(jnp.bfloat16)
    padded_two = causal_padded(act_two)
    block_out = (attended.astype(jnp.float32) + conv_valid(padded_two, w_two) + bias_two).astype(
        jnp.bfloat16
    )
    bounds = crop_boxes[0, 0]
    local_row = jnp.arange(rows)[:, None]
    local_col = jnp.arange(cols)[None, :]
    inside = (
        (local_row >= bounds[0])
        & (local_row < bounds[1])
        & (local_col >= bounds[2])
        & (local_col < bounds[3])
    )
    masked = cotangent * inside.astype(jnp.bfloat16)[None, :, :, None]
    total_pixels = (
        frames * lax.axis_size("ta") * rows * lax.axis_size("ha") * cols * lax.axis_size("wa")
    )
    norm_scale = 1.0 / math.sqrt(total_pixels)
    local_two = kernel_grad(padded_two, masked)
    flipped = jnp.transpose(w_two[::-1, ::-1, ::-1], (0, 1, 2, 4, 3))
    back_two = conv_valid(future_padded(masked), flipped)
    back_one = norm_back(pre_two, gain_two, back_two).astype(jnp.bfloat16)
    local_one = kernel_grad(padded_one, back_one)
    summed_two = summed_over(local_two, ("ta", "wa", "ha"))
    summed_one = summed_over(local_one, ("ta", "wa", "ha"))
    return (block_out, summed_one * norm_scale, summed_two * norm_scale)


def solution(mesh):
    in_specs = (
        P(("groups", "ta"), "ha", "wa", None),
        P(),
        P(),
        P(),
        P(),
        P(),
        P(),
        P(),
        P(),
        P(),
        P(),
        P(),
        P(("groups", "ta"), "ha", "wa", None),
        P(("groups", "ha"), "wa", None),
    )
    out_specs = (
        P(("groups", "ta"), "ha", "wa", None),
        P("groups", None, None, None, None),
        P("groups", None, None, None, None),
    )
    return jax.shard_map(local, mesh=mesh, in_specs=in_specs, out_specs=out_specs, check_vma=False)
```

```python
import math

import jax
import jax.numpy as jnp
from jax import lax
from jax.sharding import PartitionSpec as P

POOL = 4


eps_norm = 1e-06


def shifted(x, axis, by):
    size = lax.axis_size(axis)
    pairs = [(i, i + by) for i in range(size) if 0 <= i + by < size]
    return lax.ppermute(x, axis, pairs)


def padded_2(block, sides, width):
    for axis, dim in sides:
        count = lax.axis_size(axis)
        forward = [(i, i + 1) for i in range(count - 1)]
        backward = [(target, source) for source, target in forward]
        low = lax.ppermute(
            lax.slice_in_dim(block, block.shape[dim] - width, None, axis=dim), axis, forward
        )
        high = lax.ppermute(lax.slice_in_dim(block, 0, width, axis=dim), axis, backward)
        block = jnp.concatenate([low, block, high], axis=dim)
    return block


def halving_stages(axes):
    out = []
    for axis in axes:
        count = lax.axis_size(axis)
        distance = 1
        while distance < count:
            out.append((axis, distance, count))
            distance *= 2
    return out


def reduce_scatter_rows(x, stages):
    for axis, distance, count in stages:
        bit = (lax.axis_index(axis) // distance) % 2
        half = x.shape[0] // 2
        keep = lax.dynamic_slice_in_dim(x, bit * half, half)
        send = lax.dynamic_slice_in_dim(x, (1 - bit) * half, half)
        pairs = [(j, j ^ distance) for j in range(count)]
        x = keep + lax.ppermute(send, axis, pairs)
    return x


def all_gather_rows(x, stages):
    for axis, distance, count in reversed(stages):
        bit = (lax.axis_index(axis) // distance) % 2
        pairs = [(j, j ^ distance) for j in range(count)]
        got = lax.ppermute(x, axis, pairs)
        low = jnp.where(bit == 0, x, got)
        high = jnp.where(bit == 0, got, x)
        x = jnp.concatenate([low, high], axis=0)
    return x


def summed_over(value, axes, chunks=2):
    sizes = [lax.axis_size(axis) for axis in axes]
    if any(size & (size - 1) for size in sizes):
        return lax.psum(value, axes)
    stages = halving_stages(axes)
    rows = value.reshape(-1, value.shape[-1])
    while chunks > 1 and rows.shape[0] % (chunks << len(stages)):
        chunks //= 2
    if rows.shape[0] % (chunks << len(stages)):
        return lax.psum(value, axes)
    pieces = jnp.split(rows, chunks, axis=0)
    joined = [all_gather_rows(reduce_scatter_rows(piece, stages), stages) for piece in pieces]
    return jnp.concatenate(joined, axis=0).reshape(value.shape)


def gathered_tokens(tokens, axes):
    count = lax.axis_size(axes)
    if count > 8:
        return lax.all_gather(tokens, axes, axis=0)
    me = lax.axis_index(axes)
    full = jnp.zeros((count,) + tokens.shape, tokens.dtype)
    full = lax.dynamic_update_index_in_dim(full, tokens, me, 0)
    for by in range(1, count):
        pairs = [(i, (i + by) % count) for i in range(count)]
        part = lax.ppermute(tokens, axes, pairs)
        full = lax.dynamic_update_index_in_dim(full, part, (me - by) % count, 0)
    return full

def rms_norm(values, gain):
    scale = lax.rsqrt(jnp.mean(values * values, axis=-1, keepdims=True) + eps_norm)
    return values * scale * gain


def conv_valid(padded, kernel):
    return lax.conv_general_dilated(
        padded[None],
        kernel,
        (1, 1, 1),
        "VALID",
        dimension_numbers=("NDHWC", "DHWIO", "NDHWC"),
        preferred_element_type=jnp.float32,
    )[0]


def kernel_grad(padded, upstream):
    frames, rows, cols, chans = upstream.shape
    taps = []
    for tap_t in range(3):
        for tap_h in range(3):
            for tap_w in range(3):
                window = padded[tap_t : tap_t + frames, tap_h : tap_h + rows, tap_w : tap_w + cols]
                taps.append(
                    lax.dot_general(
                        window,
                        upstream,
                        (((0, 1, 2), (0, 1, 2)), ((), ())),
                        preferred_element_type=jnp.float32,
                    )
                )
    return jnp.stack(taps).reshape(3, 3, 3, chans, chans)


def norm_back(pre, gain, upstream):
    scale = lax.rsqrt(jnp.mean(pre * pre, axis=-1, keepdims=True) + eps_norm)
    normed = pre * scale
    gated = normed * gain
    sigma = jax.nn.sigmoid(gated)
    dgated = upstream * sigma * (1.0 + gated * (1.0 - sigma))
    dnormed = dgated * gain
    return scale * (dnormed - normed * jnp.mean(dnormed * normed, axis=-1, keepdims=True))


def attend(query, keys_all, values_all):
    width = query.shape[-1]
    scores = jnp.einsum(
        "fqc,fkc->fqk", query, keys_all, preferred_element_type=jnp.float32
    ) / math.sqrt(width)
    top = jnp.max(scores, axis=-1, keepdims=True)
    weights = jnp.exp(scores - top)
    probs = (weights / jnp.sum(weights, axis=-1, keepdims=True)).astype(jnp.bfloat16)
    return jnp.einsum("fqk,fkc->fqc", probs, values_all, preferred_element_type=jnp.float32).astype(
        jnp.bfloat16
    )


def causal_padded(block):
    earlier = shifted(block[-2:], "ta", 1)
    extended = jnp.concatenate([earlier, block], axis=0)
    return padded_2(extended, (("ha", 1), ("wa", 2)), 1)


def future_padded(block):
    later = shifted(block[:2], "ta", -1)
    extended = jnp.concatenate([block, later], axis=0)
    return padded_2(extended, (("ha", 1), ("wa", 2)), 1)


def local(
    clip,
    gain_attn,
    w_query,
    w_key,
    w_value,
    w_out,
    gain_one,
    w_one,
    bias_one,
    gain_two,
    w_two,
    bias_two,
    cotangent,
    crop_boxes,
):
    frames, rows, cols, chans = clip.shape
    n_ha, n_wa = lax.axis_size("ha"), lax.axis_size("wa")
    at_ha, at_wa = lax.axis_index("ha"), lax.axis_index("wa")
    clip_f = clip.astype(jnp.float32)
    pooled = (
        rms_norm(clip_f, gain_attn)
        .reshape(frames, rows // POOL, POOL, cols // POOL, POOL, chans)
        .mean(axis=(2, 4))
        .astype(jnp.bfloat16)
    )
    grid_rows, grid_cols = rows // POOL, cols // POOL
    full = gathered_tokens(pooled, ("ha", "wa")).reshape(
        n_ha, n_wa, frames, grid_rows, grid_cols, chans
    )
    grid = jnp.transpose(full, (2, 0, 3, 1, 4, 5)).reshape(
        frames, n_ha * grid_rows, n_wa * grid_cols, chans
    )
    tokens_all = grid.reshape(frames, -1, chans)
    keys_all = jnp.dot(tokens_all, w_key, preferred_element_type=jnp.float32).astype(jnp.bfloat16)
    values_all = jnp.dot(tokens_all, w_value, preferred_element_type=jnp.float32).astype(
        jnp.bfloat16
    )
    near = lax.dynamic_slice(
        jnp.pad(grid, ((0, 0), (1, 1), (1, 1), (0, 0))),
        (0, at_ha * grid_rows, at_wa * grid_cols, 0),
        (frames, grid_rows + 2, grid_cols + 2, chans),
    )
    query = jnp.dot(
        near.reshape(frames, -1, chans), w_query, preferred_element_type=jnp.float32
    ).astype(jnp.bfloat16)
    mixed = attend(query, keys_all, values_all)
    projected = jnp.dot(mixed, w_out, preferred_element_type=jnp.float32).reshape(
        frames, grid_rows + 2, grid_cols + 2, chans
    )
    upsampled = jnp.repeat(jnp.repeat(projected, POOL, axis=1), POOL, axis=2)
    upsampled = upsampled[:, POOL - 2 : POOL + rows + 2, POOL - 2 : POOL + cols + 2]
    clip_wide = padded_2(clip, (("ha", 1), ("wa", 2)), 2).astype(jnp.float32)
    attended_wide = (clip_wide + upsampled).astype(jnp.bfloat16)
    attended = attended_wide[:, 2 : 2 + rows, 2 : 2 + cols]

    def inside_frame(border):
        row_ids = at_ha * rows - border + jnp.arange(rows + 2 * border)
        col_ids = at_wa * cols - border + jnp.arange(cols + 2 * border)
        row_ok = (row_ids >= 0) & (row_ids < n_ha * rows)
        col_ok = (col_ids >= 0) & (col_ids < n_wa * cols)
        return (row_ok[:, None] & col_ok[None, :])[None, :, :, None]

    act_one_wide = jax.nn.silu(rms_norm(attended_wide.astype(jnp.float32), gain_one)).astype(
        jnp.bfloat16
    )
    act_one_wide = jnp.where(inside_frame(2), act_one_wide, jnp.zeros_like(act_one_wide))
    padded_one_wide = jnp.concatenate([shifted(act_one_wide[-2:], "ta", 1), act_one_wide], axis=0)
    pre_two_wide = conv_valid(padded_one_wide, w_one) + bias_one
    act_two_wide = jax.nn.silu(rms_norm(pre_two_wide, gain_two)).astype(jnp.bfloat16)
    act_two_wide = jnp.where(inside_frame(1), act_two_wide, jnp.zeros_like(act_two_wide))
    padded_two = jnp.concatenate([shifted(act_two_wide[-2:], "ta", 1), act_two_wide], axis=0)
    padded_one = padded_one_wide[:, 1 : 3 + rows, 1 : 3 + cols]
    pre_two = pre_two_wide[:, 1 : 1 + rows, 1 : 1 + cols]
    block_out = (attended.astype(jnp.float32) + conv_valid(padded_two, w_two) + bias_two).astype(
        jnp.bfloat16
    )
    bounds = crop_boxes[0, 0]
    local_row = jnp.arange(rows)[:, None]
    local_col = jnp.arange(cols)[None, :]
    inside = (
        (local_row >= bounds[0])
        & (local_row < bounds[1])
        & (local_col >= bounds[2])
        & (local_col < bounds[3])
    )
    masked = cotangent * inside.astype(jnp.bfloat16)[None, :, :, None]
    total_pixels = (
        frames * lax.axis_size("ta") * rows * lax.axis_size("ha") * cols * lax.axis_size("wa")
    )
    norm_scale = 1.0 / math.sqrt(total_pixels)
    local_two = kernel_grad(padded_two, masked)
    flipped = jnp.transpose(w_two[::-1, ::-1, ::-1], (0, 1, 2, 4, 3))
    back_two = conv_valid(future_padded(masked), flipped)
    back_one = norm_back(pre_two, gain_two, back_two).astype(jnp.bfloat16)
    local_one = kernel_grad(padded_one, back_one)
    summed_two = summed_over(local_two, ("ta", "wa", "ha"))
    summed_one = summed_over(local_one, ("ta", "wa", "ha"))
    return (block_out, summed_one * norm_scale, summed_two * norm_scale)


def solution(mesh):
    in_specs = (
        P(("groups", "ta"), "ha", "wa", None),
        P(),
        P(),
        P(),
        P(),
        P(),
        P(),
        P(),
        P(),
        P(),
        P(),
        P(),
        P(("groups", "ta"), "ha", "wa", None),
        P(("groups", "ha"), "wa", None),
    )
    out_specs = (
        P(("groups", "ta"), "ha", "wa", None),
        P("groups", None, None, None, None),
        P("groups", None, None, None, None),
    )
    return jax.shard_map(local, mesh=mesh, in_specs=in_specs, out_specs=out_specs, check_vma=False)
```

```python
import math

import jax
import jax.numpy as jnp
from jax import lax
from jax.sharding import PartitionSpec as P

POOL = 4


eps_norm = 1e-06


def shifted(x, axis, by):
    size = lax.axis_size(axis)
    pairs = [(i, i + by) for i in range(size) if 0 <= i + by < size]
    return lax.ppermute(x, axis, pairs)


def padded_2(block, sides, width):
    for axis, dim in sides:
        count = lax.axis_size(axis)
        forward = [(i, i + 1) for i in range(count - 1)]
        backward = [(target, source) for source, target in forward]
        low = lax.ppermute(
            lax.slice_in_dim(block, block.shape[dim] - width, None, axis=dim), axis, forward
        )
        high = lax.ppermute(lax.slice_in_dim(block, 0, width, axis=dim), axis, backward)
        block = jnp.concatenate([low, block, high], axis=dim)
    return block


def halving_stages(axes):
    out = []
    for axis in axes:
        count = lax.axis_size(axis)
        distance = 1
        while distance < count:
            out.append((axis, distance, count))
            distance *= 2
    return out


def reduce_scatter_rows(x, stages):
    for axis, distance, count in stages:
        bit = (lax.axis_index(axis) // distance) % 2
        half = x.shape[0] // 2
        keep = lax.dynamic_slice_in_dim(x, bit * half, half)
        send = lax.dynamic_slice_in_dim(x, (1 - bit) * half, half)
        pairs = [(j, j ^ distance) for j in range(count)]
        x = keep + lax.ppermute(send, axis, pairs)
    return x


def all_gather_rows(x, stages):
    for axis, distance, count in reversed(stages):
        bit = (lax.axis_index(axis) // distance) % 2
        pairs = [(j, j ^ distance) for j in range(count)]
        got = lax.ppermute(x, axis, pairs)
        low = jnp.where(bit == 0, x, got)
        high = jnp.where(bit == 0, got, x)
        x = jnp.concatenate([low, high], axis=0)
    return x


def summed_over(value, axes, chunks=2):
    sizes = [lax.axis_size(axis) for axis in axes]
    if any(size & (size - 1) for size in sizes):
        return lax.psum(value, axes)
    stages = halving_stages(axes)
    rows = value.reshape(-1, value.shape[-1])
    while chunks > 1 and rows.shape[0] % (chunks << len(stages)):
        chunks //= 2
    if rows.shape[0] % (chunks << len(stages)):
        return lax.psum(value, axes)
    pieces = jnp.split(rows, chunks, axis=0)
    joined = [all_gather_rows(reduce_scatter_rows(piece, stages), stages) for piece in pieces]
    return jnp.concatenate(joined, axis=0).reshape(value.shape)


def gathered_tokens(tokens, axes):
    count = lax.axis_size(axes)
    if count > 8:
        return lax.all_gather(tokens, axes, axis=0)
    me = lax.axis_index(axes)
    full = jnp.zeros((count,) + tokens.shape, tokens.dtype)
    full = lax.dynamic_update_index_in_dim(full, tokens, me, 0)
    for by in range(1, count):
        pairs = [(i, (i + by) % count) for i in range(count)]
        part = lax.ppermute(tokens, axes, pairs)
        full = lax.dynamic_update_index_in_dim(full, part, (me - by) % count, 0)
    return full

def padded_together(blocks, widths):
    for axis, dim in (("ha", 1), ("wa", 2)):
        count = lax.axis_size(axis)
        forward = [(i, i + 1) for i in range(count - 1)]
        backward = [(target, source) for source, target in forward]
        frames, chans = blocks[0].shape[0], blocks[0].shape[-1]

        def flat(parts):
            return jnp.concatenate([p.reshape(frames, -1, chans) for p in parts], axis=1)

        tails = [lax.slice_in_dim(b, b.shape[dim] - w, None, axis=dim) for b, w in zip(blocks, widths)]
        heads = [lax.slice_in_dim(b, 0, w, axis=dim) for b, w in zip(blocks, widths)]
        low = lax.ppermute(flat(tails), axis, forward)
        high = lax.ppermute(flat(heads), axis, backward)
        out, at = [], 0
        for b, t, h in zip(blocks, tails, heads):
            size = t.size // (frames * chans)
            got_low = low[:, at : at + size].reshape(t.shape)
            got_high = high[:, at : at + size].reshape(h.shape)
            at += size
            out.append(jnp.concatenate([got_low, b, got_high], axis=dim))
        blocks = out
    return blocks


def rms_norm(values, gain):
    scale = lax.rsqrt(jnp.mean(values * values, axis=-1, keepdims=True) + eps_norm)
    return values * scale * gain


def conv_valid(padded, kernel):
    return lax.conv_general_dilated(
        padded[None],
        kernel,
        (1, 1, 1),
        "VALID",
        dimension_numbers=("NDHWC", "DHWIO", "NDHWC"),
        preferred_element_type=jnp.float32,
    )[0]


def kernel_grad(padded, upstream):
    frames, rows, cols, chans = upstream.shape
    taps = []
    for tap_t in range(3):
        for tap_h in range(3):
            for tap_w in range(3):
                window = padded[tap_t : tap_t + frames, tap_h : tap_h + rows, tap_w : tap_w + cols]
                taps.append(
                    lax.dot_general(
                        window,
                        upstream,
                        (((0, 1, 2), (0, 1, 2)), ((), ())),
                        preferred_element_type=jnp.float32,
                    )
                )
    return jnp.stack(taps).reshape(3, 3, 3, chans, chans)


def norm_back(pre, gain, upstream):
    scale = lax.rsqrt(jnp.mean(pre * pre, axis=-1, keepdims=True) + eps_norm)
    normed = pre * scale
    gated = normed * gain
    sigma = jax.nn.sigmoid(gated)
    dgated = upstream * sigma * (1.0 + gated * (1.0 - sigma))
    dnormed = dgated * gain
    return scale * (dnormed - normed * jnp.mean(dnormed * normed, axis=-1, keepdims=True))


def attend(query, keys_all, values_all):
    width = query.shape[-1]
    scores = jnp.einsum(
        "fqc,fkc->fqk", query, keys_all, preferred_element_type=jnp.float32
    ) / math.sqrt(width)
    top = jnp.max(scores, axis=-1, keepdims=True)
    weights = jnp.exp(scores - top)
    probs = (weights / jnp.sum(weights, axis=-1, keepdims=True)).astype(jnp.bfloat16)
    return jnp.einsum("fqk,fkc->fqc", probs, values_all, preferred_element_type=jnp.float32).astype(
        jnp.bfloat16
    )


def causal_padded(block):
    earlier = shifted(block[-2:], "ta", 1)
    extended = jnp.concatenate([earlier, block], axis=0)
    return padded_2(extended, (("ha", 1), ("wa", 2)), 1)


def future_padded(block):
    later = shifted(block[:2], "ta", -1)
    extended = jnp.concatenate([block, later], axis=0)
    return padded_2(extended, (("ha", 1), ("wa", 2)), 1)


def local(
    clip,
    gain_attn,
    w_query,
    w_key,
    w_value,
    w_out,
    gain_one,
    w_one,
    bias_one,
    gain_two,
    w_two,
    bias_two,
    cotangent,
    crop_boxes,
):
    frames, rows, cols, chans = clip.shape
    n_ha, n_wa = lax.axis_size("ha"), lax.axis_size("wa")
    at_ha, at_wa = lax.axis_index("ha"), lax.axis_index("wa")
    clip_f = clip.astype(jnp.float32)
    pooled = (
        rms_norm(clip_f, gain_attn)
        .reshape(frames, rows // POOL, POOL, cols // POOL, POOL, chans)
        .mean(axis=(2, 4))
        .astype(jnp.bfloat16)
    )
    grid_rows, grid_cols = rows // POOL, cols // POOL
    full = gathered_tokens(pooled, ("ha", "wa")).reshape(
        n_ha, n_wa, frames, grid_rows, grid_cols, chans
    )
    grid = jnp.transpose(full, (2, 0, 3, 1, 4, 5)).reshape(
        frames, n_ha * grid_rows, n_wa * grid_cols, chans
    )
    tokens_all = grid.reshape(frames, -1, chans)
    keys_all = jnp.dot(tokens_all, w_key, preferred_element_type=jnp.float32).astype(jnp.bfloat16)
    values_all = jnp.dot(tokens_all, w_value, preferred_element_type=jnp.float32).astype(
        jnp.bfloat16
    )
    near = lax.dynamic_slice(
        jnp.pad(grid, ((0, 0), (1, 1), (1, 1), (0, 0))),
        (0, at_ha * grid_rows, at_wa * grid_cols, 0),
        (frames, grid_rows + 2, grid_cols + 2, chans),
    )
    query = jnp.dot(
        near.reshape(frames, -1, chans), w_query, preferred_element_type=jnp.float32
    ).astype(jnp.bfloat16)
    mixed = attend(query, keys_all, values_all)
    projected = jnp.dot(mixed, w_out, preferred_element_type=jnp.float32).reshape(
        frames, grid_rows + 2, grid_cols + 2, chans
    )
    upsampled = jnp.repeat(jnp.repeat(projected, POOL, axis=1), POOL, axis=2)
    upsampled = upsampled[:, POOL - 2 : POOL + rows + 2, POOL - 2 : POOL + cols + 2]
    bounds = crop_boxes[0, 0]
    local_row = jnp.arange(rows)[:, None]
    local_col = jnp.arange(cols)[None, :]
    inside = (
        (local_row >= bounds[0])
        & (local_row < bounds[1])
        & (local_col >= bounds[2])
        & (local_col < bounds[3])
    )
    masked = cotangent * inside.astype(jnp.bfloat16)[None, :, :, None]
    clip_wide, masked_wide = padded_together([clip, masked], [2, 1])
    clip_wide = clip_wide.astype(jnp.float32)
    masked_future = jnp.concatenate([masked_wide, shifted(masked_wide[:2], "ta", -1)], axis=0)
    attended_wide = (clip_wide + upsampled).astype(jnp.bfloat16)
    attended = attended_wide[:, 2 : 2 + rows, 2 : 2 + cols]

    def inside_frame(border):
        row_ids = at_ha * rows - border + jnp.arange(rows + 2 * border)
        col_ids = at_wa * cols - border + jnp.arange(cols + 2 * border)
        row_ok = (row_ids >= 0) & (row_ids < n_ha * rows)
        col_ok = (col_ids >= 0) & (col_ids < n_wa * cols)
        return (row_ok[:, None] & col_ok[None, :])[None, :, :, None]

    act_one_wide = jax.nn.silu(rms_norm(attended_wide.astype(jnp.float32), gain_one)).astype(
        jnp.bfloat16
    )
    act_one_wide = jnp.where(inside_frame(2), act_one_wide, jnp.zeros_like(act_one_wide))
    padded_one_wide = jnp.concatenate([shifted(act_one_wide[-2:], "ta", 1), act_one_wide], axis=0)
    pre_two_wide = conv_valid(padded_one_wide, w_one) + bias_one
    act_two_wide = jax.nn.silu(rms_norm(pre_two_wide, gain_two)).astype(jnp.bfloat16)
    act_two_wide = jnp.where(inside_frame(1), act_two_wide, jnp.zeros_like(act_two_wide))
    padded_two = jnp.concatenate([shifted(act_two_wide[-2:], "ta", 1), act_two_wide], axis=0)
    padded_one = padded_one_wide[:, 1 : 3 + rows, 1 : 3 + cols]
    pre_two = pre_two_wide[:, 1 : 1 + rows, 1 : 1 + cols]
    block_out = (attended.astype(jnp.float32) + conv_valid(padded_two, w_two) + bias_two).astype(
        jnp.bfloat16
    )
    total_pixels = (
        frames * lax.axis_size("ta") * rows * lax.axis_size("ha") * cols * lax.axis_size("wa")
    )
    norm_scale = 1.0 / math.sqrt(total_pixels)
    local_two = kernel_grad(padded_two, masked)
    flipped = jnp.transpose(w_two[::-1, ::-1, ::-1], (0, 1, 2, 4, 3))
    back_two = conv_valid(masked_future, flipped)
    back_one = norm_back(pre_two, gain_two, back_two).astype(jnp.bfloat16)
    local_one = kernel_grad(padded_one, back_one)
    summed_two = summed_over(local_two, ("ta", "wa", "ha"))
    summed_one = summed_over(local_one, ("ta", "wa", "ha"))
    return (block_out, summed_one * norm_scale, summed_two * norm_scale)


def solution(mesh):
    in_specs = (
        P(("groups", "ta"), "ha", "wa", None),
        P(),
        P(),
        P(),
        P(),
        P(),
        P(),
        P(),
        P(),
        P(),
        P(),
        P(),
        P(("groups", "ta"), "ha", "wa", None),
        P(("groups", "ha"), "wa", None),
    )
    out_specs = (
        P(("groups", "ta"), "ha", "wa", None),
        P("groups", None, None, None, None),
        P("groups", None, None, None, None),
    )
    return jax.shard_map(local, mesh=mesh, in_specs=in_specs, out_specs=out_specs, check_vma=False)
```

```python
import math

import jax
import jax.numpy as jnp
from jax import lax
from jax.sharding import PartitionSpec as P

POOL = 4


eps_norm = 1e-06


def shifted(x, axis, by):
    size = lax.axis_size(axis)
    pairs = [(i, i + by) for i in range(size) if 0 <= i + by < size]
    return lax.ppermute(x, axis, pairs)


def padded_2(block, sides, width):
    for axis, dim in sides:
        count = lax.axis_size(axis)
        forward = [(i, i + 1) for i in range(count - 1)]
        backward = [(target, source) for source, target in forward]
        low = lax.ppermute(
            lax.slice_in_dim(block, block.shape[dim] - width, None, axis=dim), axis, forward
        )
        high = lax.ppermute(lax.slice_in_dim(block, 0, width, axis=dim), axis, backward)
        block = jnp.concatenate([low, block, high], axis=dim)
    return block


def halving_stages(axes):
    out = []
    for axis in axes:
        count = lax.axis_size(axis)
        distance = 1
        while distance < count:
            out.append((axis, distance, count))
            distance *= 2
    return out


def reduce_scatter_rows(x, stages):
    for axis, distance, count in stages:
        bit = (lax.axis_index(axis) // distance) % 2
        half = x.shape[0] // 2
        keep = lax.dynamic_slice_in_dim(x, bit * half, half)
        send = lax.dynamic_slice_in_dim(x, (1 - bit) * half, half)
        pairs = [(j, j ^ distance) for j in range(count)]
        x = keep + lax.ppermute(send, axis, pairs)
    return x


def all_gather_rows(x, stages):
    for axis, distance, count in reversed(stages):
        bit = (lax.axis_index(axis) // distance) % 2
        pairs = [(j, j ^ distance) for j in range(count)]
        got = lax.ppermute(x, axis, pairs)
        low = jnp.where(bit == 0, x, got)
        high = jnp.where(bit == 0, got, x)
        x = jnp.concatenate([low, high], axis=0)
    return x


def summed_over(value, axes, chunks=2):
    sizes = [lax.axis_size(axis) for axis in axes]
    if any(size & (size - 1) for size in sizes):
        return lax.psum(value, axes)
    stages = halving_stages(axes)
    rows = value.reshape(-1, value.shape[-1])
    while chunks > 1 and rows.shape[0] % (chunks << len(stages)):
        chunks //= 2
    if rows.shape[0] % (chunks << len(stages)):
        return lax.psum(value, axes)
    pieces = jnp.split(rows, chunks, axis=0)
    joined = [all_gather_rows(reduce_scatter_rows(piece, stages), stages) for piece in pieces]
    return jnp.concatenate(joined, axis=0).reshape(value.shape)


def gathered_tokens(tokens, axes):
    sizes = [lax.axis_size(axis) for axis in axes]
    if any(size & (size - 1) for size in sizes):
        return lax.all_gather(tokens, axes, axis=0)
    full = tokens[None]
    for axis, size in reversed(list(zip(axes, sizes))):
        block = full
        distance = 1
        while distance < size:
            bit = (lax.axis_index(axis) // distance) % 2
            pairs = [(j, j ^ distance) for j in range(size)]
            got = lax.ppermute(block, axis, pairs)
            low = jnp.where(bit == 0, block, got)
            high = jnp.where(bit == 0, got, block)
            block = jnp.concatenate([low[None], high[None]], axis=0)
            block = block.reshape((-1,) + full.shape)
            distance *= 2
        full = block.reshape((-1,) + tokens.shape)
    return full

def padded_together(blocks, widths):
    for axis, dim in (("ha", 1), ("wa", 2)):
        count = lax.axis_size(axis)
        forward = [(i, i + 1) for i in range(count - 1)]
        backward = [(target, source) for source, target in forward]
        frames, chans = blocks[0].shape[0], blocks[0].shape[-1]

        def flat(parts):
            return jnp.concatenate([p.reshape(frames, -1, chans) for p in parts], axis=1)

        tails = [lax.slice_in_dim(b, b.shape[dim] - w, None, axis=dim) for b, w in zip(blocks, widths)]
        heads = [lax.slice_in_dim(b, 0, w, axis=dim) for b, w in zip(blocks, widths)]
        low = lax.ppermute(flat(tails), axis, forward)
        high = lax.ppermute(flat(heads), axis, backward)
        out, at = [], 0
        for b, t, h in zip(blocks, tails, heads):
            size = t.size // (frames * chans)
            got_low = low[:, at : at + size].reshape(t.shape)
            got_high = high[:, at : at + size].reshape(h.shape)
            at += size
            out.append(jnp.concatenate([got_low, b, got_high], axis=dim))
        blocks = out
    return blocks


def rms_norm(values, gain):
    scale = lax.rsqrt(jnp.mean(values * values, axis=-1, keepdims=True) + eps_norm)
    return values * scale * gain


def conv_valid(padded, kernel):
    return lax.conv_general_dilated(
        padded[None],
        kernel,
        (1, 1, 1),
        "VALID",
        dimension_numbers=("NDHWC", "DHWIO", "NDHWC"),
        preferred_element_type=jnp.float32,
    )[0]


def kernel_grad(padded, upstream):
    frames, rows, cols, chans = upstream.shape
    taps = []
    for tap_t in range(3):
        for tap_h in range(3):
            for tap_w in range(3):
                window = padded[tap_t : tap_t + frames, tap_h : tap_h + rows, tap_w : tap_w + cols]
                taps.append(
                    lax.dot_general(
                        window,
                        upstream,
                        (((0, 1, 2), (0, 1, 2)), ((), ())),
                        preferred_element_type=jnp.float32,
                    )
                )
    return jnp.stack(taps).reshape(3, 3, 3, chans, chans)


def norm_back(pre, gain, upstream):
    scale = lax.rsqrt(jnp.mean(pre * pre, axis=-1, keepdims=True) + eps_norm)
    normed = pre * scale
    gated = normed * gain
    sigma = jax.nn.sigmoid(gated)
    dgated = upstream * sigma * (1.0 + gated * (1.0 - sigma))
    dnormed = dgated * gain
    return scale * (dnormed - normed * jnp.mean(dnormed * normed, axis=-1, keepdims=True))


def attend(query, keys_all, values_all):
    width = query.shape[-1]
    scores = jnp.einsum(
        "fqc,fkc->fqk", query, keys_all, preferred_element_type=jnp.float32
    ) / math.sqrt(width)
    top = jnp.max(scores, axis=-1, keepdims=True)
    weights = jnp.exp(scores - top)
    probs = (weights / jnp.sum(weights, axis=-1, keepdims=True)).astype(jnp.bfloat16)
    return jnp.einsum("fqk,fkc->fqc", probs, values_all, preferred_element_type=jnp.float32).astype(
        jnp.bfloat16
    )


def causal_padded(block):
    earlier = shifted(block[-2:], "ta", 1)
    extended = jnp.concatenate([earlier, block], axis=0)
    return padded_2(extended, (("ha", 1), ("wa", 2)), 1)


def future_padded(block):
    later = shifted(block[:2], "ta", -1)
    extended = jnp.concatenate([block, later], axis=0)
    return padded_2(extended, (("ha", 1), ("wa", 2)), 1)


def local(
    clip,
    gain_attn,
    w_query,
    w_key,
    w_value,
    w_out,
    gain_one,
    w_one,
    bias_one,
    gain_two,
    w_two,
    bias_two,
    cotangent,
    crop_boxes,
):
    frames, rows, cols, chans = clip.shape
    n_ha, n_wa = lax.axis_size("ha"), lax.axis_size("wa")
    at_ha, at_wa = lax.axis_index("ha"), lax.axis_index("wa")
    clip_f = clip.astype(jnp.float32)
    pooled = (
        rms_norm(clip_f, gain_attn)
        .reshape(frames, rows // POOL, POOL, cols // POOL, POOL, chans)
        .mean(axis=(2, 4))
        .astype(jnp.bfloat16)
    )
    grid_rows, grid_cols = rows // POOL, cols // POOL
    full = gathered_tokens(pooled, ("ha", "wa")).reshape(
        n_ha, n_wa, frames, grid_rows, grid_cols, chans
    )
    grid = jnp.transpose(full, (2, 0, 3, 1, 4, 5)).reshape(
        frames, n_ha * grid_rows, n_wa * grid_cols, chans
    )
    tokens_all = grid.reshape(frames, -1, chans)
    keys_all = jnp.dot(tokens_all, w_key, preferred_element_type=jnp.float32).astype(jnp.bfloat16)
    values_all = jnp.dot(tokens_all, w_value, preferred_element_type=jnp.float32).astype(
        jnp.bfloat16
    )
    near = lax.dynamic_slice(
        jnp.pad(grid, ((0, 0), (1, 1), (1, 1), (0, 0))),
        (0, at_ha * grid_rows, at_wa * grid_cols, 0),
        (frames, grid_rows + 2, grid_cols + 2, chans),
    )
    query = jnp.dot(
        near.reshape(frames, -1, chans), w_query, preferred_element_type=jnp.float32
    ).astype(jnp.bfloat16)
    mixed = attend(query, keys_all, values_all)
    projected = jnp.dot(mixed, w_out, preferred_element_type=jnp.float32).reshape(
        frames, grid_rows + 2, grid_cols + 2, chans
    )
    upsampled = jnp.repeat(jnp.repeat(projected, POOL, axis=1), POOL, axis=2)
    upsampled = upsampled[:, POOL - 2 : POOL + rows + 2, POOL - 2 : POOL + cols + 2]
    bounds = crop_boxes[0, 0]
    local_row = jnp.arange(rows)[:, None]
    local_col = jnp.arange(cols)[None, :]
    inside = (
        (local_row >= bounds[0])
        & (local_row < bounds[1])
        & (local_col >= bounds[2])
        & (local_col < bounds[3])
    )
    masked = cotangent * inside.astype(jnp.bfloat16)[None, :, :, None]
    clip_wide, masked_wide = padded_together([clip, masked], [2, 1])
    clip_wide = clip_wide.astype(jnp.float32)
    masked_future = jnp.concatenate([masked_wide, shifted(masked_wide[:2], "ta", -1)], axis=0)
    attended_wide = (clip_wide + upsampled).astype(jnp.bfloat16)
    attended = attended_wide[:, 2 : 2 + rows, 2 : 2 + cols]

    def inside_frame(border):
        row_ids = at_ha * rows - border + jnp.arange(rows + 2 * border)
        col_ids = at_wa * cols - border + jnp.arange(cols + 2 * border)
        row_ok = (row_ids >= 0) & (row_ids < n_ha * rows)
        col_ok = (col_ids >= 0) & (col_ids < n_wa * cols)
        return (row_ok[:, None] & col_ok[None, :])[None, :, :, None]

    act_one_wide = jax.nn.silu(rms_norm(attended_wide.astype(jnp.float32), gain_one)).astype(
        jnp.bfloat16
    )
    act_one_wide = jnp.where(inside_frame(2), act_one_wide, jnp.zeros_like(act_one_wide))
    padded_one_wide = jnp.concatenate([shifted(act_one_wide[-2:], "ta", 1), act_one_wide], axis=0)
    pre_two_wide = conv_valid(padded_one_wide, w_one) + bias_one
    act_two_wide = jax.nn.silu(rms_norm(pre_two_wide, gain_two)).astype(jnp.bfloat16)
    act_two_wide = jnp.where(inside_frame(1), act_two_wide, jnp.zeros_like(act_two_wide))
    padded_two = jnp.concatenate([shifted(act_two_wide[-2:], "ta", 1), act_two_wide], axis=0)
    padded_one = padded_one_wide[:, 1 : 3 + rows, 1 : 3 + cols]
    pre_two = pre_two_wide[:, 1 : 1 + rows, 1 : 1 + cols]
    block_out = (attended.astype(jnp.float32) + conv_valid(padded_two, w_two) + bias_two).astype(
        jnp.bfloat16
    )
    total_pixels = (
        frames * lax.axis_size("ta") * rows * lax.axis_size("ha") * cols * lax.axis_size("wa")
    )
    norm_scale = 1.0 / math.sqrt(total_pixels)
    local_two = kernel_grad(padded_two, masked)
    flipped = jnp.transpose(w_two[::-1, ::-1, ::-1], (0, 1, 2, 4, 3))
    back_two = conv_valid(masked_future, flipped)
    back_one = norm_back(pre_two, gain_two, back_two).astype(jnp.bfloat16)
    local_one = kernel_grad(padded_one, back_one)
    summed_two = summed_over(local_two, ("ta", "wa", "ha"))
    summed_one = summed_over(local_one, ("ta", "wa", "ha"))
    return (block_out, summed_one * norm_scale, summed_two * norm_scale)


def solution(mesh):
    in_specs = (
        P(("groups", "ta"), "ha", "wa", None),
        P(),
        P(),
        P(),
        P(),
        P(),
        P(),
        P(),
        P(),
        P(),
        P(),
        P(),
        P(("groups", "ta"), "ha", "wa", None),
        P(("groups", "ha"), "wa", None),
    )
    out_specs = (
        P(("groups", "ta"), "ha", "wa", None),
        P("groups", None, None, None, None),
        P("groups", None, None, None, None),
    )
    return jax.shard_map(local, mesh=mesh, in_specs=in_specs, out_specs=out_specs, check_vma=False)
```

```python
import math

import jax
import jax.numpy as jnp
from jax import lax
from jax.sharding import PartitionSpec as P

POOL = 4


eps_norm = 1e-06


def shifted(x, axis, by):
    size = lax.axis_size(axis)
    pairs = [(i, i + by) for i in range(size) if 0 <= i + by < size]
    return lax.ppermute(x, axis, pairs)


def padded_2(block, sides, width):
    for axis, dim in sides:
        count = lax.axis_size(axis)
        forward = [(i, i + 1) for i in range(count - 1)]
        backward = [(target, source) for source, target in forward]
        low = lax.ppermute(
            lax.slice_in_dim(block, block.shape[dim] - width, None, axis=dim), axis, forward
        )
        high = lax.ppermute(lax.slice_in_dim(block, 0, width, axis=dim), axis, backward)
        block = jnp.concatenate([low, block, high], axis=dim)
    return block


def halving_stages(axes):
    out = []
    for axis in axes:
        count = lax.axis_size(axis)
        distance = 1
        while distance < count:
            out.append((axis, distance, count))
            distance *= 2
    return out


def reduce_scatter_rows(x, stages):
    for axis, distance, count in stages:
        bit = (lax.axis_index(axis) // distance) % 2
        half = x.shape[0] // 2
        keep = lax.dynamic_slice_in_dim(x, bit * half, half)
        send = lax.dynamic_slice_in_dim(x, (1 - bit) * half, half)
        pairs = [(j, j ^ distance) for j in range(count)]
        x = keep + lax.ppermute(send, axis, pairs)
    return x


def all_gather_rows(x, stages):
    for axis, distance, count in reversed(stages):
        bit = (lax.axis_index(axis) // distance) % 2
        pairs = [(j, j ^ distance) for j in range(count)]
        got = lax.ppermute(x, axis, pairs)
        low = jnp.where(bit == 0, x, got)
        high = jnp.where(bit == 0, got, x)
        x = jnp.concatenate([low, high], axis=0)
    return x


def summed_over(value, axes, chunks=1):
    sizes = [lax.axis_size(axis) for axis in axes]
    if any(size & (size - 1) for size in sizes):
        return lax.psum(value, axes)
    stages = halving_stages(axes)
    rows = value.reshape(-1, value.shape[-1])
    while chunks > 1 and rows.shape[0] % (chunks << len(stages)):
        chunks //= 2
    if rows.shape[0] % (chunks << len(stages)):
        return lax.psum(value, axes)
    pieces = jnp.split(rows, chunks, axis=0)
    joined = [all_gather_rows(reduce_scatter_rows(piece, stages), stages) for piece in pieces]
    return jnp.concatenate(joined, axis=0).reshape(value.shape)


def gathered_tokens(tokens, axes):
    sizes = [lax.axis_size(axis) for axis in axes]
    if any(size & (size - 1) for size in sizes):
        return lax.all_gather(tokens, axes, axis=0)
    full = tokens[None]
    for axis, size in reversed(list(zip(axes, sizes))):
        block = full
        distance = 1
        while distance < size:
            bit = (lax.axis_index(axis) // distance) % 2
            pairs = [(j, j ^ distance) for j in range(size)]
            got = lax.ppermute(block, axis, pairs)
            low = jnp.where(bit == 0, block, got)
            high = jnp.where(bit == 0, got, block)
            block = jnp.concatenate([low[None], high[None]], axis=0)
            block = block.reshape((-1,) + full.shape)
            distance *= 2
        full = block.reshape((-1,) + tokens.shape)
    return full

def padded_together(blocks, widths):
    for axis, dim in (("ha", 1), ("wa", 2)):
        count = lax.axis_size(axis)
        forward = [(i, i + 1) for i in range(count - 1)]
        backward = [(target, source) for source, target in forward]
        frames, chans = blocks[0].shape[0], blocks[0].shape[-1]

        def flat(parts):
            return jnp.concatenate([p.reshape(frames, -1, chans) for p in parts], axis=1)

        tails = [lax.slice_in_dim(b, b.shape[dim] - w, None, axis=dim) for b, w in zip(blocks, widths)]
        heads = [lax.slice_in_dim(b, 0, w, axis=dim) for b, w in zip(blocks, widths)]
        low = lax.ppermute(flat(tails), axis, forward)
        high = lax.ppermute(flat(heads), axis, backward)
        out, at = [], 0
        for b, t, h in zip(blocks, tails, heads):
            size = t.size // (frames * chans)
            got_low = low[:, at : at + size].reshape(t.shape)
            got_high = high[:, at : at + size].reshape(h.shape)
            at += size
            out.append(jnp.concatenate([got_low, b, got_high], axis=dim))
        blocks = out
    return blocks


def rms_norm(values, gain):
    scale = lax.rsqrt(jnp.mean(values * values, axis=-1, keepdims=True) + eps_norm)
    return values * scale * gain


def conv_valid(padded, kernel):
    return lax.conv_general_dilated(
        padded[None],
        kernel,
        (1, 1, 1),
        "VALID",
        dimension_numbers=("NDHWC", "DHWIO", "NDHWC"),
        preferred_element_type=jnp.float32,
    )[0]


def kernel_grad(padded, upstream):
    frames, rows, cols, chans = upstream.shape
    taps = []
    for tap_t in range(3):
        for tap_h in range(3):
            for tap_w in range(3):
                window = padded[tap_t : tap_t + frames, tap_h : tap_h + rows, tap_w : tap_w + cols]
                taps.append(
                    lax.dot_general(
                        window,
                        upstream,
                        (((0, 1, 2), (0, 1, 2)), ((), ())),
                        preferred_element_type=jnp.float32,
                    )
                )
    return jnp.stack(taps).reshape(3, 3, 3, chans, chans)


def norm_back(pre, gain, upstream):
    scale = lax.rsqrt(jnp.mean(pre * pre, axis=-1, keepdims=True) + eps_norm)
    normed = pre * scale
    gated = normed * gain
    sigma = jax.nn.sigmoid(gated)
    dgated = upstream * sigma * (1.0 + gated * (1.0 - sigma))
    dnormed = dgated * gain
    return scale * (dnormed - normed * jnp.mean(dnormed * normed, axis=-1, keepdims=True))


def attend(query, keys_all, values_all):
    width = query.shape[-1]
    scores = jnp.einsum(
        "fqc,fkc->fqk", query, keys_all, preferred_element_type=jnp.float32
    ) / math.sqrt(width)
    top = jnp.max(scores, axis=-1, keepdims=True)
    weights = jnp.exp(scores - top)
    probs = (weights / jnp.sum(weights, axis=-1, keepdims=True)).astype(jnp.bfloat16)
    return jnp.einsum("fqk,fkc->fqc", probs, values_all, preferred_element_type=jnp.float32).astype(
        jnp.bfloat16
    )


def causal_padded(block):
    earlier = shifted(block[-2:], "ta", 1)
    extended = jnp.concatenate([earlier, block], axis=0)
    return padded_2(extended, (("ha", 1), ("wa", 2)), 1)


def future_padded(block):
    later = shifted(block[:2], "ta", -1)
    extended = jnp.concatenate([block, later], axis=0)
    return padded_2(extended, (("ha", 1), ("wa", 2)), 1)


def local(
    clip,
    gain_attn,
    w_query,
    w_key,
    w_value,
    w_out,
    gain_one,
    w_one,
    bias_one,
    gain_two,
    w_two,
    bias_two,
    cotangent,
    crop_boxes,
):
    frames, rows, cols, chans = clip.shape
    n_ha, n_wa = lax.axis_size("ha"), lax.axis_size("wa")
    at_ha, at_wa = lax.axis_index("ha"), lax.axis_index("wa")
    clip_f = clip.astype(jnp.float32)
    pooled = (
        rms_norm(clip_f, gain_attn)
        .reshape(frames, rows // POOL, POOL, cols // POOL, POOL, chans)
        .mean(axis=(2, 4))
        .astype(jnp.bfloat16)
    )
    grid_rows, grid_cols = rows // POOL, cols // POOL
    full = gathered_tokens(pooled, ("ha", "wa")).reshape(
        n_ha, n_wa, frames, grid_rows, grid_cols, chans
    )
    grid = jnp.transpose(full, (2, 0, 3, 1, 4, 5)).reshape(
        frames, n_ha * grid_rows, n_wa * grid_cols, chans
    )
    tokens_all = grid.reshape(frames, -1, chans)
    keys_all = jnp.dot(tokens_all, w_key, preferred_element_type=jnp.float32).astype(jnp.bfloat16)
    values_all = jnp.dot(tokens_all, w_value, preferred_element_type=jnp.float32).astype(
        jnp.bfloat16
    )
    near = lax.dynamic_slice(
        jnp.pad(grid, ((0, 0), (1, 1), (1, 1), (0, 0))),
        (0, at_ha * grid_rows, at_wa * grid_cols, 0),
        (frames, grid_rows + 2, grid_cols + 2, chans),
    )
    query = jnp.dot(
        near.reshape(frames, -1, chans), w_query, preferred_element_type=jnp.float32
    ).astype(jnp.bfloat16)
    mixed = attend(query, keys_all, values_all)
    projected = jnp.dot(mixed, w_out, preferred_element_type=jnp.float32).reshape(
        frames, grid_rows + 2, grid_cols + 2, chans
    )
    upsampled = jnp.repeat(jnp.repeat(projected, POOL, axis=1), POOL, axis=2)
    upsampled = upsampled[:, POOL - 2 : POOL + rows + 2, POOL - 2 : POOL + cols + 2]
    bounds = crop_boxes[0, 0]
    local_row = jnp.arange(rows)[:, None]
    local_col = jnp.arange(cols)[None, :]
    inside = (
        (local_row >= bounds[0])
        & (local_row < bounds[1])
        & (local_col >= bounds[2])
        & (local_col < bounds[3])
    )
    masked = cotangent * inside.astype(jnp.bfloat16)[None, :, :, None]
    clip_wide, masked_wide = padded_together([clip, masked], [2, 1])
    clip_wide = clip_wide.astype(jnp.float32)
    masked_future = jnp.concatenate([masked_wide, shifted(masked_wide[:2], "ta", -1)], axis=0)
    attended_wide = (clip_wide + upsampled).astype(jnp.bfloat16)
    attended = attended_wide[:, 2 : 2 + rows, 2 : 2 + cols]

    def inside_frame(border):
        row_ids = at_ha * rows - border + jnp.arange(rows + 2 * border)
        col_ids = at_wa * cols - border + jnp.arange(cols + 2 * border)
        row_ok = (row_ids >= 0) & (row_ids < n_ha * rows)
        col_ok = (col_ids >= 0) & (col_ids < n_wa * cols)
        return (row_ok[:, None] & col_ok[None, :])[None, :, :, None]

    act_one_wide = jax.nn.silu(rms_norm(attended_wide.astype(jnp.float32), gain_one)).astype(
        jnp.bfloat16
    )
    act_one_wide = jnp.where(inside_frame(2), act_one_wide, jnp.zeros_like(act_one_wide))
    padded_one_wide = jnp.concatenate([shifted(act_one_wide[-2:], "ta", 1), act_one_wide], axis=0)
    pre_two_wide = conv_valid(padded_one_wide, w_one) + bias_one
    act_two_wide = jax.nn.silu(rms_norm(pre_two_wide, gain_two)).astype(jnp.bfloat16)
    act_two_wide = jnp.where(inside_frame(1), act_two_wide, jnp.zeros_like(act_two_wide))
    padded_two = jnp.concatenate([shifted(act_two_wide[-2:], "ta", 1), act_two_wide], axis=0)
    padded_one = padded_one_wide[:, 1 : 3 + rows, 1 : 3 + cols]
    pre_two = pre_two_wide[:, 1 : 1 + rows, 1 : 1 + cols]
    block_out = (attended.astype(jnp.float32) + conv_valid(padded_two, w_two) + bias_two).astype(
        jnp.bfloat16
    )
    total_pixels = (
        frames * lax.axis_size("ta") * rows * lax.axis_size("ha") * cols * lax.axis_size("wa")
    )
    norm_scale = 1.0 / math.sqrt(total_pixels)
    local_two = kernel_grad(padded_two, masked)
    flipped = jnp.transpose(w_two[::-1, ::-1, ::-1], (0, 1, 2, 4, 3))
    back_two = conv_valid(masked_future, flipped)
    back_one = norm_back(pre_two, gain_two, back_two).astype(jnp.bfloat16)
    local_one = kernel_grad(padded_one, back_one)
    summed_two = summed_over(local_two, ("ta", "wa", "ha"))
    summed_one = summed_over(local_one, ("ta", "wa", "ha"))
    return (block_out, summed_one * norm_scale, summed_two * norm_scale)


def solution(mesh):
    in_specs = (
        P(("groups", "ta"), "ha", "wa", None),
        P(),
        P(),
        P(),
        P(),
        P(),
        P(),
        P(),
        P(),
        P(),
        P(),
        P(),
        P(("groups", "ta"), "ha", "wa", None),
        P(("groups", "ha"), "wa", None),
    )
    out_specs = (
        P(("groups", "ta"), "ha", "wa", None),
        P("groups", None, None, None, None),
        P("groups", None, None, None, None),
    )
    return jax.shard_map(local, mesh=mesh, in_specs=in_specs, out_specs=out_specs, check_vma=False)
```

```python
import math

import jax
import jax.numpy as jnp
from jax import lax
from jax.experimental import pallas as pl
from jax.sharding import PartitionSpec as P

POOL = 4


eps_norm = 1e-06


def shifted(x, axis, by):
    size = lax.axis_size(axis)
    pairs = [(i, i + by) for i in range(size) if 0 <= i + by < size]
    return lax.ppermute(x, axis, pairs)


def padded_2(block, sides, width):
    for axis, dim in sides:
        count = lax.axis_size(axis)
        forward = [(i, i + 1) for i in range(count - 1)]
        backward = [(target, source) for source, target in forward]
        low = lax.ppermute(
            lax.slice_in_dim(block, block.shape[dim] - width, None, axis=dim), axis, forward
        )
        high = lax.ppermute(lax.slice_in_dim(block, 0, width, axis=dim), axis, backward)
        block = jnp.concatenate([low, block, high], axis=dim)
    return block


def halving_stages(axes):
    out = []
    for axis in axes:
        count = lax.axis_size(axis)
        distance = 1
        while distance < count:
            out.append((axis, distance, count))
            distance *= 2
    return out


def reduce_scatter_rows(x, stages):
    for axis, distance, count in stages:
        bit = (lax.axis_index(axis) // distance) % 2
        half = x.shape[0] // 2
        keep = lax.dynamic_slice_in_dim(x, bit * half, half)
        send = lax.dynamic_slice_in_dim(x, (1 - bit) * half, half)
        pairs = [(j, j ^ distance) for j in range(count)]
        x = keep + lax.ppermute(send, axis, pairs)
    return x


def all_gather_rows(x, stages):
    for axis, distance, count in reversed(stages):
        bit = (lax.axis_index(axis) // distance) % 2
        pairs = [(j, j ^ distance) for j in range(count)]
        got = lax.ppermute(x, axis, pairs)
        low = jnp.where(bit == 0, x, got)
        high = jnp.where(bit == 0, got, x)
        x = jnp.concatenate([low, high], axis=0)
    return x


def summed_over(value, axes, chunks=1):
    sizes = [lax.axis_size(axis) for axis in axes]
    if any(size & (size - 1) for size in sizes):
        return lax.psum(value, axes)
    stages = halving_stages(axes)
    rows = value.reshape(-1, value.shape[-1])
    while chunks > 1 and rows.shape[0] % (chunks << len(stages)):
        chunks //= 2
    if rows.shape[0] % (chunks << len(stages)):
        return lax.psum(value, axes)
    pieces = jnp.split(rows, chunks, axis=0)
    joined = [all_gather_rows(reduce_scatter_rows(piece, stages), stages) for piece in pieces]
    return jnp.concatenate(joined, axis=0).reshape(value.shape)


def gathered_tokens(tokens, axes):
    sizes = [lax.axis_size(axis) for axis in axes]
    if any(size & (size - 1) for size in sizes):
        return lax.all_gather(tokens, axes, axis=0)
    full = tokens[None]
    for axis, size in reversed(list(zip(axes, sizes))):
        block = full
        distance = 1
        while distance < size:
            bit = (lax.axis_index(axis) // distance) % 2
            pairs = [(j, j ^ distance) for j in range(size)]
            got = lax.ppermute(block, axis, pairs)
            low = jnp.where(bit == 0, block, got)
            high = jnp.where(bit == 0, got, block)
            block = jnp.concatenate([low[None], high[None]], axis=0)
            block = block.reshape((-1,) + full.shape)
            distance *= 2
        full = block.reshape((-1,) + tokens.shape)
    return full

def padded_together(blocks, widths):
    for axis, dim in (("ha", 1), ("wa", 2)):
        count = lax.axis_size(axis)
        forward = [(i, i + 1) for i in range(count - 1)]
        backward = [(target, source) for source, target in forward]
        frames, chans = blocks[0].shape[0], blocks[0].shape[-1]

        def flat(parts):
            return jnp.concatenate([p.reshape(frames, -1, chans) for p in parts], axis=1)

        tails = [lax.slice_in_dim(b, b.shape[dim] - w, None, axis=dim) for b, w in zip(blocks, widths)]
        heads = [lax.slice_in_dim(b, 0, w, axis=dim) for b, w in zip(blocks, widths)]
        low = lax.ppermute(flat(tails), axis, forward)
        high = lax.ppermute(flat(heads), axis, backward)
        out, at = [], 0
        for b, t, h in zip(blocks, tails, heads):
            size = t.size // (frames * chans)
            got_low = low[:, at : at + size].reshape(t.shape)
            got_high = high[:, at : at + size].reshape(h.shape)
            at += size
            out.append(jnp.concatenate([got_low, b, got_high], axis=dim))
        blocks = out
    return blocks


def rms_norm(values, gain):
    scale = lax.rsqrt(jnp.mean(values * values, axis=-1, keepdims=True) + eps_norm)
    return values * scale * gain


def conv_valid(padded, kernel):
    return lax.conv_general_dilated(
        padded[None],
        kernel,
        (1, 1, 1),
        "VALID",
        dimension_numbers=("NDHWC", "DHWIO", "NDHWC"),
        preferred_element_type=jnp.float32,
    )[0]


def taps_kernel(shifted_ref, upstream_t_ref, out_ref):
    _, frames_in, rows_in, cols, chans = shifted_ref.shape
    frames, rows = frames_in - 2, rows_in - 2
    upstream_t = upstream_t_ref[...]
    for tap_t in range(3):
        for tap_h in range(3):
            for tap_w in range(3):
                window = shifted_ref[tap_w, tap_t : tap_t + frames, tap_h : tap_h + rows]
                out_ref[(tap_t * 3 + tap_h) * 3 + tap_w] = jnp.dot(
                    upstream_t,
                    window.reshape(frames * rows * cols, chans),
                    preferred_element_type=jnp.float32,
                )


def kernel_grad(padded, upstream):
    frames, rows, cols, chans = upstream.shape
    shifted = jnp.stack([padded[:, :, tap_w : tap_w + cols] for tap_w in range(3)])
    upstream_t = upstream.reshape(-1, chans).T
    taps = pl.pallas_call(
        taps_kernel,
        out_shape=jax.ShapeDtypeStruct((27, chans, padded.shape[-1]), jnp.float32),
    )(shifted, upstream_t)
    return jnp.transpose(taps, (0, 2, 1)).reshape(3, 3, 3, padded.shape[-1], chans)


def norm_back(pre, gain, upstream):
    scale = lax.rsqrt(jnp.mean(pre * pre, axis=-1, keepdims=True) + eps_norm)
    normed = pre * scale
    gated = normed * gain
    sigma = jax.nn.sigmoid(gated)
    dgated = upstream * sigma * (1.0 + gated * (1.0 - sigma))
    dnormed = dgated * gain
    return scale * (dnormed - normed * jnp.mean(dnormed * normed, axis=-1, keepdims=True))


def attend(query, keys_all, values_all):
    width = query.shape[-1]
    scores = jnp.einsum(
        "fqc,fkc->fqk", query, keys_all, preferred_element_type=jnp.float32
    ) / math.sqrt(width)
    top = jnp.max(scores, axis=-1, keepdims=True)
    weights = jnp.exp(scores - top)
    probs = (weights / jnp.sum(weights, axis=-1, keepdims=True)).astype(jnp.bfloat16)
    return jnp.einsum("fqk,fkc->fqc", probs, values_all, preferred_element_type=jnp.float32).astype(
        jnp.bfloat16
    )


def causal_padded(block):
    earlier = shifted(block[-2:], "ta", 1)
    extended = jnp.concatenate([earlier, block], axis=0)
    return padded_2(extended, (("ha", 1), ("wa", 2)), 1)


def future_padded(block):
    later = shifted(block[:2], "ta", -1)
    extended = jnp.concatenate([block, later], axis=0)
    return padded_2(extended, (("ha", 1), ("wa", 2)), 1)


def local(
    clip,
    gain_attn,
    w_query,
    w_key,
    w_value,
    w_out,
    gain_one,
    w_one,
    bias_one,
    gain_two,
    w_two,
    bias_two,
    cotangent,
    crop_boxes,
):
    frames, rows, cols, chans = clip.shape
    n_ha, n_wa = lax.axis_size("ha"), lax.axis_size("wa")
    at_ha, at_wa = lax.axis_index("ha"), lax.axis_index("wa")
    clip_f = clip.astype(jnp.float32)
    pooled = (
        rms_norm(clip_f, gain_attn)
        .reshape(frames, rows // POOL, POOL, cols // POOL, POOL, chans)
        .mean(axis=(2, 4))
        .astype(jnp.bfloat16)
    )
    grid_rows, grid_cols = rows // POOL, cols // POOL
    full = gathered_tokens(pooled, ("ha", "wa")).reshape(
        n_ha, n_wa, frames, grid_rows, grid_cols, chans
    )
    grid = jnp.transpose(full, (2, 0, 3, 1, 4, 5)).reshape(
        frames, n_ha * grid_rows, n_wa * grid_cols, chans
    )
    tokens_all = grid.reshape(frames, -1, chans)
    keys_all = jnp.dot(tokens_all, w_key, preferred_element_type=jnp.float32).astype(jnp.bfloat16)
    values_all = jnp.dot(tokens_all, w_value, preferred_element_type=jnp.float32).astype(
        jnp.bfloat16
    )
    near = lax.dynamic_slice(
        jnp.pad(grid, ((0, 0), (1, 1), (1, 1), (0, 0))),
        (0, at_ha * grid_rows, at_wa * grid_cols, 0),
        (frames, grid_rows + 2, grid_cols + 2, chans),
    )
    query = jnp.dot(
        near.reshape(frames, -1, chans), w_query, preferred_element_type=jnp.float32
    ).astype(jnp.bfloat16)
    mixed = attend(query, keys_all, values_all)
    projected = jnp.dot(mixed, w_out, preferred_element_type=jnp.float32).reshape(
        frames, grid_rows + 2, grid_cols + 2, chans
    )
    upsampled = jnp.repeat(jnp.repeat(projected, POOL, axis=1), POOL, axis=2)
    upsampled = upsampled[:, POOL - 2 : POOL + rows + 2, POOL - 2 : POOL + cols + 2]
    bounds = crop_boxes[0, 0]
    local_row = jnp.arange(rows)[:, None]
    local_col = jnp.arange(cols)[None, :]
    inside = (
        (local_row >= bounds[0])
        & (local_row < bounds[1])
        & (local_col >= bounds[2])
        & (local_col < bounds[3])
    )
    masked = cotangent * inside.astype(jnp.bfloat16)[None, :, :, None]
    clip_wide, masked_wide = padded_together([clip, masked], [2, 1])
    clip_wide = clip_wide.astype(jnp.float32)
    masked_future = jnp.concatenate([masked_wide, shifted(masked_wide[:2], "ta", -1)], axis=0)
    attended_wide = (clip_wide + upsampled).astype(jnp.bfloat16)
    attended = attended_wide[:, 2 : 2 + rows, 2 : 2 + cols]

    def inside_frame(border):
        row_ids = at_ha * rows - border + jnp.arange(rows + 2 * border)
        col_ids = at_wa * cols - border + jnp.arange(cols + 2 * border)
        row_ok = (row_ids >= 0) & (row_ids < n_ha * rows)
        col_ok = (col_ids >= 0) & (col_ids < n_wa * cols)
        return (row_ok[:, None] & col_ok[None, :])[None, :, :, None]

    act_one_wide = jax.nn.silu(rms_norm(attended_wide.astype(jnp.float32), gain_one)).astype(
        jnp.bfloat16
    )
    act_one_wide = jnp.where(inside_frame(2), act_one_wide, jnp.zeros_like(act_one_wide))
    padded_one_wide = jnp.concatenate([shifted(act_one_wide[-2:], "ta", 1), act_one_wide], axis=0)
    pre_two_wide = conv_valid(padded_one_wide, w_one) + bias_one
    act_two_wide = jax.nn.silu(rms_norm(pre_two_wide, gain_two)).astype(jnp.bfloat16)
    act_two_wide = jnp.where(inside_frame(1), act_two_wide, jnp.zeros_like(act_two_wide))
    padded_two = jnp.concatenate([shifted(act_two_wide[-2:], "ta", 1), act_two_wide], axis=0)
    padded_one = padded_one_wide[:, 1 : 3 + rows, 1 : 3 + cols]
    pre_two = pre_two_wide[:, 1 : 1 + rows, 1 : 1 + cols]
    block_out = (attended.astype(jnp.float32) + conv_valid(padded_two, w_two) + bias_two).astype(
        jnp.bfloat16
    )
    total_pixels = (
        frames * lax.axis_size("ta") * rows * lax.axis_size("ha") * cols * lax.axis_size("wa")
    )
    norm_scale = 1.0 / math.sqrt(total_pixels)
    local_two = kernel_grad(padded_two, masked)
    flipped = jnp.transpose(w_two[::-1, ::-1, ::-1], (0, 1, 2, 4, 3))
    back_two = conv_valid(masked_future, flipped)
    back_one = norm_back(pre_two, gain_two, back_two).astype(jnp.bfloat16)
    local_one = kernel_grad(padded_one, back_one)
    summed_two = summed_over(local_two, ("ta", "wa", "ha"))
    summed_one = summed_over(local_one, ("ta", "wa", "ha"))
    return (block_out, summed_one * norm_scale, summed_two * norm_scale)


def solution(mesh):
    in_specs = (
        P(("groups", "ta"), "ha", "wa", None),
        P(),
        P(),
        P(),
        P(),
        P(),
        P(),
        P(),
        P(),
        P(),
        P(),
        P(),
        P(("groups", "ta"), "ha", "wa", None),
        P(("groups", "ha"), "wa", None),
    )
    out_specs = (
        P(("groups", "ta"), "ha", "wa", None),
        P("groups", None, None, None, None),
        P("groups", None, None, None, None),
    )
    return jax.shard_map(local, mesh=mesh, in_specs=in_specs, out_specs=out_specs, check_vma=False)
```

```python
import math

import jax
import jax.numpy as jnp
from jax import lax
from jax.sharding import PartitionSpec as P

POOL = 4


eps_norm = 1e-06


def shifted(x, axis, by):
    size = lax.axis_size(axis)
    pairs = [(i, i + by) for i in range(size) if 0 <= i + by < size]
    return lax.ppermute(x, axis, pairs)


def padded_2(block, sides, width):
    for axis, dim in sides:
        count = lax.axis_size(axis)
        forward = [(i, i + 1) for i in range(count - 1)]
        backward = [(target, source) for source, target in forward]
        low = lax.ppermute(
            lax.slice_in_dim(block, block.shape[dim] - width, None, axis=dim), axis, forward
        )
        high = lax.ppermute(lax.slice_in_dim(block, 0, width, axis=dim), axis, backward)
        block = jnp.concatenate([low, block, high], axis=dim)
    return block


def halving_stages(axes):
    out = []
    for axis in axes:
        count = lax.axis_size(axis)
        distance = 1
        while distance < count:
            out.append((axis, distance, count))
            distance *= 2
    return out


def reduce_scatter_rows(x, stages):
    for axis, distance, count in stages:
        bit = (lax.axis_index(axis) // distance) % 2
        half = x.shape[0] // 2
        keep = lax.dynamic_slice_in_dim(x, bit * half, half)
        send = lax.dynamic_slice_in_dim(x, (1 - bit) * half, half)
        pairs = [(j, j ^ distance) for j in range(count)]
        x = keep + lax.ppermute(send, axis, pairs)
    return x


def all_gather_rows(x, stages):
    for axis, distance, count in reversed(stages):
        bit = (lax.axis_index(axis) // distance) % 2
        pairs = [(j, j ^ distance) for j in range(count)]
        got = lax.ppermute(x, axis, pairs)
        low = jnp.where(bit == 0, x, got)
        high = jnp.where(bit == 0, got, x)
        x = jnp.concatenate([low, high], axis=0)
    return x


def summed_over(value, axes, chunks=1):
    sizes = [lax.axis_size(axis) for axis in axes]
    if any(size & (size - 1) for size in sizes):
        return lax.psum(value, axes)
    stages = halving_stages(axes)
    rows = value.reshape(-1, value.shape[-1])
    while chunks > 1 and rows.shape[0] % (chunks << len(stages)):
        chunks //= 2
    if rows.shape[0] % (chunks << len(stages)):
        return lax.psum(value, axes)
    pieces = jnp.split(rows, chunks, axis=0)
    joined = [all_gather_rows(reduce_scatter_rows(piece, stages), stages) for piece in pieces]
    return jnp.concatenate(joined, axis=0).reshape(value.shape)


def gathered_tokens(tokens, axes):
    sizes = [lax.axis_size(axis) for axis in axes]
    if any(size & (size - 1) for size in sizes):
        return lax.all_gather(tokens, axes, axis=0)
    full = tokens[None]
    for axis, size in reversed(list(zip(axes, sizes))):
        block = full
        distance = 1
        while distance < size:
            bit = (lax.axis_index(axis) // distance) % 2
            pairs = [(j, j ^ distance) for j in range(size)]
            got = lax.ppermute(block, axis, pairs)
            low = jnp.where(bit == 0, block, got)
            high = jnp.where(bit == 0, got, block)
            block = jnp.concatenate([low[None], high[None]], axis=0)
            block = block.reshape((-1,) + full.shape)
            distance *= 2
        full = block.reshape((-1,) + tokens.shape)
    return full

def padded_together(blocks, widths):
    for axis, dim in (("ha", 1), ("wa", 2)):
        count = lax.axis_size(axis)
        forward = [(i, i + 1) for i in range(count - 1)]
        backward = [(target, source) for source, target in forward]
        frames, chans = blocks[0].shape[0], blocks[0].shape[-1]

        def flat(parts):
            return jnp.concatenate([p.reshape(frames, -1, chans) for p in parts], axis=1)

        tails = [lax.slice_in_dim(b, b.shape[dim] - w, None, axis=dim) for b, w in zip(blocks, widths)]
        heads = [lax.slice_in_dim(b, 0, w, axis=dim) for b, w in zip(blocks, widths)]
        low = lax.ppermute(flat(tails), axis, forward)
        high = lax.ppermute(flat(heads), axis, backward)
        out, at = [], 0
        for b, t, h in zip(blocks, tails, heads):
            size = t.size // (frames * chans)
            got_low = low[:, at : at + size].reshape(t.shape)
            got_high = high[:, at : at + size].reshape(h.shape)
            at += size
            out.append(jnp.concatenate([got_low, b, got_high], axis=dim))
        blocks = out
    return blocks


def rms_norm(values, gain):
    scale = lax.rsqrt(jnp.mean(values * values, axis=-1, keepdims=True) + eps_norm)
    return values * scale * gain


def conv_valid(padded, kernel):
    return lax.conv_general_dilated(
        padded[None],
        kernel,
        (1, 1, 1),
        "VALID",
        dimension_numbers=("NDHWC", "DHWIO", "NDHWC"),
        preferred_element_type=jnp.float32,
    )[0]


def kernel_grad(padded, upstream):
    frames, rows, cols, chans = upstream.shape
    taps = []
    for tap_t in range(3):
        for tap_h in range(3):
            for tap_w in range(3):
                window = padded[tap_t : tap_t + frames, tap_h : tap_h + rows, tap_w : tap_w + cols]
                taps.append(
                    lax.dot_general(
                        window,
                        upstream,
                        (((0, 1, 2), (0, 1, 2)), ((), ())),
                        preferred_element_type=jnp.float32,
                    )
                )
    return jnp.stack(taps).reshape(3, 3, 3, chans, chans)


def norm_back(pre, gain, upstream):
    scale = lax.rsqrt(jnp.mean(pre * pre, axis=-1, keepdims=True) + eps_norm)
    normed = pre * scale
    gated = normed * gain
    sigma = jax.nn.sigmoid(gated)
    dgated = upstream * sigma * (1.0 + gated * (1.0 - sigma))
    dnormed = dgated * gain
    return scale * (dnormed - normed * jnp.mean(dnormed * normed, axis=-1, keepdims=True))


def attend(query, keys_all, values_all):
    width = query.shape[-1]
    scores = jnp.einsum(
        "fqc,fkc->fqk", query, keys_all, preferred_element_type=jnp.float32
    ) / math.sqrt(width)
    top = jnp.max(scores, axis=-1, keepdims=True)
    weights = jnp.exp(scores - top)
    probs = (weights / jnp.sum(weights, axis=-1, keepdims=True)).astype(jnp.bfloat16)
    return jnp.einsum("fqk,fkc->fqc", probs, values_all, preferred_element_type=jnp.float32).astype(
        jnp.bfloat16
    )


def causal_padded(block):
    earlier = shifted(block[-2:], "ta", 1)
    extended = jnp.concatenate([earlier, block], axis=0)
    return padded_2(extended, (("ha", 1), ("wa", 2)), 1)


def future_padded(block):
    later = shifted(block[:2], "ta", -1)
    extended = jnp.concatenate([block, later], axis=0)
    return padded_2(extended, (("ha", 1), ("wa", 2)), 1)


def local(
    clip,
    gain_attn,
    w_query,
    w_key,
    w_value,
    w_out,
    gain_one,
    w_one,
    bias_one,
    gain_two,
    w_two,
    bias_two,
    cotangent,
    crop_boxes,
):
    frames, rows, cols, chans = clip.shape
    n_ha, n_wa = lax.axis_size("ha"), lax.axis_size("wa")
    at_ha, at_wa = lax.axis_index("ha"), lax.axis_index("wa")
    clip_f = clip.astype(jnp.float32)
    pooled = (
        rms_norm(clip_f, gain_attn)
        .reshape(frames, rows // POOL, POOL, cols // POOL, POOL, chans)
        .mean(axis=(2, 4))
        .astype(jnp.bfloat16)
    )
    grid_rows, grid_cols = rows // POOL, cols // POOL
    full = gathered_tokens(pooled, ("ha", "wa")).reshape(
        n_ha, n_wa, frames, grid_rows, grid_cols, chans
    )
    grid = jnp.transpose(full, (2, 0, 3, 1, 4, 5)).reshape(
        frames, n_ha * grid_rows, n_wa * grid_cols, chans
    )
    tokens_all = grid.reshape(frames, -1, chans)
    keys_all = jnp.dot(tokens_all, w_key, preferred_element_type=jnp.float32).astype(jnp.bfloat16)
    values_all = jnp.dot(tokens_all, w_value, preferred_element_type=jnp.float32).astype(
        jnp.bfloat16
    )
    near = lax.dynamic_slice(
        jnp.pad(grid, ((0, 0), (1, 1), (1, 1), (0, 0))),
        (0, at_ha * grid_rows, at_wa * grid_cols, 0),
        (frames, grid_rows + 2, grid_cols + 2, chans),
    )
    query = jnp.dot(
        near.reshape(frames, -1, chans), w_query, preferred_element_type=jnp.float32
    ).astype(jnp.bfloat16)
    mixed = attend(query, keys_all, values_all)
    projected = jnp.dot(mixed, w_out, preferred_element_type=jnp.float32).reshape(
        frames, grid_rows + 2, grid_cols + 2, chans
    )
    upsampled = jnp.repeat(jnp.repeat(projected, POOL, axis=1), POOL, axis=2)
    upsampled = upsampled[:, POOL - 2 : POOL + rows + 2, POOL - 2 : POOL + cols + 2]
    bounds = crop_boxes[0, 0]
    local_row = jnp.arange(rows)[:, None]
    local_col = jnp.arange(cols)[None, :]
    inside = (
        (local_row >= bounds[0])
        & (local_row < bounds[1])
        & (local_col >= bounds[2])
        & (local_col < bounds[3])
    )
    masked = cotangent * inside.astype(jnp.bfloat16)[None, :, :, None]
    clip_wide, masked_wide = padded_together([clip, masked], [2, 1])
    clip_wide = clip_wide.astype(jnp.float32)
    masked_future = jnp.concatenate([masked_wide, shifted(masked_wide[:2], "ta", -1)], axis=0)
    attended_wide = (clip_wide + upsampled).astype(jnp.bfloat16)
    attended = attended_wide[:, 2 : 2 + rows, 2 : 2 + cols]

    def inside_frame(border):
        row_ids = at_ha * rows - border + jnp.arange(rows + 2 * border)
        col_ids = at_wa * cols - border + jnp.arange(cols + 2 * border)
        row_ok = (row_ids >= 0) & (row_ids < n_ha * rows)
        col_ok = (col_ids >= 0) & (col_ids < n_wa * cols)
        return (row_ok[:, None] & col_ok[None, :])[None, :, :, None]

    act_one_wide = jax.nn.silu(rms_norm(attended_wide.astype(jnp.float32), gain_one)).astype(
        jnp.bfloat16
    )
    act_one_wide = jnp.where(inside_frame(2), act_one_wide, jnp.zeros_like(act_one_wide))
    padded_one_wide = jnp.concatenate([shifted(act_one_wide[-2:], "ta", 1), act_one_wide], axis=0)
    pre_two_wide = conv_valid(padded_one_wide, w_one) + bias_one
    act_two_wide = jax.nn.silu(rms_norm(pre_two_wide, gain_two)).astype(jnp.bfloat16)
    act_two_wide = jnp.where(inside_frame(1), act_two_wide, jnp.zeros_like(act_two_wide))
    padded_two = jnp.concatenate([shifted(act_two_wide[-2:], "ta", 1), act_two_wide], axis=0)
    padded_one = padded_one_wide[:, 1 : 3 + rows, 1 : 3 + cols]
    pre_two = pre_two_wide[:, 1 : 1 + rows, 1 : 1 + cols]
    total_pixels = (
        frames * lax.axis_size("ta") * rows * lax.axis_size("ha") * cols * lax.axis_size("wa")
    )
    norm_scale = 1.0 / math.sqrt(total_pixels)
    local_two = kernel_grad(padded_two, masked)
    flipped = jnp.transpose(w_two[::-1, ::-1, ::-1], (0, 1, 2, 4, 3))
    back_two = conv_valid(masked_future, flipped)
    back_one = norm_back(pre_two, gain_two, back_two).astype(jnp.bfloat16)
    local_one = kernel_grad(padded_one, back_one)
    padded_two, local_one, local_two = lax.optimization_barrier((padded_two, local_one, local_two))
    block_out = (attended.astype(jnp.float32) + conv_valid(padded_two, w_two) + bias_two).astype(
        jnp.bfloat16
    )
    summed_two = summed_over(local_two, ("ta", "wa", "ha"))
    summed_one = summed_over(local_one, ("ta", "wa", "ha"))
    return (block_out, summed_one * norm_scale, summed_two * norm_scale)


def solution(mesh):
    in_specs = (
        P(("groups", "ta"), "ha", "wa", None),
        P(),
        P(),
        P(),
        P(),
        P(),
        P(),
        P(),
        P(),
        P(),
        P(),
        P(),
        P(("groups", "ta"), "ha", "wa", None),
        P(("groups", "ha"), "wa", None),
    )
    out_specs = (
        P(("groups", "ta"), "ha", "wa", None),
        P("groups", None, None, None, None),
        P("groups", None, None, None, None),
    )
    return jax.shard_map(local, mesh=mesh, in_specs=in_specs, out_specs=out_specs, check_vma=False)
```

```python
import math

import jax
import jax.numpy as jnp
from jax import lax
from jax.sharding import PartitionSpec as P

POOL = 4


eps_norm = 1e-06


def shifted(x, axis, by):
    size = lax.axis_size(axis)
    pairs = [(i, i + by) for i in range(size) if 0 <= i + by < size]
    return lax.ppermute(x, axis, pairs)


def padded_2(block, sides, width):
    for axis, dim in sides:
        count = lax.axis_size(axis)
        forward = [(i, i + 1) for i in range(count - 1)]
        backward = [(target, source) for source, target in forward]
        low = lax.ppermute(
            lax.slice_in_dim(block, block.shape[dim] - width, None, axis=dim), axis, forward
        )
        high = lax.ppermute(lax.slice_in_dim(block, 0, width, axis=dim), axis, backward)
        block = jnp.concatenate([low, block, high], axis=dim)
    return block


def halving_stages(axes):
    out = []
    for axis in axes:
        count = lax.axis_size(axis)
        distance = 1
        while distance < count:
            out.append((axis, distance, count))
            distance *= 2
    return out


def reduce_scatter_rows(x, stages):
    for axis, distance, count in stages:
        bit = (lax.axis_index(axis) // distance) % 2
        half = x.shape[0] // 2
        keep = lax.dynamic_slice_in_dim(x, bit * half, half)
        send = lax.dynamic_slice_in_dim(x, (1 - bit) * half, half)
        pairs = [(j, j ^ distance) for j in range(count)]
        x = keep + lax.ppermute(send, axis, pairs)
    return x


def all_gather_rows(x, stages):
    for axis, distance, count in reversed(stages):
        bit = (lax.axis_index(axis) // distance) % 2
        pairs = [(j, j ^ distance) for j in range(count)]
        got = lax.ppermute(x, axis, pairs)
        low = jnp.where(bit == 0, x, got)
        high = jnp.where(bit == 0, got, x)
        x = jnp.concatenate([low, high], axis=0)
    return x


def summed_over(value, axes, chunks=1):
    sizes = [lax.axis_size(axis) for axis in axes]
    if any(size & (size - 1) for size in sizes):
        return lax.psum(value, axes)
    stages = halving_stages(axes)
    rows = value.reshape(-1, value.shape[-1])
    while chunks > 1 and rows.shape[0] % (chunks << len(stages)):
        chunks //= 2
    if rows.shape[0] % (chunks << len(stages)):
        return lax.psum(value, axes)
    pieces = jnp.split(rows, chunks, axis=0)
    joined = [all_gather_rows(reduce_scatter_rows(piece, stages), stages) for piece in pieces]
    return jnp.concatenate(joined, axis=0).reshape(value.shape)


def gathered_tokens(tokens, axes):
    sizes = [lax.axis_size(axis) for axis in axes]
    if any(size & (size - 1) for size in sizes):
        return lax.all_gather(tokens, axes, axis=0)
    full = tokens[None]
    for axis, size in reversed(list(zip(axes, sizes))):
        block = full
        distance = 1
        while distance < size:
            bit = (lax.axis_index(axis) // distance) % 2
            pairs = [(j, j ^ distance) for j in range(size)]
            got = lax.ppermute(block, axis, pairs)
            low = jnp.where(bit == 0, block, got)
            high = jnp.where(bit == 0, got, block)
            block = jnp.concatenate([low[None], high[None]], axis=0)
            block = block.reshape((-1,) + full.shape)
            distance *= 2
        full = block.reshape((-1,) + tokens.shape)
    return full

def padded_together(blocks, widths):
    for axis, dim in (("ha", 1), ("wa", 2)):
        count = lax.axis_size(axis)
        forward = [(i, i + 1) for i in range(count - 1)]
        backward = [(target, source) for source, target in forward]
        frames, chans = blocks[0].shape[0], blocks[0].shape[-1]

        def flat(parts):
            return jnp.concatenate([p.reshape(frames, -1, chans) for p in parts], axis=1)

        tails = [lax.slice_in_dim(b, b.shape[dim] - w, None, axis=dim) for b, w in zip(blocks, widths)]
        heads = [lax.slice_in_dim(b, 0, w, axis=dim) for b, w in zip(blocks, widths)]
        low = lax.ppermute(flat(tails), axis, forward)
        high = lax.ppermute(flat(heads), axis, backward)
        out, at = [], 0
        for b, t, h in zip(blocks, tails, heads):
            size = t.size // (frames * chans)
            got_low = low[:, at : at + size].reshape(t.shape)
            got_high = high[:, at : at + size].reshape(h.shape)
            at += size
            out.append(jnp.concatenate([got_low, b, got_high], axis=dim))
        blocks = out
    return blocks


def rms_norm(values, gain):
    scale = lax.rsqrt(jnp.mean(values * values, axis=-1, keepdims=True) + eps_norm)
    return values * scale * gain


def conv_valid(padded, kernel):
    return lax.conv_general_dilated(
        padded[None],
        kernel,
        (1, 1, 1),
        "VALID",
        dimension_numbers=("NDHWC", "DHWIO", "NDHWC"),
        preferred_element_type=jnp.float32,
    )[0]


def conv_causal(earlier, block, kernel):
    late = conv_valid(block, kernel)
    early = conv_valid(jnp.concatenate([earlier, block[:2]], axis=0), kernel)
    return jnp.concatenate([early, late], axis=0)


def kernel_grad(padded, upstream):
    frames, rows, cols, chans = upstream.shape
    taps = []
    for tap_t in range(3):
        for tap_h in range(3):
            for tap_w in range(3):
                window = padded[tap_t : tap_t + frames, tap_h : tap_h + rows, tap_w : tap_w + cols]
                taps.append(
                    lax.dot_general(
                        window,
                        upstream,
                        (((0, 1, 2), (0, 1, 2)), ((), ())),
                        preferred_element_type=jnp.float32,
                    )
                )
    return jnp.stack(taps).reshape(3, 3, 3, chans, chans)


def norm_back(pre, gain, upstream):
    scale = lax.rsqrt(jnp.mean(pre * pre, axis=-1, keepdims=True) + eps_norm)
    normed = pre * scale
    gated = normed * gain
    sigma = jax.nn.sigmoid(gated)
    dgated = upstream * sigma * (1.0 + gated * (1.0 - sigma))
    dnormed = dgated * gain
    return scale * (dnormed - normed * jnp.mean(dnormed * normed, axis=-1, keepdims=True))


def attend(query, keys_all, values_all):
    width = query.shape[-1]
    scores = jnp.einsum(
        "fqc,fkc->fqk", query, keys_all, preferred_element_type=jnp.float32
    ) / math.sqrt(width)
    top = jnp.max(scores, axis=-1, keepdims=True)
    weights = jnp.exp(scores - top)
    probs = (weights / jnp.sum(weights, axis=-1, keepdims=True)).astype(jnp.bfloat16)
    return jnp.einsum("fqk,fkc->fqc", probs, values_all, preferred_element_type=jnp.float32).astype(
        jnp.bfloat16
    )


def causal_padded(block):
    earlier = shifted(block[-2:], "ta", 1)
    extended = jnp.concatenate([earlier, block], axis=0)
    return padded_2(extended, (("ha", 1), ("wa", 2)), 1)


def future_padded(block):
    later = shifted(block[:2], "ta", -1)
    extended = jnp.concatenate([block, later], axis=0)
    return padded_2(extended, (("ha", 1), ("wa", 2)), 1)


def local(
    clip,
    gain_attn,
    w_query,
    w_key,
    w_value,
    w_out,
    gain_one,
    w_one,
    bias_one,
    gain_two,
    w_two,
    bias_two,
    cotangent,
    crop_boxes,
):
    frames, rows, cols, chans = clip.shape
    n_ha, n_wa = lax.axis_size("ha"), lax.axis_size("wa")
    at_ha, at_wa = lax.axis_index("ha"), lax.axis_index("wa")
    clip_f = clip.astype(jnp.float32)
    pooled = (
        rms_norm(clip_f, gain_attn)
        .reshape(frames, rows // POOL, POOL, cols // POOL, POOL, chans)
        .mean(axis=(2, 4))
        .astype(jnp.bfloat16)
    )
    grid_rows, grid_cols = rows // POOL, cols // POOL
    full = gathered_tokens(pooled, ("ha", "wa")).reshape(
        n_ha, n_wa, frames, grid_rows, grid_cols, chans
    )
    grid = jnp.transpose(full, (2, 0, 3, 1, 4, 5)).reshape(
        frames, n_ha * grid_rows, n_wa * grid_cols, chans
    )
    tokens_all = grid.reshape(frames, -1, chans)
    keys_all = jnp.dot(tokens_all, w_key, preferred_element_type=jnp.float32).astype(jnp.bfloat16)
    values_all = jnp.dot(tokens_all, w_value, preferred_element_type=jnp.float32).astype(
        jnp.bfloat16
    )
    near = lax.dynamic_slice(
        jnp.pad(grid, ((0, 0), (1, 1), (1, 1), (0, 0))),
        (0, at_ha * grid_rows, at_wa * grid_cols, 0),
        (frames, grid_rows + 2, grid_cols + 2, chans),
    )
    query = jnp.dot(
        near.reshape(frames, -1, chans), w_query, preferred_element_type=jnp.float32
    ).astype(jnp.bfloat16)
    mixed = attend(query, keys_all, values_all)
    projected = jnp.dot(mixed, w_out, preferred_element_type=jnp.float32).reshape(
        frames, grid_rows + 2, grid_cols + 2, chans
    )
    upsampled = jnp.repeat(jnp.repeat(projected, POOL, axis=1), POOL, axis=2)
    upsampled = upsampled[:, POOL - 2 : POOL + rows + 2, POOL - 2 : POOL + cols + 2]
    bounds = crop_boxes[0, 0]
    local_row = jnp.arange(rows)[:, None]
    local_col = jnp.arange(cols)[None, :]
    inside = (
        (local_row >= bounds[0])
        & (local_row < bounds[1])
        & (local_col >= bounds[2])
        & (local_col < bounds[3])
    )
    masked = cotangent * inside.astype(jnp.bfloat16)[None, :, :, None]
    clip_wide, masked_wide = padded_together([clip, masked], [2, 1])
    clip_wide = clip_wide.astype(jnp.float32)
    masked_future = jnp.concatenate([masked_wide, shifted(masked_wide[:2], "ta", -1)], axis=0)
    attended_wide = (clip_wide + upsampled).astype(jnp.bfloat16)
    attended = attended_wide[:, 2 : 2 + rows, 2 : 2 + cols]

    def inside_frame(border):
        row_ids = at_ha * rows - border + jnp.arange(rows + 2 * border)
        col_ids = at_wa * cols - border + jnp.arange(cols + 2 * border)
        row_ok = (row_ids >= 0) & (row_ids < n_ha * rows)
        col_ok = (col_ids >= 0) & (col_ids < n_wa * cols)
        return (row_ok[:, None] & col_ok[None, :])[None, :, :, None]

    act_one_wide = jax.nn.silu(rms_norm(attended_wide.astype(jnp.float32), gain_one)).astype(
        jnp.bfloat16
    )
    act_one_wide = jnp.where(inside_frame(2), act_one_wide, jnp.zeros_like(act_one_wide))
    earlier_one = shifted(act_one_wide[-2:], "ta", 1)
    padded_one_wide = jnp.concatenate([earlier_one, act_one_wide], axis=0)
    pre_two_wide = conv_causal(earlier_one, act_one_wide, w_one) + bias_one
    act_two_wide = jax.nn.silu(rms_norm(pre_two_wide, gain_two)).astype(jnp.bfloat16)
    act_two_wide = jnp.where(inside_frame(1), act_two_wide, jnp.zeros_like(act_two_wide))
    earlier_two = shifted(act_two_wide[-2:], "ta", 1)
    padded_two = jnp.concatenate([earlier_two, act_two_wide], axis=0)
    padded_one = padded_one_wide[:, 1 : 3 + rows, 1 : 3 + cols]
    pre_two = pre_two_wide[:, 1 : 1 + rows, 1 : 1 + cols]
    block_out = (attended.astype(jnp.float32) + conv_causal(earlier_two, act_two_wide, w_two) + bias_two).astype(
        jnp.bfloat16
    )
    total_pixels = (
        frames * lax.axis_size("ta") * rows * lax.axis_size("ha") * cols * lax.axis_size("wa")
    )
    norm_scale = 1.0 / math.sqrt(total_pixels)
    local_two = kernel_grad(padded_two, masked)
    flipped = jnp.transpose(w_two[::-1, ::-1, ::-1], (0, 1, 2, 4, 3))
    back_two = conv_valid(masked_future, flipped)
    back_one = norm_back(pre_two, gain_two, back_two).astype(jnp.bfloat16)
    local_one = kernel_grad(padded_one, back_one)
    summed_two = summed_over(local_two, ("ta", "wa", "ha"))
    summed_one = summed_over(local_one, ("ta", "wa", "ha"))
    return (block_out, summed_one * norm_scale, summed_two * norm_scale)


def solution(mesh):
    in_specs = (
        P(("groups", "ta"), "ha", "wa", None),
        P(),
        P(),
        P(),
        P(),
        P(),
        P(),
        P(),
        P(),
        P(),
        P(),
        P(),
        P(("groups", "ta"), "ha", "wa", None),
        P(("groups", "ha"), "wa", None),
    )
    out_specs = (
        P(("groups", "ta"), "ha", "wa", None),
        P("groups", None, None, None, None),
        P("groups", None, None, None, None),
    )
    return jax.shard_map(local, mesh=mesh, in_specs=in_specs, out_specs=out_specs, check_vma=False)
```

```python
import math

import jax
import jax.numpy as jnp
from jax import lax
from jax.sharding import PartitionSpec as P

POOL = 4


eps_norm = 1e-06


def shifted(x, axis, by):
    size = lax.axis_size(axis)
    pairs = [(i, i + by) for i in range(size) if 0 <= i + by < size]
    return lax.ppermute(x, axis, pairs)


def padded_2(block, sides, width):
    for axis, dim in sides:
        count = lax.axis_size(axis)
        forward = [(i, i + 1) for i in range(count - 1)]
        backward = [(target, source) for source, target in forward]
        low = lax.ppermute(
            lax.slice_in_dim(block, block.shape[dim] - width, None, axis=dim), axis, forward
        )
        high = lax.ppermute(lax.slice_in_dim(block, 0, width, axis=dim), axis, backward)
        block = jnp.concatenate([low, block, high], axis=dim)
    return block


def halving_stages(axes):
    out = []
    for axis in axes:
        count = lax.axis_size(axis)
        distance = 1
        while distance < count:
            out.append((axis, distance, count))
            distance *= 2
    return out


def reduce_scatter_rows(x, stages):
    for axis, distance, count in stages:
        bit = (lax.axis_index(axis) // distance) % 2
        half = x.shape[0] // 2
        keep = lax.dynamic_slice_in_dim(x, bit * half, half)
        send = lax.dynamic_slice_in_dim(x, (1 - bit) * half, half)
        pairs = [(j, j ^ distance) for j in range(count)]
        x = keep + lax.ppermute(send, axis, pairs)
    return x


def all_gather_rows(x, stages):
    for axis, distance, count in reversed(stages):
        bit = (lax.axis_index(axis) // distance) % 2
        pairs = [(j, j ^ distance) for j in range(count)]
        got = lax.ppermute(x, axis, pairs)
        low = jnp.where(bit == 0, x, got)
        high = jnp.where(bit == 0, got, x)
        x = jnp.concatenate([low, high], axis=0)
    return x


def summed_over(value, axes, chunks=1):
    sizes = [lax.axis_size(axis) for axis in axes]
    if any(size & (size - 1) for size in sizes):
        return lax.psum(value, axes)
    stages = halving_stages(axes)
    rows = value.reshape(-1, value.shape[-1])
    while chunks > 1 and rows.shape[0] % (chunks << len(stages)):
        chunks //= 2
    if rows.shape[0] % (chunks << len(stages)):
        return lax.psum(value, axes)
    pieces = jnp.split(rows, chunks, axis=0)
    joined = [all_gather_rows(reduce_scatter_rows(piece, stages), stages) for piece in pieces]
    return jnp.concatenate(joined, axis=0).reshape(value.shape)


def gathered_tokens(tokens, axes):
    sizes = [lax.axis_size(axis) for axis in axes]
    if any(size & (size - 1) for size in sizes):
        return lax.all_gather(tokens, axes, axis=0)
    full = tokens[None]
    for axis, size in reversed(list(zip(axes, sizes))):
        block = full
        distance = 1
        while distance < size:
            bit = (lax.axis_index(axis) // distance) % 2
            pairs = [(j, j ^ distance) for j in range(size)]
            got = lax.ppermute(block, axis, pairs)
            low = jnp.where(bit == 0, block, got)
            high = jnp.where(bit == 0, got, block)
            block = jnp.concatenate([low[None], high[None]], axis=0)
            block = block.reshape((-1,) + full.shape)
            distance *= 2
        full = block.reshape((-1,) + tokens.shape)
    return full

def padded_together(blocks, widths):
    for axis, dim in (("ha", 1), ("wa", 2)):
        count = lax.axis_size(axis)
        forward = [(i, i + 1) for i in range(count - 1)]
        backward = [(target, source) for source, target in forward]
        frames, chans = blocks[0].shape[0], blocks[0].shape[-1]

        def flat(parts):
            return jnp.concatenate([p.reshape(frames, -1, chans) for p in parts], axis=1)

        tails = [lax.slice_in_dim(b, b.shape[dim] - w, None, axis=dim) for b, w in zip(blocks, widths)]
        heads = [lax.slice_in_dim(b, 0, w, axis=dim) for b, w in zip(blocks, widths)]
        low = lax.ppermute(flat(tails), axis, forward)
        high = lax.ppermute(flat(heads), axis, backward)
        out, at = [], 0
        for b, t, h in zip(blocks, tails, heads):
            size = t.size // (frames * chans)
            got_low = low[:, at : at + size].reshape(t.shape)
            got_high = high[:, at : at + size].reshape(h.shape)
            at += size
            out.append(jnp.concatenate([got_low, b, got_high], axis=dim))
        blocks = out
    return blocks


def rms_norm(values, gain):
    scale = lax.rsqrt(jnp.mean(values * values, axis=-1, keepdims=True) + eps_norm)
    return values * scale * gain


def conv_valid(padded, kernel):
    return lax.conv_general_dilated(
        padded[None],
        kernel,
        (1, 1, 1),
        "VALID",
        dimension_numbers=("NDHWC", "DHWIO", "NDHWC"),
        preferred_element_type=jnp.float32,
    )[0]


def kernel_grad(padded, upstream):
    frames, rows, cols, chans = upstream.shape
    taps = []
    for tap_t in range(3):
        for tap_h in range(3):
            for tap_w in range(3):
                window = padded[tap_t : tap_t + frames, tap_h : tap_h + rows, tap_w : tap_w + cols]
                taps.append(
                    lax.dot_general(
                        window,
                        upstream,
                        (((0, 1, 2), (0, 1, 2)), ((), ())),
                        preferred_element_type=jnp.float32,
                    )
                )
    return jnp.stack(taps).reshape(3, 3, 3, chans, chans)


def norm_back(pre, gain, upstream):
    scale = lax.rsqrt(jnp.mean(pre * pre, axis=-1, keepdims=True) + eps_norm)
    normed = pre * scale
    gated = normed * gain
    sigma = jax.nn.sigmoid(gated)
    dgated = upstream * sigma * (1.0 + gated * (1.0 - sigma))
    dnormed = dgated * gain
    return scale * (dnormed - normed * jnp.mean(dnormed * normed, axis=-1, keepdims=True))


def attend(query, keys_all, values_all):
    width = query.shape[-1]
    scores = jnp.einsum(
        "fqc,fkc->fqk", query, keys_all, preferred_element_type=jnp.float32
    ) / math.sqrt(width)
    top = jnp.max(scores, axis=-1, keepdims=True)
    weights = jnp.exp(scores - top)
    probs = (weights / jnp.sum(weights, axis=-1, keepdims=True)).astype(jnp.bfloat16)
    return jnp.einsum("fqk,fkc->fqc", probs, values_all, preferred_element_type=jnp.float32).astype(
        jnp.bfloat16
    )


def causal_padded(block):
    earlier = shifted(block[-2:], "ta", 1)
    extended = jnp.concatenate([earlier, block], axis=0)
    return padded_2(extended, (("ha", 1), ("wa", 2)), 1)


def future_padded(block):
    later = shifted(block[:2], "ta", -1)
    extended = jnp.concatenate([block, later], axis=0)
    return padded_2(extended, (("ha", 1), ("wa", 2)), 1)


def local(
    clip,
    gain_attn,
    w_query,
    w_key,
    w_value,
    w_out,
    gain_one,
    w_one,
    bias_one,
    gain_two,
    w_two,
    bias_two,
    cotangent,
    crop_boxes,
):
    frames, rows, cols, chans = clip.shape
    n_ha, n_wa = lax.axis_size("ha"), lax.axis_size("wa")
    at_ha, at_wa = lax.axis_index("ha"), lax.axis_index("wa")
    clip_f = clip.astype(jnp.float32)
    pooled = (
        rms_norm(clip_f, gain_attn)
        .reshape(frames, rows // POOL, POOL, cols // POOL, POOL, chans)
        .mean(axis=(2, 4))
        .astype(jnp.bfloat16)
    )
    grid_rows, grid_cols = rows // POOL, cols // POOL
    full = gathered_tokens(pooled, ("ha", "wa")).reshape(
        n_ha, n_wa, frames, grid_rows, grid_cols, chans
    )
    grid = jnp.transpose(full, (2, 0, 3, 1, 4, 5)).reshape(
        frames, n_ha * grid_rows, n_wa * grid_cols, chans
    )
    tokens_all = grid.reshape(frames, -1, chans)
    keys_all = jnp.dot(tokens_all, w_key, preferred_element_type=jnp.float32).astype(jnp.bfloat16)
    values_all = jnp.dot(tokens_all, w_value, preferred_element_type=jnp.float32).astype(
        jnp.bfloat16
    )
    near = lax.dynamic_slice(
        jnp.pad(grid, ((0, 0), (1, 1), (1, 1), (0, 0))),
        (0, at_ha * grid_rows, at_wa * grid_cols, 0),
        (frames, grid_rows + 2, grid_cols + 2, chans),
    )
    query = jnp.dot(
        near.reshape(frames, -1, chans), w_query, preferred_element_type=jnp.float32
    ).astype(jnp.bfloat16)
    mixed = attend(query, keys_all, values_all)
    projected = jnp.dot(mixed, w_out, preferred_element_type=jnp.float32).reshape(
        frames, grid_rows + 2, grid_cols + 2, chans
    )
    upsampled = jnp.repeat(jnp.repeat(projected, POOL, axis=1), POOL, axis=2)
    upsampled = upsampled[:, POOL - 2 : POOL + rows + 2, POOL - 2 : POOL + cols + 2]
    bounds = crop_boxes[0, 0]
    local_row = jnp.arange(rows)[:, None]
    local_col = jnp.arange(cols)[None, :]
    inside = (
        (local_row >= bounds[0])
        & (local_row < bounds[1])
        & (local_col >= bounds[2])
        & (local_col < bounds[3])
    )
    masked = cotangent * inside.astype(jnp.bfloat16)[None, :, :, None]
    clip_wide, masked_wide = padded_together([clip, masked], [2, 1])
    clip_wide = clip_wide.astype(jnp.float32)
    masked_future = jnp.concatenate([masked_wide, shifted(masked_wide[:2], "ta", -1)], axis=0)
    attended_wide = (clip_wide + upsampled).astype(jnp.bfloat16)
    attended = attended_wide[:, 2 : 2 + rows, 2 : 2 + cols]

    def inside_frame(border):
        row_ids = at_ha * rows - border + jnp.arange(rows + 2 * border)
        col_ids = at_wa * cols - border + jnp.arange(cols + 2 * border)
        row_ok = (row_ids >= 0) & (row_ids < n_ha * rows)
        col_ok = (col_ids >= 0) & (col_ids < n_wa * cols)
        return (row_ok[:, None] & col_ok[None, :])[None, :, :, None]

    act_one_wide = jax.nn.silu(rms_norm(attended_wide.astype(jnp.float32), gain_one)).astype(
        jnp.bfloat16
    )
    act_one_wide = jnp.where(inside_frame(2), act_one_wide, jnp.zeros_like(act_one_wide))
    padded_one_wide = jnp.concatenate([shifted(act_one_wide[-2:], "ta", 1), act_one_wide], axis=0)
    pre_two_wide = conv_valid(padded_one_wide, w_one) + bias_one
    act_two_wide = jax.nn.silu(rms_norm(pre_two_wide, gain_two)).astype(jnp.bfloat16)
    act_two_wide = jnp.where(inside_frame(1), act_two_wide, jnp.zeros_like(act_two_wide))
    padded_two = jnp.concatenate([shifted(act_two_wide[-2:], "ta", 1), act_two_wide], axis=0)
    padded_one = padded_one_wide[:, 1 : 3 + rows, 1 : 3 + cols]
    pre_two = pre_two_wide[:, 1 : 1 + rows, 1 : 1 + cols]
    block_out = (attended.astype(jnp.float32) + conv_valid(padded_two, w_two) + bias_two).astype(
        jnp.bfloat16
    )
    total_pixels = (
        frames * lax.axis_size("ta") * rows * lax.axis_size("ha") * cols * lax.axis_size("wa")
    )
    norm_scale = 1.0 / math.sqrt(total_pixels)
    local_two = kernel_grad(padded_two, masked)
    flipped = jnp.transpose(w_two[::-1, ::-1, ::-1], (0, 1, 2, 4, 3))
    back_two = conv_valid(masked_future, flipped)
    back_one = norm_back(pre_two, gain_two, back_two).astype(jnp.bfloat16)
    local_one = kernel_grad(padded_one, back_one)
    summed_two = summed_over(local_two, ("ta", "wa", "ha"))
    summed_one = summed_over(local_one, ("ta", "ha", "wa"))
    return (block_out, summed_one * norm_scale, summed_two * norm_scale)


def solution(mesh):
    in_specs = (
        P(("groups", "ta"), "ha", "wa", None),
        P(),
        P(),
        P(),
        P(),
        P(),
        P(),
        P(),
        P(),
        P(),
        P(),
        P(),
        P(("groups", "ta"), "ha", "wa", None),
        P(("groups", "ha"), "wa", None),
    )
    out_specs = (
        P(("groups", "ta"), "ha", "wa", None),
        P("groups", None, None, None, None),
        P("groups", None, None, None, None),
    )
    return jax.shard_map(local, mesh=mesh, in_specs=in_specs, out_specs=out_specs, check_vma=False)
```

```python
import math

import jax
import jax.numpy as jnp
from jax import lax
from jax.sharding import PartitionSpec as P

POOL = 4


eps_norm = 1e-06


def shifted(x, axis, by):
    size = lax.axis_size(axis)
    pairs = [(i, i + by) for i in range(size) if 0 <= i + by < size]
    return lax.ppermute(x, axis, pairs)


def padded_2(block, sides, width):
    for axis, dim in sides:
        count = lax.axis_size(axis)
        forward = [(i, i + 1) for i in range(count - 1)]
        backward = [(target, source) for source, target in forward]
        low = lax.ppermute(
            lax.slice_in_dim(block, block.shape[dim] - width, None, axis=dim), axis, forward
        )
        high = lax.ppermute(lax.slice_in_dim(block, 0, width, axis=dim), axis, backward)
        block = jnp.concatenate([low, block, high], axis=dim)
    return block


def halving_stages(axes):
    out = []
    for axis in axes:
        count = lax.axis_size(axis)
        distance = 1
        while distance < count:
            out.append((axis, distance, count))
            distance *= 2
    return out


def reduce_scatter_rows(x, stages):
    for axis, distance, count in stages:
        bit = (lax.axis_index(axis) // distance) % 2
        half = x.shape[0] // 2
        keep = lax.dynamic_slice_in_dim(x, bit * half, half)
        send = lax.dynamic_slice_in_dim(x, (1 - bit) * half, half)
        pairs = [(j, j ^ distance) for j in range(count)]
        x = keep + lax.ppermute(send, axis, pairs)
    return x


def all_gather_rows(x, stages):
    for axis, distance, count in reversed(stages):
        bit = (lax.axis_index(axis) // distance) % 2
        pairs = [(j, j ^ distance) for j in range(count)]
        got = lax.ppermute(x, axis, pairs)
        low = jnp.where(bit == 0, x, got)
        high = jnp.where(bit == 0, got, x)
        x = jnp.concatenate([low, high], axis=0)
    return x


def summed_over(value, axes, chunks=1):
    sizes = [lax.axis_size(axis) for axis in axes]
    if any(size & (size - 1) for size in sizes):
        return lax.psum(value, axes)
    stages = halving_stages(axes)
    rows = value.reshape(-1, value.shape[-1])
    while chunks > 1 and rows.shape[0] % (chunks << len(stages)):
        chunks //= 2
    if rows.shape[0] % (chunks << len(stages)):
        return lax.psum(value, axes)
    pieces = jnp.split(rows, chunks, axis=0)
    joined = [all_gather_rows(reduce_scatter_rows(piece, stages), stages) for piece in pieces]
    return jnp.concatenate(joined, axis=0).reshape(value.shape)


def gathered_tokens(tokens, axes):
    sizes = [lax.axis_size(axis) for axis in axes]
    if any(size & (size - 1) for size in sizes):
        return lax.all_gather(tokens, axes, axis=0)
    full = tokens[None]
    for axis, size in reversed(list(zip(axes, sizes))):
        block = full
        distance = 1
        while distance < size:
            bit = (lax.axis_index(axis) // distance) % 2
            pairs = [(j, j ^ distance) for j in range(size)]
            got = lax.ppermute(block, axis, pairs)
            low = jnp.where(bit == 0, block, got)
            high = jnp.where(bit == 0, got, block)
            block = jnp.concatenate([low[None], high[None]], axis=0)
            block = block.reshape((-1,) + full.shape)
            distance *= 2
        full = block.reshape((-1,) + tokens.shape)
    return full

def padded_together(blocks, widths):
    for axis, dim in (("ha", 1), ("wa", 2)):
        count = lax.axis_size(axis)
        forward = [(i, i + 1) for i in range(count - 1)]
        backward = [(target, source) for source, target in forward]
        frames, chans = blocks[0].shape[0], blocks[0].shape[-1]

        def flat(parts):
            return jnp.concatenate([p.reshape(frames, -1, chans) for p in parts], axis=1)

        tails = [lax.slice_in_dim(b, b.shape[dim] - w, None, axis=dim) for b, w in zip(blocks, widths)]
        heads = [lax.slice_in_dim(b, 0, w, axis=dim) for b, w in zip(blocks, widths)]
        low = lax.ppermute(flat(tails), axis, forward)
        high = lax.ppermute(flat(heads), axis, backward)
        out, at = [], 0
        for b, t, h in zip(blocks, tails, heads):
            size = t.size // (frames * chans)
            got_low = low[:, at : at + size].reshape(t.shape)
            got_high = high[:, at : at + size].reshape(h.shape)
            at += size
            out.append(jnp.concatenate([got_low, b, got_high], axis=dim))
        blocks = out
    return blocks


def rms_norm(values, gain):
    scale = lax.rsqrt(jnp.mean(values * values, axis=-1, keepdims=True) + eps_norm)
    return values * scale * gain


def conv_valid(padded, kernel):
    return lax.conv_general_dilated(
        padded[None],
        kernel,
        (1, 1, 1),
        "VALID",
        dimension_numbers=("NDHWC", "DHWIO", "NDHWC"),
        preferred_element_type=jnp.float32,
    )[0]


def kernel_grad(padded, upstream):
    frames, rows, cols, chans = upstream.shape
    taps = []
    for tap_t in range(3):
        for tap_h in range(3):
            for tap_w in range(3):
                window = padded[tap_t : tap_t + frames, tap_h : tap_h + rows, tap_w : tap_w + cols]
                taps.append(
                    lax.dot_general(
                        window,
                        upstream,
                        (((0, 1, 2), (0, 1, 2)), ((), ())),
                        preferred_element_type=jnp.float32,
                    )
                )
    return jnp.stack(taps).reshape(3, 3, 3, chans, chans)


def norm_back(pre, gain, upstream):
    scale = lax.rsqrt(jnp.mean(pre * pre, axis=-1, keepdims=True) + eps_norm)
    normed = pre * scale
    gated = normed * gain
    sigma = jax.nn.sigmoid(gated)
    dgated = upstream * sigma * (1.0 + gated * (1.0 - sigma))
    dnormed = dgated * gain
    return scale * (dnormed - normed * jnp.mean(dnormed * normed, axis=-1, keepdims=True))


def attend(query, keys_all, values_all):
    width = query.shape[-1]
    scores = jnp.einsum(
        "fqc,fkc->fqk", query, keys_all, preferred_element_type=jnp.float32
    ) / math.sqrt(width)
    top = jnp.max(scores, axis=-1, keepdims=True)
    weights = jnp.exp(scores - top)
    probs = (weights / jnp.sum(weights, axis=-1, keepdims=True)).astype(jnp.bfloat16)
    return jnp.einsum("fqk,fkc->fqc", probs, values_all, preferred_element_type=jnp.float32).astype(
        jnp.bfloat16
    )


def causal_padded(block):
    earlier = shifted(block[-2:], "ta", 1)
    extended = jnp.concatenate([earlier, block], axis=0)
    return padded_2(extended, (("ha", 1), ("wa", 2)), 1)


def future_padded(block):
    later = shifted(block[:2], "ta", -1)
    extended = jnp.concatenate([block, later], axis=0)
    return padded_2(extended, (("ha", 1), ("wa", 2)), 1)


def local(
    clip,
    gain_attn,
    w_query,
    w_key,
    w_value,
    w_out,
    gain_one,
    w_one,
    bias_one,
    gain_two,
    w_two,
    bias_two,
    cotangent,
    crop_boxes,
):
    frames, rows, cols, chans = clip.shape
    n_ha, n_wa = lax.axis_size("ha"), lax.axis_size("wa")
    at_ha, at_wa = lax.axis_index("ha"), lax.axis_index("wa")
    clip_f = clip.astype(jnp.float32)
    pooled = (
        rms_norm(clip_f, gain_attn)
        .reshape(frames, rows // POOL, POOL, cols // POOL, POOL, chans)
        .mean(axis=(2, 4))
        .astype(jnp.bfloat16)
    )
    grid_rows, grid_cols = rows // POOL, cols // POOL
    full = gathered_tokens(pooled, ("ha", "wa")).reshape(
        n_ha, n_wa, frames, grid_rows, grid_cols, chans
    )
    grid = jnp.transpose(full, (2, 0, 3, 1, 4, 5)).reshape(
        frames, n_ha * grid_rows, n_wa * grid_cols, chans
    )
    tokens_all = grid.reshape(frames, -1, chans)
    keys_all = jnp.dot(tokens_all, w_key, preferred_element_type=jnp.float32).astype(jnp.bfloat16)
    values_all = jnp.dot(tokens_all, w_value, preferred_element_type=jnp.float32).astype(
        jnp.bfloat16
    )
    near = lax.dynamic_slice(
        jnp.pad(grid, ((0, 0), (1, 1), (1, 1), (0, 0))),
        (0, at_ha * grid_rows, at_wa * grid_cols, 0),
        (frames, grid_rows + 2, grid_cols + 2, chans),
    )
    query = jnp.dot(
        near.reshape(frames, -1, chans), w_query, preferred_element_type=jnp.float32
    ).astype(jnp.bfloat16)
    mixed = attend(query, keys_all, values_all)
    projected = jnp.dot(mixed, w_out, preferred_element_type=jnp.float32).reshape(
        frames, grid_rows + 2, grid_cols + 2, chans
    )
    upsampled = jnp.repeat(jnp.repeat(projected, POOL, axis=1), POOL, axis=2)
    upsampled = upsampled[:, POOL - 2 : POOL + rows + 2, POOL - 2 : POOL + cols + 2]
    bounds = crop_boxes[0, 0]
    local_row = jnp.arange(rows)[:, None]
    local_col = jnp.arange(cols)[None, :]
    inside = (
        (local_row >= bounds[0])
        & (local_row < bounds[1])
        & (local_col >= bounds[2])
        & (local_col < bounds[3])
    )
    masked = cotangent * inside.astype(jnp.bfloat16)[None, :, :, None]
    clip_wide, masked_wide = padded_together([clip, masked], [2, 1])
    clip_wide = clip_wide.astype(jnp.float32)
    masked_future = jnp.concatenate([masked_wide, shifted(masked_wide[:2], "ta", -1)], axis=0)
    attended_wide = (clip_wide + upsampled).astype(jnp.bfloat16)
    attended = attended_wide[:, 2 : 2 + rows, 2 : 2 + cols]

    def inside_frame(border):
        row_ids = at_ha * rows - border + jnp.arange(rows + 2 * border)
        col_ids = at_wa * cols - border + jnp.arange(cols + 2 * border)
        row_ok = (row_ids >= 0) & (row_ids < n_ha * rows)
        col_ok = (col_ids >= 0) & (col_ids < n_wa * cols)
        return (row_ok[:, None] & col_ok[None, :])[None, :, :, None]

    act_one_wide = jax.nn.silu(rms_norm(attended_wide.astype(jnp.float32), gain_one)).astype(
        jnp.bfloat16
    )
    act_one_wide = jnp.where(inside_frame(2), act_one_wide, jnp.zeros_like(act_one_wide))
    padded_one_wide = jnp.concatenate([shifted(act_one_wide[-2:], "ta", 1), act_one_wide], axis=0)
    pre_two_wide = conv_valid(padded_one_wide, w_one) + bias_one
    act_two_wide = jax.nn.silu(rms_norm(pre_two_wide, gain_two)).astype(jnp.bfloat16)
    act_two_wide = jnp.where(inside_frame(1), act_two_wide, jnp.zeros_like(act_two_wide))
    padded_two = jnp.concatenate([shifted(act_two_wide[-2:], "ta", 1), act_two_wide], axis=0)
    padded_one = padded_one_wide[:, 1 : 3 + rows, 1 : 3 + cols]
    pre_two = pre_two_wide[:, 1 : 1 + rows, 1 : 1 + cols]
    block_out = (attended.astype(jnp.float32) + conv_valid(padded_two, w_two) + bias_two).astype(
        jnp.bfloat16
    )
    total_pixels = (
        frames * lax.axis_size("ta") * rows * lax.axis_size("ha") * cols * lax.axis_size("wa")
    )
    norm_scale = 1.0 / math.sqrt(total_pixels)
    local_two = kernel_grad(padded_two, masked) * norm_scale
    flipped = jnp.transpose(w_two[::-1, ::-1, ::-1], (0, 1, 2, 4, 3))
    back_two = conv_valid(masked_future, flipped)
    back_one = norm_back(pre_two, gain_two, back_two).astype(jnp.bfloat16)
    local_one = kernel_grad(padded_one, back_one) * norm_scale
    summed_two = summed_over(local_two, ("ta", "wa", "ha"))
    summed_one = summed_over(local_one, ("ta", "wa", "ha"))
    return (block_out, summed_one, summed_two)


def solution(mesh):
    in_specs = (
        P(("groups", "ta"), "ha", "wa", None),
        P(),
        P(),
        P(),
        P(),
        P(),
        P(),
        P(),
        P(),
        P(),
        P(),
        P(),
        P(("groups", "ta"), "ha", "wa", None),
        P(("groups", "ha"), "wa", None),
    )
    out_specs = (
        P(("groups", "ta"), "ha", "wa", None),
        P("groups", None, None, None, None),
        P("groups", None, None, None, None),
    )
    return jax.shard_map(local, mesh=mesh, in_specs=in_specs, out_specs=out_specs, check_vma=False)
```

```python
import math

import jax
import jax.numpy as jnp
from jax import lax
from jax.sharding import PartitionSpec as P

POOL = 4


eps_norm = 1e-06


def shifted(x, axis, by):
    size = lax.axis_size(axis)
    pairs = [(i, i + by) for i in range(size) if 0 <= i + by < size]
    return lax.ppermute(x, axis, pairs)


def padded_2(block, sides, width):
    for axis, dim in sides:
        count = lax.axis_size(axis)
        forward = [(i, i + 1) for i in range(count - 1)]
        backward = [(target, source) for source, target in forward]
        low = lax.ppermute(
            lax.slice_in_dim(block, block.shape[dim] - width, None, axis=dim), axis, forward
        )
        high = lax.ppermute(lax.slice_in_dim(block, 0, width, axis=dim), axis, backward)
        block = jnp.concatenate([low, block, high], axis=dim)
    return block


def halving_stages(axes):
    out = []
    for axis in axes:
        count = lax.axis_size(axis)
        distance = 1
        while distance < count:
            out.append((axis, distance, count))
            distance *= 2
    return out


def reduce_scatter_rows(x, stages):
    for axis, distance, count in stages:
        bit = (lax.axis_index(axis) // distance) % 2
        half = x.shape[0] // 2
        keep = lax.dynamic_slice_in_dim(x, bit * half, half)
        send = lax.dynamic_slice_in_dim(x, (1 - bit) * half, half)
        pairs = [(j, j ^ distance) for j in range(count)]
        x = keep + lax.ppermute(send, axis, pairs)
    return x


def all_gather_rows(x, stages):
    for axis, distance, count in reversed(stages):
        bit = (lax.axis_index(axis) // distance) % 2
        pairs = [(j, j ^ distance) for j in range(count)]
        got = lax.ppermute(x, axis, pairs)
        low = jnp.where(bit == 0, x, got)
        high = jnp.where(bit == 0, got, x)
        x = jnp.concatenate([low, high], axis=0)
    return x


def summed_over(value, axes, chunks=1):
    sizes = [lax.axis_size(axis) for axis in axes]
    if any(size & (size - 1) for size in sizes):
        return lax.psum(value, axes)
    stages = halving_stages(axes)
    rows = value.reshape(-1, value.shape[-1])
    while chunks > 1 and rows.shape[0] % (chunks << len(stages)):
        chunks //= 2
    if rows.shape[0] % (chunks << len(stages)):
        return lax.psum(value, axes)
    pieces = jnp.split(rows, chunks, axis=0)
    joined = [all_gather_rows(reduce_scatter_rows(piece, stages), stages) for piece in pieces]
    return jnp.concatenate(joined, axis=0).reshape(value.shape)


def gathered_tokens(tokens, axes):
    sizes = [lax.axis_size(axis) for axis in axes]
    if any(size & (size - 1) for size in sizes):
        return lax.all_gather(tokens, axes, axis=0)
    full = tokens[None]
    for axis, size in reversed(list(zip(axes, sizes))):
        block = full
        distance = 1
        while distance < size:
            bit = (lax.axis_index(axis) // distance) % 2
            pairs = [(j, j ^ distance) for j in range(size)]
            got = lax.ppermute(block, axis, pairs)
            low = jnp.where(bit == 0, block, got)
            high = jnp.where(bit == 0, got, block)
            block = jnp.concatenate([low[None], high[None]], axis=0)
            block = block.reshape((-1,) + full.shape)
            distance *= 2
        full = block.reshape((-1,) + tokens.shape)
    return full

def padded_together(blocks, widths):
    for axis, dim in (("ha", 1), ("wa", 2)):
        count = lax.axis_size(axis)
        forward = [(i, i + 1) for i in range(count - 1)]
        backward = [(target, source) for source, target in forward]
        frames, chans = blocks[0].shape[0], blocks[0].shape[-1]

        def flat(parts):
            return jnp.concatenate([p.reshape(frames, -1, chans) for p in parts], axis=1)

        tails = [lax.slice_in_dim(b, b.shape[dim] - w, None, axis=dim) for b, w in zip(blocks, widths)]
        heads = [lax.slice_in_dim(b, 0, w, axis=dim) for b, w in zip(blocks, widths)]
        low = lax.ppermute(flat(tails), axis, forward)
        high = lax.ppermute(flat(heads), axis, backward)
        out, at = [], 0
        for b, t, h in zip(blocks, tails, heads):
            size = t.size // (frames * chans)
            got_low = low[:, at : at + size].reshape(t.shape)
            got_high = high[:, at : at + size].reshape(h.shape)
            at += size
            out.append(jnp.concatenate([got_low, b, got_high], axis=dim))
        blocks = out
    return blocks


def rms_norm(values, gain):
    scale = lax.rsqrt(jnp.mean(values * values, axis=-1, keepdims=True) + eps_norm)
    return values * scale * gain


def conv_valid(padded, kernel):
    return lax.conv_general_dilated(
        padded[None],
        kernel,
        (1, 1, 1),
        "VALID",
        dimension_numbers=("NDHWC", "DHWIO", "NDHWC"),
        preferred_element_type=jnp.float32,
    )[0]


def kernel_grad(padded, upstream):
    frames, rows, cols, chans = upstream.shape
    taps = []
    for tap_t in range(3):
        for tap_h in range(3):
            for tap_w in range(3):
                window = padded[tap_t : tap_t + frames, tap_h : tap_h + rows, tap_w : tap_w + cols]
                taps.append(
                    lax.dot_general(
                        window,
                        upstream,
                        (((0, 1, 2), (0, 1, 2)), ((), ())),
                        preferred_element_type=jnp.float32,
                    )
                )
    return jnp.stack(taps).reshape(3, 3, 3, chans, chans)


def norm_back(pre, gain, upstream):
    scale = lax.rsqrt(jnp.mean(pre * pre, axis=-1, keepdims=True) + eps_norm)
    normed = pre * scale
    gated = normed * gain
    sigma = jax.nn.sigmoid(gated)
    dgated = upstream * sigma * (1.0 + gated * (1.0 - sigma))
    dnormed = dgated * gain
    return scale * (dnormed - normed * jnp.mean(dnormed * normed, axis=-1, keepdims=True))


def attend(query, keys_all, values_all):
    width = query.shape[-1]
    scores = jnp.einsum(
        "fqc,fkc->fqk", query, keys_all, preferred_element_type=jnp.float32
    ) / math.sqrt(width)
    top = jnp.max(scores, axis=-1, keepdims=True)
    weights = jnp.exp(scores - top)
    probs = (weights / jnp.sum(weights, axis=-1, keepdims=True)).astype(jnp.bfloat16)
    return jnp.einsum("fqk,fkc->fqc", probs, values_all, preferred_element_type=jnp.float32).astype(
        jnp.bfloat16
    )


def causal_padded(block):
    earlier = shifted(block[-2:], "ta", 1)
    extended = jnp.concatenate([earlier, block], axis=0)
    return padded_2(extended, (("ha", 1), ("wa", 2)), 1)


def future_padded(block):
    later = shifted(block[:2], "ta", -1)
    extended = jnp.concatenate([block, later], axis=0)
    return padded_2(extended, (("ha", 1), ("wa", 2)), 1)


def local(
    clip,
    gain_attn,
    w_query,
    w_key,
    w_value,
    w_out,
    gain_one,
    w_one,
    bias_one,
    gain_two,
    w_two,
    bias_two,
    cotangent,
    crop_boxes,
):
    frames, rows, cols, chans = clip.shape
    n_ha, n_wa = lax.axis_size("ha"), lax.axis_size("wa")
    at_ha, at_wa = lax.axis_index("ha"), lax.axis_index("wa")
    clip_f = clip.astype(jnp.float32)
    pooled = (
        rms_norm(clip_f, gain_attn)
        .reshape(frames, rows // POOL, POOL, cols // POOL, POOL, chans)
        .mean(axis=(2, 4))
        .astype(jnp.bfloat16)
    )
    grid_rows, grid_cols = rows // POOL, cols // POOL
    full = gathered_tokens(pooled, ("ha", "wa")).reshape(
        n_ha, n_wa, frames, grid_rows, grid_cols, chans
    )
    grid = jnp.transpose(full, (2, 0, 3, 1, 4, 5)).reshape(
        frames, n_ha * grid_rows, n_wa * grid_cols, chans
    )
    tokens_all = grid.reshape(frames, -1, chans)
    keys_all = jnp.dot(tokens_all, w_key, preferred_element_type=jnp.float32).astype(jnp.bfloat16)
    values_all = jnp.dot(tokens_all, w_value, preferred_element_type=jnp.float32).astype(
        jnp.bfloat16
    )
    near = lax.dynamic_slice(
        jnp.pad(grid, ((0, 0), (1, 1), (1, 1), (0, 0))),
        (0, at_ha * grid_rows, at_wa * grid_cols, 0),
        (frames, grid_rows + 2, grid_cols + 2, chans),
    )
    query = jnp.dot(
        near.reshape(frames, -1, chans), w_query, preferred_element_type=jnp.float32
    ).astype(jnp.bfloat16)
    mixed = attend(query, keys_all, values_all)
    projected = jnp.dot(mixed, w_out, preferred_element_type=jnp.float32).reshape(
        frames, grid_rows + 2, grid_cols + 2, chans
    )
    upsampled = jnp.repeat(jnp.repeat(projected, POOL, axis=1), POOL, axis=2)
    upsampled = upsampled[:, POOL - 2 : POOL + rows + 2, POOL - 2 : POOL + cols + 2]
    bounds = crop_boxes[0, 0]
    local_row = lax.broadcasted_iota(jnp.int32, cotangent.shape, 1)
    local_col = lax.broadcasted_iota(jnp.int32, cotangent.shape, 2)
    inside = (
        (local_row >= bounds[0])
        & (local_row < bounds[1])
        & (local_col >= bounds[2])
        & (local_col < bounds[3])
    )
    masked = jnp.where(inside, cotangent, jnp.zeros_like(cotangent))
    clip_wide, masked_wide = padded_together([clip, masked], [2, 1])
    clip_wide = clip_wide.astype(jnp.float32)
    masked_future = jnp.concatenate([masked_wide, shifted(masked_wide[:2], "ta", -1)], axis=0)
    attended_wide = (clip_wide + upsampled).astype(jnp.bfloat16)
    attended = attended_wide[:, 2 : 2 + rows, 2 : 2 + cols]

    def inside_frame(border):
        row_ids = at_ha * rows - border + jnp.arange(rows + 2 * border)
        col_ids = at_wa * cols - border + jnp.arange(cols + 2 * border)
        row_ok = (row_ids >= 0) & (row_ids < n_ha * rows)
        col_ok = (col_ids >= 0) & (col_ids < n_wa * cols)
        return (row_ok[:, None] & col_ok[None, :])[None, :, :, None]

    act_one_wide = jax.nn.silu(rms_norm(attended_wide.astype(jnp.float32), gain_one)).astype(
        jnp.bfloat16
    )
    act_one_wide = jnp.where(inside_frame(2), act_one_wide, jnp.zeros_like(act_one_wide))
    padded_one_wide = jnp.concatenate([shifted(act_one_wide[-2:], "ta", 1), act_one_wide], axis=0)
    pre_two_wide = conv_valid(padded_one_wide, w_one) + bias_one
    act_two_wide = jax.nn.silu(rms_norm(pre_two_wide, gain_two)).astype(jnp.bfloat16)
    act_two_wide = jnp.where(inside_frame(1), act_two_wide, jnp.zeros_like(act_two_wide))
    padded_two = jnp.concatenate([shifted(act_two_wide[-2:], "ta", 1), act_two_wide], axis=0)
    padded_one = padded_one_wide[:, 1 : 3 + rows, 1 : 3 + cols]
    pre_two = pre_two_wide[:, 1 : 1 + rows, 1 : 1 + cols]
    block_out = (attended.astype(jnp.float32) + conv_valid(padded_two, w_two) + bias_two).astype(
        jnp.bfloat16
    )
    total_pixels = (
        frames * lax.axis_size("ta") * rows * lax.axis_size("ha") * cols * lax.axis_size("wa")
    )
    norm_scale = 1.0 / math.sqrt(total_pixels)
    local_two = kernel_grad(padded_two, masked)
    flipped = jnp.transpose(w_two[::-1, ::-1, ::-1], (0, 1, 2, 4, 3))
    back_two = conv_valid(masked_future, flipped)
    back_one = norm_back(pre_two, gain_two, back_two).astype(jnp.bfloat16)
    local_one = kernel_grad(padded_one, back_one)
    summed_two = summed_over(local_two, ("ta", "wa", "ha"))
    summed_one = summed_over(local_one, ("ta", "wa", "ha"))
    return (block_out, summed_one * norm_scale, summed_two * norm_scale)


def solution(mesh):
    in_specs = (
        P(("groups", "ta"), "ha", "wa", None),
        P(),
        P(),
        P(),
        P(),
        P(),
        P(),
        P(),
        P(),
        P(),
        P(),
        P(),
        P(("groups", "ta"), "ha", "wa", None),
        P(("groups", "ha"), "wa", None),
    )
    out_specs = (
        P(("groups", "ta"), "ha", "wa", None),
        P("groups", None, None, None, None),
        P("groups", None, None, None, None),
    )
    return jax.shard_map(local, mesh=mesh, in_specs=in_specs, out_specs=out_specs, check_vma=False)
```

```python
import math

import jax
import jax.numpy as jnp
from jax import lax
from jax.sharding import PartitionSpec as P

POOL = 4


eps_norm = 1e-06


def shifted(x, axis, by):
    size = lax.axis_size(axis)
    pairs = [(i, i + by) for i in range(size) if 0 <= i + by < size]
    return lax.ppermute(x, axis, pairs)


def padded_2(block, sides, width):
    for axis, dim in sides:
        count = lax.axis_size(axis)
        forward = [(i, i + 1) for i in range(count - 1)]
        backward = [(target, source) for source, target in forward]
        low = lax.ppermute(
            lax.slice_in_dim(block, block.shape[dim] - width, None, axis=dim), axis, forward
        )
        high = lax.ppermute(lax.slice_in_dim(block, 0, width, axis=dim), axis, backward)
        block = jnp.concatenate([low, block, high], axis=dim)
    return block


def halving_stages(axes):
    out = []
    for axis in axes:
        count = lax.axis_size(axis)
        distance = 1
        while distance < count:
            out.append((axis, distance, count))
            distance *= 2
    return out


def reduce_scatter_rows(x, stages):
    for axis, distance, count in stages:
        bit = (lax.axis_index(axis) // distance) % 2
        half = x.shape[0] // 2
        keep = lax.dynamic_slice_in_dim(x, bit * half, half)
        send = lax.dynamic_slice_in_dim(x, (1 - bit) * half, half)
        pairs = [(j, j ^ distance) for j in range(count)]
        x = keep + lax.ppermute(send, axis, pairs)
    return x


def all_gather_rows(x, stages):
    for axis, distance, count in reversed(stages):
        bit = (lax.axis_index(axis) // distance) % 2
        pairs = [(j, j ^ distance) for j in range(count)]
        got = lax.ppermute(x, axis, pairs)
        low = jnp.where(bit == 0, x, got)
        high = jnp.where(bit == 0, got, x)
        x = jnp.concatenate([low, high], axis=0)
    return x


def summed_over(value, axes, chunks=1):
    sizes = [lax.axis_size(axis) for axis in axes]
    if any(size & (size - 1) for size in sizes):
        return lax.psum(value, axes)
    stages = halving_stages(axes)
    rows = value.reshape(-1, value.shape[-1])
    while chunks > 1 and rows.shape[0] % (chunks << len(stages)):
        chunks //= 2
    if rows.shape[0] % (chunks << len(stages)):
        return lax.psum(value, axes)
    pieces = jnp.split(rows, chunks, axis=0)
    joined = [all_gather_rows(reduce_scatter_rows(piece, stages), stages) for piece in pieces]
    return jnp.concatenate(joined, axis=0).reshape(value.shape)


def gathered_tokens(tokens, axes):
    sizes = [lax.axis_size(axis) for axis in axes]
    if any(size & (size - 1) for size in sizes):
        return lax.all_gather(tokens, axes, axis=0)
    full = tokens[None]
    for axis, size in reversed(list(zip(axes, sizes))):
        block = full
        distance = 1
        while distance < size:
            bit = (lax.axis_index(axis) // distance) % 2
            pairs = [(j, j ^ distance) for j in range(size)]
            got = lax.ppermute(block, axis, pairs)
            low = jnp.where(bit == 0, block, got)
            high = jnp.where(bit == 0, got, block)
            block = jnp.concatenate([low[None], high[None]], axis=0)
            block = block.reshape((-1,) + full.shape)
            distance *= 2
        full = block.reshape((-1,) + tokens.shape)
    return full

def padded_together(blocks, widths):
    for axis, dim in (("ha", 1), ("wa", 2)):
        count = lax.axis_size(axis)
        forward = [(i, i + 1) for i in range(count - 1)]
        backward = [(target, source) for source, target in forward]
        frames, chans = blocks[0].shape[0], blocks[0].shape[-1]

        def flat(parts):
            return jnp.concatenate([p.reshape(frames, -1, chans) for p in parts], axis=1)

        tails = [lax.slice_in_dim(b, b.shape[dim] - w, None, axis=dim) for b, w in zip(blocks, widths)]
        heads = [lax.slice_in_dim(b, 0, w, axis=dim) for b, w in zip(blocks, widths)]
        low = lax.ppermute(flat(tails), axis, forward)
        high = lax.ppermute(flat(heads), axis, backward)
        out, at = [], 0
        for b, t, h in zip(blocks, tails, heads):
            size = t.size // (frames * chans)
            got_low = low[:, at : at + size].reshape(t.shape)
            got_high = high[:, at : at + size].reshape(h.shape)
            at += size
            out.append(jnp.concatenate([got_low, b, got_high], axis=dim))
        blocks = out
    return blocks


def rms_norm(values, gain):
    scale = lax.rsqrt(jnp.mean(values * values, axis=-1, keepdims=True) + eps_norm)
    return values * scale * gain


def conv_valid(padded, kernel):
    return lax.conv_general_dilated(
        padded[None],
        kernel,
        (1, 1, 1),
        "VALID",
        dimension_numbers=("NDHWC", "DHWIO", "NDHWC"),
        preferred_element_type=jnp.float32,
    )[0]


def kernel_grad(padded, upstream):
    frames, rows, cols, chans = upstream.shape

    def tap(index, taps):
        offsets = (index // 9, (index // 3) % 3, index % 3, 0)
        window = lax.dynamic_slice(padded, offsets, (frames, rows, cols, padded.shape[-1]))
        term = lax.dot_general(
            window,
            upstream,
            (((0, 1, 2), (0, 1, 2)), ((), ())),
            preferred_element_type=jnp.float32,
        )
        return lax.dynamic_update_index_in_dim(taps, term, index, 0)

    taps = jnp.zeros((27, padded.shape[-1], chans), jnp.float32)
    taps = lax.fori_loop(0, 27, tap, taps)
    return taps.reshape(3, 3, 3, padded.shape[-1], chans)


def norm_back(pre, gain, upstream):
    scale = lax.rsqrt(jnp.mean(pre * pre, axis=-1, keepdims=True) + eps_norm)
    normed = pre * scale
    gated = normed * gain
    sigma = jax.nn.sigmoid(gated)
    dgated = upstream * sigma * (1.0 + gated * (1.0 - sigma))
    dnormed = dgated * gain
    return scale * (dnormed - normed * jnp.mean(dnormed * normed, axis=-1, keepdims=True))


def attend(query, keys_all, values_all):
    width = query.shape[-1]
    scores = jnp.einsum(
        "fqc,fkc->fqk", query, keys_all, preferred_element_type=jnp.float32
    ) / math.sqrt(width)
    top = jnp.max(scores, axis=-1, keepdims=True)
    weights = jnp.exp(scores - top)
    probs = (weights / jnp.sum(weights, axis=-1, keepdims=True)).astype(jnp.bfloat16)
    return jnp.einsum("fqk,fkc->fqc", probs, values_all, preferred_element_type=jnp.float32).astype(
        jnp.bfloat16
    )


def causal_padded(block):
    earlier = shifted(block[-2:], "ta", 1)
    extended = jnp.concatenate([earlier, block], axis=0)
    return padded_2(extended, (("ha", 1), ("wa", 2)), 1)


def future_padded(block):
    later = shifted(block[:2], "ta", -1)
    extended = jnp.concatenate([block, later], axis=0)
    return padded_2(extended, (("ha", 1), ("wa", 2)), 1)


def local(
    clip,
    gain_attn,
    w_query,
    w_key,
    w_value,
    w_out,
    gain_one,
    w_one,
    bias_one,
    gain_two,
    w_two,
    bias_two,
    cotangent,
    crop_boxes,
):
    frames, rows, cols, chans = clip.shape
    n_ha, n_wa = lax.axis_size("ha"), lax.axis_size("wa")
    at_ha, at_wa = lax.axis_index("ha"), lax.axis_index("wa")
    clip_f = clip.astype(jnp.float32)
    pooled = (
        rms_norm(clip_f, gain_attn)
        .reshape(frames, rows // POOL, POOL, cols // POOL, POOL, chans)
        .mean(axis=(2, 4))
        .astype(jnp.bfloat16)
    )
    grid_rows, grid_cols = rows // POOL, cols // POOL
    full = gathered_tokens(pooled, ("ha", "wa")).reshape(
        n_ha, n_wa, frames, grid_rows, grid_cols, chans
    )
    grid = jnp.transpose(full, (2, 0, 3, 1, 4, 5)).reshape(
        frames, n_ha * grid_rows, n_wa * grid_cols, chans
    )
    tokens_all = grid.reshape(frames, -1, chans)
    keys_all = jnp.dot(tokens_all, w_key, preferred_element_type=jnp.float32).astype(jnp.bfloat16)
    values_all = jnp.dot(tokens_all, w_value, preferred_element_type=jnp.float32).astype(
        jnp.bfloat16
    )
    near = lax.dynamic_slice(
        jnp.pad(grid, ((0, 0), (1, 1), (1, 1), (0, 0))),
        (0, at_ha * grid_rows, at_wa * grid_cols, 0),
        (frames, grid_rows + 2, grid_cols + 2, chans),
    )
    query = jnp.dot(
        near.reshape(frames, -1, chans), w_query, preferred_element_type=jnp.float32
    ).astype(jnp.bfloat16)
    mixed = attend(query, keys_all, values_all)
    projected = jnp.dot(mixed, w_out, preferred_element_type=jnp.float32).reshape(
        frames, grid_rows + 2, grid_cols + 2, chans
    )
    upsampled = jnp.repeat(jnp.repeat(projected, POOL, axis=1), POOL, axis=2)
    upsampled = upsampled[:, POOL - 2 : POOL + rows + 2, POOL - 2 : POOL + cols + 2]
    bounds = crop_boxes[0, 0]
    local_row = jnp.arange(rows)[:, None]
    local_col = jnp.arange(cols)[None, :]
    inside = (
        (local_row >= bounds[0])
        & (local_row < bounds[1])
        & (local_col >= bounds[2])
        & (local_col < bounds[3])
    )
    masked = cotangent * inside.astype(jnp.bfloat16)[None, :, :, None]
    clip_wide, masked_wide = padded_together([clip, masked], [2, 1])
    clip_wide = clip_wide.astype(jnp.float32)
    masked_future = jnp.concatenate([masked_wide, shifted(masked_wide[:2], "ta", -1)], axis=0)
    attended_wide = (clip_wide + upsampled).astype(jnp.bfloat16)
    attended = attended_wide[:, 2 : 2 + rows, 2 : 2 + cols]

    def inside_frame(border):
        row_ids = at_ha * rows - border + jnp.arange(rows + 2 * border)
        col_ids = at_wa * cols - border + jnp.arange(cols + 2 * border)
        row_ok = (row_ids >= 0) & (row_ids < n_ha * rows)
        col_ok = (col_ids >= 0) & (col_ids < n_wa * cols)
        return (row_ok[:, None] & col_ok[None, :])[None, :, :, None]

    act_one_wide = jax.nn.silu(rms_norm(attended_wide.astype(jnp.float32), gain_one)).astype(
        jnp.bfloat16
    )
    act_one_wide = jnp.where(inside_frame(2), act_one_wide, jnp.zeros_like(act_one_wide))
    padded_one_wide = jnp.concatenate([shifted(act_one_wide[-2:], "ta", 1), act_one_wide], axis=0)
    pre_two_wide = conv_valid(padded_one_wide, w_one) + bias_one
    act_two_wide = jax.nn.silu(rms_norm(pre_two_wide, gain_two)).astype(jnp.bfloat16)
    act_two_wide = jnp.where(inside_frame(1), act_two_wide, jnp.zeros_like(act_two_wide))
    padded_two = jnp.concatenate([shifted(act_two_wide[-2:], "ta", 1), act_two_wide], axis=0)
    padded_one = padded_one_wide[:, 1 : 3 + rows, 1 : 3 + cols]
    pre_two = pre_two_wide[:, 1 : 1 + rows, 1 : 1 + cols]
    block_out = (attended.astype(jnp.float32) + conv_valid(padded_two, w_two) + bias_two).astype(
        jnp.bfloat16
    )
    total_pixels = (
        frames * lax.axis_size("ta") * rows * lax.axis_size("ha") * cols * lax.axis_size("wa")
    )
    norm_scale = 1.0 / math.sqrt(total_pixels)
    local_two = kernel_grad(padded_two, masked)
    flipped = jnp.transpose(w_two[::-1, ::-1, ::-1], (0, 1, 2, 4, 3))
    back_two = conv_valid(masked_future, flipped)
    back_one = norm_back(pre_two, gain_two, back_two).astype(jnp.bfloat16)
    local_one = kernel_grad(padded_one, back_one)
    summed_two = summed_over(local_two, ("ta", "wa", "ha"))
    summed_one = summed_over(local_one, ("ta", "wa", "ha"))
    return (block_out, summed_one * norm_scale, summed_two * norm_scale)


def solution(mesh):
    in_specs = (
        P(("groups", "ta"), "ha", "wa", None),
        P(),
        P(),
        P(),
        P(),
        P(),
        P(),
        P(),
        P(),
        P(),
        P(),
        P(),
        P(("groups", "ta"), "ha", "wa", None),
        P(("groups", "ha"), "wa", None),
    )
    out_specs = (
        P(("groups", "ta"), "ha", "wa", None),
        P("groups", None, None, None, None),
        P("groups", None, None, None, None),
    )
    return jax.shard_map(local, mesh=mesh, in_specs=in_specs, out_specs=out_specs, check_vma=False)
```

```python
import math

import jax
import jax.numpy as jnp
from jax import lax
from jax.sharding import PartitionSpec as P

POOL = 4


eps_norm = 1e-06


def shifted(x, axis, by):
    size = lax.axis_size(axis)
    pairs = [(i, i + by) for i in range(size) if 0 <= i + by < size]
    return lax.ppermute(x, axis, pairs)


def padded_2(block, sides, width):
    for axis, dim in sides:
        count = lax.axis_size(axis)
        forward = [(i, i + 1) for i in range(count - 1)]
        backward = [(target, source) for source, target in forward]
        low = lax.ppermute(
            lax.slice_in_dim(block, block.shape[dim] - width, None, axis=dim), axis, forward
        )
        high = lax.ppermute(lax.slice_in_dim(block, 0, width, axis=dim), axis, backward)
        block = jnp.concatenate([low, block, high], axis=dim)
    return block


def halving_stages(axes):
    out = []
    for axis in axes:
        count = lax.axis_size(axis)
        distance = 1
        while distance < count:
            out.append((axis, distance, count))
            distance *= 2
    return out


def reduce_scatter_rows(x, stages):
    for axis, distance, count in stages:
        bit = (lax.axis_index(axis) // distance) % 2
        half = x.shape[0] // 2
        keep = lax.dynamic_slice_in_dim(x, bit * half, half)
        send = lax.dynamic_slice_in_dim(x, (1 - bit) * half, half)
        pairs = [(j, j ^ distance) for j in range(count)]
        x = keep + lax.ppermute(send, axis, pairs)
    return x


def all_gather_rows(x, stages):
    for axis, distance, count in reversed(stages):
        bit = (lax.axis_index(axis) // distance) % 2
        pairs = [(j, j ^ distance) for j in range(count)]
        got = lax.ppermute(x, axis, pairs)
        low = jnp.where(bit == 0, x, got)
        high = jnp.where(bit == 0, got, x)
        x = jnp.concatenate([low, high], axis=0)
    return x


def summed_over(value, axes, chunks=1):
    sizes = [lax.axis_size(axis) for axis in axes]
    if any(size & (size - 1) for size in sizes):
        return lax.psum(value, axes)
    stages = halving_stages(axes)
    rows = value.reshape(-1, value.shape[-1])
    while chunks > 1 and rows.shape[0] % (chunks << len(stages)):
        chunks //= 2
    if rows.shape[0] % (chunks << len(stages)):
        return lax.psum(value, axes)
    pieces = jnp.split(rows, chunks, axis=0)
    joined = [all_gather_rows(reduce_scatter_rows(piece, stages), stages) for piece in pieces]
    return jnp.concatenate(joined, axis=0).reshape(value.shape)


def gathered_tokens(tokens, axes):
    sizes = [lax.axis_size(axis) for axis in axes]
    if any(size & (size - 1) for size in sizes):
        return lax.all_gather(tokens, axes, axis=0)
    full = tokens[None]
    for axis, size in reversed(list(zip(axes, sizes))):
        block = full
        distance = 1
        while distance < size:
            bit = (lax.axis_index(axis) // distance) % 2
            pairs = [(j, j ^ distance) for j in range(size)]
            got = lax.ppermute(block, axis, pairs)
            low = jnp.where(bit == 0, block, got)
            high = jnp.where(bit == 0, got, block)
            block = jnp.concatenate([low[None], high[None]], axis=0)
            block = block.reshape((-1,) + full.shape)
            distance *= 2
        full = block.reshape((-1,) + tokens.shape)
    return full

def padded_together(blocks, widths):
    for axis, dim in (("ha", 1), ("wa", 2)):
        count = lax.axis_size(axis)
        forward = [(i, i + 1) for i in range(count - 1)]
        backward = [(target, source) for source, target in forward]
        frames, chans = blocks[0].shape[0], blocks[0].shape[-1]

        def flat(parts):
            return jnp.concatenate([p.reshape(frames, -1, chans) for p in parts], axis=1)

        tails = [lax.slice_in_dim(b, b.shape[dim] - w, None, axis=dim) for b, w in zip(blocks, widths)]
        heads = [lax.slice_in_dim(b, 0, w, axis=dim) for b, w in zip(blocks, widths)]
        low = lax.ppermute(flat(tails), axis, forward)
        high = lax.ppermute(flat(heads), axis, backward)
        out, at = [], 0
        for b, t, h in zip(blocks, tails, heads):
            size = t.size // (frames * chans)
            got_low = low[:, at : at + size].reshape(t.shape)
            got_high = high[:, at : at + size].reshape(h.shape)
            at += size
            out.append(jnp.concatenate([got_low, b, got_high], axis=dim))
        blocks = out
    return blocks


def rms_norm(values, gain):
    scale = lax.rsqrt(jnp.mean(values * values, axis=-1, keepdims=True) + eps_norm)
    return values * scale * gain


def conv_valid(padded, kernel):
    return lax.conv_general_dilated(
        padded[None],
        kernel,
        (1, 1, 1),
        "VALID",
        dimension_numbers=("NDHWC", "DHWIO", "NDHWC"),
        preferred_element_type=jnp.float32,
    )[0]


def kernel_grad(padded, upstream):
    frames, rows, cols, chans = upstream.shape
    taps = []
    for tap_t in range(3):
        for tap_h in range(3):
            for tap_w in range(3):
                window = padded[tap_t : tap_t + frames, tap_h : tap_h + rows, tap_w : tap_w + cols]
                taps.append(
                    lax.dot_general(
                        window,
                        upstream,
                        (((0, 1, 2), (0, 1, 2)), ((), ())),
                        preferred_element_type=jnp.float32,
                    )
                )
    return jnp.stack(taps).reshape(3, 3, 3, chans, chans)


def norm_back(pre, gain, upstream):
    scale = lax.rsqrt(jnp.mean(pre * pre, axis=-1, keepdims=True) + eps_norm)
    normed = pre * scale
    gated = normed * gain
    sigma = jax.nn.sigmoid(gated)
    dgated = upstream * sigma * (1.0 + gated * (1.0 - sigma))
    dnormed = dgated * gain
    return scale * (dnormed - normed * jnp.mean(dnormed * normed, axis=-1, keepdims=True))


def attend(query, keys_all, values_all):
    width = query.shape[-1]
    scores = jnp.einsum(
        "fqc,fkc->fqk", query, keys_all, preferred_element_type=jnp.float32
    ) / math.sqrt(width)
    top = jnp.max(scores, axis=-1, keepdims=True)
    weights = jnp.exp(scores - top)
    probs = (weights / jnp.sum(weights, axis=-1, keepdims=True)).astype(jnp.bfloat16)
    return jnp.einsum("fqk,fkc->fqc", probs, values_all, preferred_element_type=jnp.float32).astype(
        jnp.bfloat16
    )


def causal_padded(block):
    earlier = shifted(block[-2:], "ta", 1)
    extended = jnp.concatenate([earlier, block], axis=0)
    return padded_2(extended, (("ha", 1), ("wa", 2)), 1)


def future_padded(block):
    later = shifted(block[:2], "ta", -1)
    extended = jnp.concatenate([block, later], axis=0)
    return padded_2(extended, (("ha", 1), ("wa", 2)), 1)


def local(
    clip,
    gain_attn,
    w_query,
    w_key,
    w_value,
    w_out,
    gain_one,
    w_one,
    bias_one,
    gain_two,
    w_two,
    bias_two,
    cotangent,
    crop_boxes,
):
    frames, rows, cols, chans = clip.shape
    n_ha, n_wa = lax.axis_size("ha"), lax.axis_size("wa")
    at_ha, at_wa = lax.axis_index("ha"), lax.axis_index("wa")
    clip_f = clip.astype(jnp.float32)
    pooled = (
        rms_norm(clip_f, gain_attn)
        .reshape(frames, rows // POOL, POOL, cols // POOL, POOL, chans)
        .mean(axis=(2, 4))
        .astype(jnp.bfloat16)
    )
    grid_rows, grid_cols = rows // POOL, cols // POOL
    full = gathered_tokens(pooled, ("ha", "wa")).reshape(
        n_ha, n_wa, frames, grid_rows, grid_cols, chans
    )
    grid = jnp.transpose(full, (2, 0, 3, 1, 4, 5)).reshape(
        frames, n_ha * grid_rows, n_wa * grid_cols, chans
    )
    tokens_all = grid.reshape(frames, -1, chans)
    keys_all = jnp.dot(tokens_all, w_key, preferred_element_type=jnp.float32).astype(jnp.bfloat16)
    values_all = jnp.dot(tokens_all, w_value, preferred_element_type=jnp.float32).astype(
        jnp.bfloat16
    )
    near = lax.dynamic_slice(
        jnp.pad(grid, ((0, 0), (1, 1), (1, 1), (0, 0))),
        (0, at_ha * grid_rows, at_wa * grid_cols, 0),
        (frames, grid_rows + 2, grid_cols + 2, chans),
    )
    query = jnp.dot(
        near.reshape(frames, -1, chans), w_query, preferred_element_type=jnp.float32
    ).astype(jnp.bfloat16)
    mixed = attend(query, keys_all, values_all)
    projected = jnp.dot(mixed, w_out, preferred_element_type=jnp.float32).reshape(
        frames, grid_rows + 2, grid_cols + 2, chans
    )
    upsampled = jnp.repeat(jnp.repeat(projected, POOL, axis=1), POOL, axis=2)
    upsampled = upsampled[:, POOL - 2 : POOL + rows + 2, POOL - 2 : POOL + cols + 2]
    bounds = crop_boxes[0, 0]
    local_row = jnp.arange(rows)[:, None]
    local_col = jnp.arange(cols)[None, :]
    inside = (
        (local_row >= bounds[0])
        & (local_row < bounds[1])
        & (local_col >= bounds[2])
        & (local_col < bounds[3])
    )
    masked = cotangent * inside.astype(jnp.bfloat16)[None, :, :, None]
    clip_wide, masked_wide = padded_together([clip, masked], [2, 1])
    clip_wide = clip_wide.astype(jnp.float32)
    masked_future = jnp.concatenate([masked_wide, shifted(masked_wide[:2], "ta", -1)], axis=0)
    attended_wide = (clip_wide + upsampled).astype(jnp.bfloat16)
    attended = attended_wide[:, 2 : 2 + rows, 2 : 2 + cols]

    def inside_frame(border):
        row_ids = at_ha * rows - border + jnp.arange(rows + 2 * border)
        col_ids = at_wa * cols - border + jnp.arange(cols + 2 * border)
        row_ok = (row_ids >= 0) & (row_ids < n_ha * rows)
        col_ok = (col_ids >= 0) & (col_ids < n_wa * cols)
        return (row_ok[:, None] & col_ok[None, :])[None, :, :, None]

    act_one_wide = jax.nn.silu(rms_norm(attended_wide.astype(jnp.float32), gain_one)).astype(
        jnp.bfloat16
    )
    act_one_wide = jnp.where(inside_frame(2), act_one_wide, jnp.zeros_like(act_one_wide))
    padded_one_wide = jnp.concatenate([shifted(act_one_wide[-2:], "ta", 1), act_one_wide], axis=0)
    pre_two_wide = conv_valid(padded_one_wide, w_one) + bias_one
    act_two_wide = jax.nn.silu(rms_norm(pre_two_wide, gain_two)).astype(jnp.bfloat16)
    act_two_wide = jnp.where(inside_frame(1), act_two_wide, jnp.zeros_like(act_two_wide))
    padded_two = jnp.concatenate([shifted(act_two_wide[-2:], "ta", 1), act_two_wide], axis=0)
    padded_one = padded_one_wide[:, 1 : 3 + rows, 1 : 3 + cols]
    pre_two = pre_two_wide[:, 1 : 1 + rows, 1 : 1 + cols]
    block_out = (attended.astype(jnp.float32) + conv_valid(padded_two, w_two) + bias_two).astype(
        jnp.bfloat16
    )
    total_pixels = (
        frames * lax.axis_size("ta") * rows * lax.axis_size("ha") * cols * lax.axis_size("wa")
    )
    norm_scale = 1.0 / math.sqrt(total_pixels)
    local_two = kernel_grad(padded_two, masked)
    flipped = jnp.transpose(w_two[::-1, ::-1, ::-1], (0, 1, 2, 4, 3))
    back_two = conv_valid(masked_future, flipped)
    back_one = norm_back(pre_two, gain_two, back_two).astype(jnp.bfloat16)
    local_one = kernel_grad(padded_one, back_one)
    summed_two = summed_over(local_two, ("ta", "wa", "ha"), chunks=2)
    summed_one = summed_over(local_one, ("ta", "wa", "ha"))
    return (block_out, summed_one * norm_scale, summed_two * norm_scale)


def solution(mesh):
    in_specs = (
        P(("groups", "ta"), "ha", "wa", None),
        P(),
        P(),
        P(),
        P(),
        P(),
        P(),
        P(),
        P(),
        P(),
        P(),
        P(),
        P(("groups", "ta"), "ha", "wa", None),
        P(("groups", "ha"), "wa", None),
    )
    out_specs = (
        P(("groups", "ta"), "ha", "wa", None),
        P("groups", None, None, None, None),
        P("groups", None, None, None, None),
    )
    return jax.shard_map(local, mesh=mesh, in_specs=in_specs, out_specs=out_specs, check_vma=False)
```

```python
import math

import jax
import jax.numpy as jnp
from jax import lax
from jax.sharding import PartitionSpec as P

POOL = 4


eps_norm = 1e-06


def shifted(x, axis, by):
    size = lax.axis_size(axis)
    pairs = [(i, i + by) for i in range(size) if 0 <= i + by < size]
    return lax.ppermute(x, axis, pairs)


def padded_2(block, sides, width):
    for axis, dim in sides:
        count = lax.axis_size(axis)
        forward = [(i, i + 1) for i in range(count - 1)]
        backward = [(target, source) for source, target in forward]
        low = lax.ppermute(
            lax.slice_in_dim(block, block.shape[dim] - width, None, axis=dim), axis, forward
        )
        high = lax.ppermute(lax.slice_in_dim(block, 0, width, axis=dim), axis, backward)
        block = jnp.concatenate([low, block, high], axis=dim)
    return block


def halving_stages(axes):
    out = []
    for axis in axes:
        count = lax.axis_size(axis)
        distance = 1
        while distance < count:
            out.append((axis, distance, count))
            distance *= 2
    return out


def reduce_scatter_rows(x, stages):
    for axis, distance, count in stages:
        bit = (lax.axis_index(axis) // distance) % 2
        half = x.shape[0] // 2
        keep = lax.dynamic_slice_in_dim(x, bit * half, half)
        send = lax.dynamic_slice_in_dim(x, (1 - bit) * half, half)
        pairs = [(j, j ^ distance) for j in range(count)]
        x = keep + lax.ppermute(send, axis, pairs)
    return x


def all_gather_rows(x, stages):
    for axis, distance, count in reversed(stages):
        bit = (lax.axis_index(axis) // distance) % 2
        pairs = [(j, j ^ distance) for j in range(count)]
        got = lax.ppermute(x, axis, pairs)
        half = x.shape[0]
        both = jnp.zeros((2 * half,) + x.shape[1:], x.dtype)
        both = lax.dynamic_update_slice_in_dim(both, x, bit * half, 0)
        x = lax.dynamic_update_slice_in_dim(both, got, (1 - bit) * half, 0)
    return x


def summed_over(value, axes, chunks=1):
    sizes = [lax.axis_size(axis) for axis in axes]
    if any(size & (size - 1) for size in sizes):
        return lax.psum(value, axes)
    stages = halving_stages(axes)
    rows = value.reshape(-1, value.shape[-1])
    while chunks > 1 and rows.shape[0] % (chunks << len(stages)):
        chunks //= 2
    if rows.shape[0] % (chunks << len(stages)):
        return lax.psum(value, axes)
    pieces = jnp.split(rows, chunks, axis=0)
    joined = [all_gather_rows(reduce_scatter_rows(piece, stages), stages) for piece in pieces]
    return jnp.concatenate(joined, axis=0).reshape(value.shape)


def gathered_tokens(tokens, axes):
    sizes = [lax.axis_size(axis) for axis in axes]
    if any(size & (size - 1) for size in sizes):
        return lax.all_gather(tokens, axes, axis=0)
    full = tokens[None]
    for axis, size in reversed(list(zip(axes, sizes))):
        block = full
        distance = 1
        while distance < size:
            bit = (lax.axis_index(axis) // distance) % 2
            pairs = [(j, j ^ distance) for j in range(size)]
            got = lax.ppermute(block, axis, pairs)
            low = jnp.where(bit == 0, block, got)
            high = jnp.where(bit == 0, got, block)
            block = jnp.concatenate([low[None], high[None]], axis=0)
            block = block.reshape((-1,) + full.shape)
            distance *= 2
        full = block.reshape((-1,) + tokens.shape)
    return full

def padded_together(blocks, widths):
    for axis, dim in (("ha", 1), ("wa", 2)):
        count = lax.axis_size(axis)
        forward = [(i, i + 1) for i in range(count - 1)]
        backward = [(target, source) for source, target in forward]
        frames, chans = blocks[0].shape[0], blocks[0].shape[-1]

        def flat(parts):
            return jnp.concatenate([p.reshape(frames, -1, chans) for p in parts], axis=1)

        tails = [lax.slice_in_dim(b, b.shape[dim] - w, None, axis=dim) for b, w in zip(blocks, widths)]
        heads = [lax.slice_in_dim(b, 0, w, axis=dim) for b, w in zip(blocks, widths)]
        low = lax.ppermute(flat(tails), axis, forward)
        high = lax.ppermute(flat(heads), axis, backward)
        out, at = [], 0
        for b, t, h in zip(blocks, tails, heads):
            size = t.size // (frames * chans)
            got_low = low[:, at : at + size].reshape(t.shape)
            got_high = high[:, at : at + size].reshape(h.shape)
            at += size
            out.append(jnp.concatenate([got_low, b, got_high], axis=dim))
        blocks = out
    return blocks


def rms_norm(values, gain):
    scale = lax.rsqrt(jnp.mean(values * values, axis=-1, keepdims=True) + eps_norm)
    return values * scale * gain


def conv_valid(padded, kernel):
    return lax.conv_general_dilated(
        padded[None],
        kernel,
        (1, 1, 1),
        "VALID",
        dimension_numbers=("NDHWC", "DHWIO", "NDHWC"),
        preferred_element_type=jnp.float32,
    )[0]


def kernel_grad(padded, upstream):
    frames, rows, cols, chans = upstream.shape
    taps = []
    for tap_t in range(3):
        for tap_h in range(3):
            for tap_w in range(3):
                window = padded[tap_t : tap_t + frames, tap_h : tap_h + rows, tap_w : tap_w + cols]
                taps.append(
                    lax.dot_general(
                        window,
                        upstream,
                        (((0, 1, 2), (0, 1, 2)), ((), ())),
                        preferred_element_type=jnp.float32,
                    )
                )
    return jnp.stack(taps).reshape(3, 3, 3, chans, chans)


def norm_back(pre, gain, upstream):
    scale = lax.rsqrt(jnp.mean(pre * pre, axis=-1, keepdims=True) + eps_norm)
    normed = pre * scale
    gated = normed * gain
    sigma = jax.nn.sigmoid(gated)
    dgated = upstream * sigma * (1.0 + gated * (1.0 - sigma))
    dnormed = dgated * gain
    return scale * (dnormed - normed * jnp.mean(dnormed * normed, axis=-1, keepdims=True))


def attend(query, keys_all, values_all):
    width = query.shape[-1]
    scores = jnp.einsum(
        "fqc,fkc->fqk", query, keys_all, preferred_element_type=jnp.float32
    ) / math.sqrt(width)
    top = jnp.max(scores, axis=-1, keepdims=True)
    weights = jnp.exp(scores - top)
    probs = (weights / jnp.sum(weights, axis=-1, keepdims=True)).astype(jnp.bfloat16)
    return jnp.einsum("fqk,fkc->fqc", probs, values_all, preferred_element_type=jnp.float32).astype(
        jnp.bfloat16
    )


def causal_padded(block):
    earlier = shifted(block[-2:], "ta", 1)
    extended = jnp.concatenate([earlier, block], axis=0)
    return padded_2(extended, (("ha", 1), ("wa", 2)), 1)


def future_padded(block):
    later = shifted(block[:2], "ta", -1)
    extended = jnp.concatenate([block, later], axis=0)
    return padded_2(extended, (("ha", 1), ("wa", 2)), 1)


def local(
    clip,
    gain_attn,
    w_query,
    w_key,
    w_value,
    w_out,
    gain_one,
    w_one,
    bias_one,
    gain_two,
    w_two,
    bias_two,
    cotangent,
    crop_boxes,
):
    frames, rows, cols, chans = clip.shape
    n_ha, n_wa = lax.axis_size("ha"), lax.axis_size("wa")
    at_ha, at_wa = lax.axis_index("ha"), lax.axis_index("wa")
    clip_f = clip.astype(jnp.float32)
    pooled = (
        rms_norm(clip_f, gain_attn)
        .reshape(frames, rows // POOL, POOL, cols // POOL, POOL, chans)
        .mean(axis=(2, 4))
        .astype(jnp.bfloat16)
    )
    grid_rows, grid_cols = rows // POOL, cols // POOL
    full = gathered_tokens(pooled, ("ha", "wa")).reshape(
        n_ha, n_wa, frames, grid_rows, grid_cols, chans
    )
    grid = jnp.transpose(full, (2, 0, 3, 1, 4, 5)).reshape(
        frames, n_ha * grid_rows, n_wa * grid_cols, chans
    )
    tokens_all = grid.reshape(frames, -1, chans)
    keys_all = jnp.dot(tokens_all, w_key, preferred_element_type=jnp.float32).astype(jnp.bfloat16)
    values_all = jnp.dot(tokens_all, w_value, preferred_element_type=jnp.float32).astype(
        jnp.bfloat16
    )
    near = lax.dynamic_slice(
        jnp.pad(grid, ((0, 0), (1, 1), (1, 1), (0, 0))),
        (0, at_ha * grid_rows, at_wa * grid_cols, 0),
        (frames, grid_rows + 2, grid_cols + 2, chans),
    )
    query = jnp.dot(
        near.reshape(frames, -1, chans), w_query, preferred_element_type=jnp.float32
    ).astype(jnp.bfloat16)
    mixed = attend(query, keys_all, values_all)
    projected = jnp.dot(mixed, w_out, preferred_element_type=jnp.float32).reshape(
        frames, grid_rows + 2, grid_cols + 2, chans
    )
    upsampled = jnp.repeat(jnp.repeat(projected, POOL, axis=1), POOL, axis=2)
    upsampled = upsampled[:, POOL - 2 : POOL + rows + 2, POOL - 2 : POOL + cols + 2]
    bounds = crop_boxes[0, 0]
    local_row = jnp.arange(rows)[:, None]
    local_col = jnp.arange(cols)[None, :]
    inside = (
        (local_row >= bounds[0])
        & (local_row < bounds[1])
        & (local_col >= bounds[2])
        & (local_col < bounds[3])
    )
    masked = cotangent * inside.astype(jnp.bfloat16)[None, :, :, None]
    clip_wide, masked_wide = padded_together([clip, masked], [2, 1])
    clip_wide = clip_wide.astype(jnp.float32)
    masked_future = jnp.concatenate([masked_wide, shifted(masked_wide[:2], "ta", -1)], axis=0)
    attended_wide = (clip_wide + upsampled).astype(jnp.bfloat16)
    attended = attended_wide[:, 2 : 2 + rows, 2 : 2 + cols]

    def inside_frame(border):
        row_ids = at_ha * rows - border + jnp.arange(rows + 2 * border)
        col_ids = at_wa * cols - border + jnp.arange(cols + 2 * border)
        row_ok = (row_ids >= 0) & (row_ids < n_ha * rows)
        col_ok = (col_ids >= 0) & (col_ids < n_wa * cols)
        return (row_ok[:, None] & col_ok[None, :])[None, :, :, None]

    act_one_wide = jax.nn.silu(rms_norm(attended_wide.astype(jnp.float32), gain_one)).astype(
        jnp.bfloat16
    )
    act_one_wide = jnp.where(inside_frame(2), act_one_wide, jnp.zeros_like(act_one_wide))
    padded_one_wide = jnp.concatenate([shifted(act_one_wide[-2:], "ta", 1), act_one_wide], axis=0)
    pre_two_wide = conv_valid(padded_one_wide, w_one) + bias_one
    act_two_wide = jax.nn.silu(rms_norm(pre_two_wide, gain_two)).astype(jnp.bfloat16)
    act_two_wide = jnp.where(inside_frame(1), act_two_wide, jnp.zeros_like(act_two_wide))
    padded_two = jnp.concatenate([shifted(act_two_wide[-2:], "ta", 1), act_two_wide], axis=0)
    padded_one = padded_one_wide[:, 1 : 3 + rows, 1 : 3 + cols]
    pre_two = pre_two_wide[:, 1 : 1 + rows, 1 : 1 + cols]
    block_out = (attended.astype(jnp.float32) + conv_valid(padded_two, w_two) + bias_two).astype(
        jnp.bfloat16
    )
    total_pixels = (
        frames * lax.axis_size("ta") * rows * lax.axis_size("ha") * cols * lax.axis_size("wa")
    )
    norm_scale = 1.0 / math.sqrt(total_pixels)
    local_two = kernel_grad(padded_two, masked)
    flipped = jnp.transpose(w_two[::-1, ::-1, ::-1], (0, 1, 2, 4, 3))
    back_two = conv_valid(masked_future, flipped)
    back_one = norm_back(pre_two, gain_two, back_two).astype(jnp.bfloat16)
    local_one = kernel_grad(padded_one, back_one)
    summed_two = summed_over(local_two, ("ta", "wa", "ha"))
    summed_one = summed_over(local_one, ("ta", "wa", "ha"))
    return (block_out, summed_one * norm_scale, summed_two * norm_scale)


def solution(mesh):
    in_specs = (
        P(("groups", "ta"), "ha", "wa", None),
        P(),
        P(),
        P(),
        P(),
        P(),
        P(),
        P(),
        P(),
        P(),
        P(),
        P(),
        P(("groups", "ta"), "ha", "wa", None),
        P(("groups", "ha"), "wa", None),
    )
    out_specs = (
        P(("groups", "ta"), "ha", "wa", None),
        P("groups", None, None, None, None),
        P("groups", None, None, None, None),
    )
    return jax.shard_map(local, mesh=mesh, in_specs=in_specs, out_specs=out_specs, check_vma=False)
```

```python
import math

import jax
import jax.numpy as jnp
from jax import lax
from jax.sharding import PartitionSpec as P

POOL = 4


eps_norm = 1e-06


def shifted(x, axis, by):
    size = lax.axis_size(axis)
    pairs = [(i, i + by) for i in range(size) if 0 <= i + by < size]
    return lax.ppermute(x, axis, pairs)


def padded_2(block, sides, width):
    for axis, dim in sides:
        count = lax.axis_size(axis)
        forward = [(i, i + 1) for i in range(count - 1)]
        backward = [(target, source) for source, target in forward]
        low = lax.ppermute(
            lax.slice_in_dim(block, block.shape[dim] - width, None, axis=dim), axis, forward
        )
        high = lax.ppermute(lax.slice_in_dim(block, 0, width, axis=dim), axis, backward)
        block = jnp.concatenate([low, block, high], axis=dim)
    return block


def halving_stages(axes):
    out = []
    for axis in axes:
        count = lax.axis_size(axis)
        distance = 1
        while distance < count:
            out.append((axis, distance, count))
            distance *= 2
    return out


def reduce_scatter_rows(x, stages):
    for axis, distance, count in stages:
        bit = (lax.axis_index(axis) // distance) % 2
        half = x.shape[0] // 2
        keep = lax.dynamic_slice_in_dim(x, bit * half, half)
        send = lax.dynamic_slice_in_dim(x, (1 - bit) * half, half)
        pairs = [(j, j ^ distance) for j in range(count)]
        x = keep + lax.ppermute(send, axis, pairs)
    return x


def all_gather_rows(x, stages):
    for axis, distance, count in reversed(stages):
        bit = (lax.axis_index(axis) // distance) % 2
        pairs = [(j, j ^ distance) for j in range(count)]
        got = lax.ppermute(x, axis, pairs)
        half = x.shape[0]
        both = jnp.zeros((2 * half,) + x.shape[1:], x.dtype)
        both = lax.dynamic_update_slice_in_dim(both, x, bit * half, 0)
        x = lax.dynamic_update_slice_in_dim(both, got, (1 - bit) * half, 0)
    return x


def summed_over(value, axes, chunks=1):
    sizes = [lax.axis_size(axis) for axis in axes]
    if any(size & (size - 1) for size in sizes):
        return lax.psum(value, axes)
    stages = halving_stages(axes)
    rows = value.reshape(-1, value.shape[-1])
    while chunks > 1 and rows.shape[0] % (chunks << len(stages)):
        chunks //= 2
    if rows.shape[0] % (chunks << len(stages)):
        return lax.psum(value, axes)
    pieces = jnp.split(rows, chunks, axis=0)
    joined = [all_gather_rows(reduce_scatter_rows(piece, stages), stages) for piece in pieces]
    return jnp.concatenate(joined, axis=0).reshape(value.shape)


def gathered_tokens(tokens, axes):
    sizes = [lax.axis_size(axis) for axis in axes]
    if any(size & (size - 1) for size in sizes):
        return lax.all_gather(tokens, axes, axis=0)
    full = tokens[None]
    for axis, size in reversed(list(zip(axes, sizes))):
        block = full
        distance = 1
        while distance < size:
            bit = (lax.axis_index(axis) // distance) % 2
            pairs = [(j, j ^ distance) for j in range(size)]
            got = lax.ppermute(block, axis, pairs)
            both = jnp.zeros((2,) + block.shape, block.dtype)
            both = lax.dynamic_update_index_in_dim(both, block, bit, 0)
            both = lax.dynamic_update_index_in_dim(both, got, 1 - bit, 0)
            block = both.reshape((-1,) + full.shape)
            distance *= 2
        full = block.reshape((-1,) + tokens.shape)
    return full

def padded_together(blocks, widths):
    for axis, dim in (("ha", 1), ("wa", 2)):
        count = lax.axis_size(axis)
        forward = [(i, i + 1) for i in range(count - 1)]
        backward = [(target, source) for source, target in forward]
        frames, chans = blocks[0].shape[0], blocks[0].shape[-1]

        def flat(parts):
            return jnp.concatenate([p.reshape(frames, -1, chans) for p in parts], axis=1)

        tails = [lax.slice_in_dim(b, b.shape[dim] - w, None, axis=dim) for b, w in zip(blocks, widths)]
        heads = [lax.slice_in_dim(b, 0, w, axis=dim) for b, w in zip(blocks, widths)]
        low = lax.ppermute(flat(tails), axis, forward)
        high = lax.ppermute(flat(heads), axis, backward)
        out, at = [], 0
        for b, t, h in zip(blocks, tails, heads):
            size = t.size // (frames * chans)
            got_low = low[:, at : at + size].reshape(t.shape)
            got_high = high[:, at : at + size].reshape(h.shape)
            at += size
            out.append(jnp.concatenate([got_low, b, got_high], axis=dim))
        blocks = out
    return blocks


def rms_norm(values, gain):
    scale = lax.rsqrt(jnp.mean(values * values, axis=-1, keepdims=True) + eps_norm)
    return values * scale * gain


def conv_valid(padded, kernel):
    return lax.conv_general_dilated(
        padded[None],
        kernel,
        (1, 1, 1),
        "VALID",
        dimension_numbers=("NDHWC", "DHWIO", "NDHWC"),
        preferred_element_type=jnp.float32,
    )[0]


def kernel_grad(padded, upstream):
    frames, rows, cols, chans = upstream.shape
    taps = []
    for tap_t in range(3):
        for tap_h in range(3):
            for tap_w in range(3):
                window = padded[tap_t : tap_t + frames, tap_h : tap_h + rows, tap_w : tap_w + cols]
                taps.append(
                    lax.dot_general(
                        window,
                        upstream,
                        (((0, 1, 2), (0, 1, 2)), ((), ())),
                        preferred_element_type=jnp.float32,
                    )
                )
    return jnp.stack(taps).reshape(3, 3, 3, chans, chans)


def norm_back(pre, gain, upstream):
    scale = lax.rsqrt(jnp.mean(pre * pre, axis=-1, keepdims=True) + eps_norm)
    normed = pre * scale
    gated = normed * gain
    sigma = jax.nn.sigmoid(gated)
    dgated = upstream * sigma * (1.0 + gated * (1.0 - sigma))
    dnormed = dgated * gain
    return scale * (dnormed - normed * jnp.mean(dnormed * normed, axis=-1, keepdims=True))


def attend(query, keys_all, values_all):
    width = query.shape[-1]
    scores = jnp.einsum(
        "fqc,fkc->fqk", query, keys_all, preferred_element_type=jnp.float32
    ) / math.sqrt(width)
    top = jnp.max(scores, axis=-1, keepdims=True)
    weights = jnp.exp(scores - top)
    probs = (weights / jnp.sum(weights, axis=-1, keepdims=True)).astype(jnp.bfloat16)
    return jnp.einsum("fqk,fkc->fqc", probs, values_all, preferred_element_type=jnp.float32).astype(
        jnp.bfloat16
    )


def causal_padded(block):
    earlier = shifted(block[-2:], "ta", 1)
    extended = jnp.concatenate([earlier, block], axis=0)
    return padded_2(extended, (("ha", 1), ("wa", 2)), 1)


def future_padded(block):
    later = shifted(block[:2], "ta", -1)
    extended = jnp.concatenate([block, later], axis=0)
    return padded_2(extended, (("ha", 1), ("wa", 2)), 1)


def local(
    clip,
    gain_attn,
    w_query,
    w_key,
    w_value,
    w_out,
    gain_one,
    w_one,
    bias_one,
    gain_two,
    w_two,
    bias_two,
    cotangent,
    crop_boxes,
):
    frames, rows, cols, chans = clip.shape
    n_ha, n_wa = lax.axis_size("ha"), lax.axis_size("wa")
    at_ha, at_wa = lax.axis_index("ha"), lax.axis_index("wa")
    clip_f = clip.astype(jnp.float32)
    pooled = (
        rms_norm(clip_f, gain_attn)
        .reshape(frames, rows // POOL, POOL, cols // POOL, POOL, chans)
        .mean(axis=(2, 4))
        .astype(jnp.bfloat16)
    )
    grid_rows, grid_cols = rows // POOL, cols // POOL
    full = gathered_tokens(pooled, ("ha", "wa")).reshape(
        n_ha, n_wa, frames, grid_rows, grid_cols, chans
    )
    grid = jnp.transpose(full, (2, 0, 3, 1, 4, 5)).reshape(
        frames, n_ha * grid_rows, n_wa * grid_cols, chans
    )
    tokens_all = grid.reshape(frames, -1, chans)
    keys_all = jnp.dot(tokens_all, w_key, preferred_element_type=jnp.float32).astype(jnp.bfloat16)
    values_all = jnp.dot(tokens_all, w_value, preferred_element_type=jnp.float32).astype(
        jnp.bfloat16
    )
    near = lax.dynamic_slice(
        jnp.pad(grid, ((0, 0), (1, 1), (1, 1), (0, 0))),
        (0, at_ha * grid_rows, at_wa * grid_cols, 0),
        (frames, grid_rows + 2, grid_cols + 2, chans),
    )
    query = jnp.dot(
        near.reshape(frames, -1, chans), w_query, preferred_element_type=jnp.float32
    ).astype(jnp.bfloat16)
    mixed = attend(query, keys_all, values_all)
    projected = jnp.dot(mixed, w_out, preferred_element_type=jnp.float32).reshape(
        frames, grid_rows + 2, grid_cols + 2, chans
    )
    upsampled = jnp.repeat(jnp.repeat(projected, POOL, axis=1), POOL, axis=2)
    upsampled = upsampled[:, POOL - 2 : POOL + rows + 2, POOL - 2 : POOL + cols + 2]
    bounds = crop_boxes[0, 0]
    local_row = jnp.arange(rows)[:, None]
    local_col = jnp.arange(cols)[None, :]
    inside = (
        (local_row >= bounds[0])
        & (local_row < bounds[1])
        & (local_col >= bounds[2])
        & (local_col < bounds[3])
    )
    masked = cotangent * inside.astype(jnp.bfloat16)[None, :, :, None]
    clip_wide, masked_wide = padded_together([clip, masked], [2, 1])
    clip_wide = clip_wide.astype(jnp.float32)
    masked_future = jnp.concatenate([masked_wide, shifted(masked_wide[:2], "ta", -1)], axis=0)
    attended_wide = (clip_wide + upsampled).astype(jnp.bfloat16)
    attended = attended_wide[:, 2 : 2 + rows, 2 : 2 + cols]

    def inside_frame(border):
        row_ids = at_ha * rows - border + jnp.arange(rows + 2 * border)
        col_ids = at_wa * cols - border + jnp.arange(cols + 2 * border)
        row_ok = (row_ids >= 0) & (row_ids < n_ha * rows)
        col_ok = (col_ids >= 0) & (col_ids < n_wa * cols)
        return (row_ok[:, None] & col_ok[None, :])[None, :, :, None]

    act_one_wide = jax.nn.silu(rms_norm(attended_wide.astype(jnp.float32), gain_one)).astype(
        jnp.bfloat16
    )
    act_one_wide = jnp.where(inside_frame(2), act_one_wide, jnp.zeros_like(act_one_wide))
    padded_one_wide = jnp.concatenate([shifted(act_one_wide[-2:], "ta", 1), act_one_wide], axis=0)
    pre_two_wide = conv_valid(padded_one_wide, w_one) + bias_one
    act_two_wide = jax.nn.silu(rms_norm(pre_two_wide, gain_two)).astype(jnp.bfloat16)
    act_two_wide = jnp.where(inside_frame(1), act_two_wide, jnp.zeros_like(act_two_wide))
    padded_two = jnp.concatenate([shifted(act_two_wide[-2:], "ta", 1), act_two_wide], axis=0)
    padded_one = padded_one_wide[:, 1 : 3 + rows, 1 : 3 + cols]
    pre_two = pre_two_wide[:, 1 : 1 + rows, 1 : 1 + cols]
    block_out = (attended.astype(jnp.float32) + conv_valid(padded_two, w_two) + bias_two).astype(
        jnp.bfloat16
    )
    total_pixels = (
        frames * lax.axis_size("ta") * rows * lax.axis_size("ha") * cols * lax.axis_size("wa")
    )
    norm_scale = 1.0 / math.sqrt(total_pixels)
    local_two = kernel_grad(padded_two, masked)
    flipped = jnp.transpose(w_two[::-1, ::-1, ::-1], (0, 1, 2, 4, 3))
    back_two = conv_valid(masked_future, flipped)
    back_one = norm_back(pre_two, gain_two, back_two).astype(jnp.bfloat16)
    local_one = kernel_grad(padded_one, back_one)
    summed_two = summed_over(local_two, ("ta", "wa", "ha"))
    summed_one = summed_over(local_one, ("ta", "wa", "ha"))
    return (block_out, summed_one * norm_scale, summed_two * norm_scale)


def solution(mesh):
    in_specs = (
        P(("groups", "ta"), "ha", "wa", None),
        P(),
        P(),
        P(),
        P(),
        P(),
        P(),
        P(),
        P(),
        P(),
        P(),
        P(),
        P(("groups", "ta"), "ha", "wa", None),
        P(("groups", "ha"), "wa", None),
    )
    out_specs = (
        P(("groups", "ta"), "ha", "wa", None),
        P("groups", None, None, None, None),
        P("groups", None, None, None, None),
    )
    return jax.shard_map(local, mesh=mesh, in_specs=in_specs, out_specs=out_specs, check_vma=False)
```
